32 devices in a mesh: kv: 4 (over x, core), blk: 8 (over z, y).
Axes of the slice: x: 2, y: 2, z: 4, core: 2. Of those that a mesh axis runs over, the one named last changes fastest.
Arguments:
- hidden_in: bfloat16 [512, 2560], P('blk', 'kv'), may hold values from -33 to 33
- queries: bfloat16 [512, 2560], P('blk', 'kv'), may hold values from -240 to 240
- new_kv: bfloat16 [512, 4, 2, 128], P('blk', 'kv'), may hold values from -6 to 6
- cache_pool: bfloat16 [32, 16, 4, 2, 128], P('blk', None, 'kv'), may hold values from -6 to 6
- cache_len: int32 [8], replicated, may hold values from 0 to 128, as said below
- block_holder: int32 [8, 8], replicated, may hold values from 0 to 7, as said below
- block_slot: int32 [8, 8], replicated, may hold values from 0 to 3, as said below
- decode_holder: int32 [8, 12], replicated, may hold values from 0 to 7, as said below
- decode_slot: int32 [8, 12], replicated, may hold values from 0 to 7, as said below
- out_weight: bfloat16 [2560, 2560], P('kv', 'blk'), may hold values from -0.125 to 0.125
- norm_gain: bfloat16 [2560], P('kv'), may hold values from 0.5 to 1.5
- router_weight: float32 [2560, 64], P('kv'), may hold values from -0.125 to 0.125
- expert_routes: int32 [512, 6], P('blk'), may hold values from 0 to 63, all different within a row; in each aligned block of 64 rows (0 to 63, 64 to 127, ...) at most 8 rows name the same one
- w_gate: bfloat16 [128, 2560, 768], P('blk', 'kv'), may hold values from -0.125 to 0.125
- w_up: bfloat16 [128, 2560, 768], P('blk', 'kv'), may hold values from -0.125 to 0.125
- w_down: bfloat16 [128, 768, 2560], P('blk', None, 'kv'), may hold values from -0.15625 to 0.15625
Outputs:
- layer_out: bfloat16 [512, 2560], P('blk', 'kv')
- decode_pool: bfloat16 [64, 16, 4, 2, 128], P('blk', None, 'kv')
The draws below stay inside these ranges and needn't reach their ends.
Inputs may be any that keep to these rules, and one draw needn't show every extreme that they name: `cache_len`: every value is a multiple of 16; half of the requests have 0, the others at least 16. `block_holder`: the entries of one request are distinct devices; entries beyond cache_len / 16 are unused. `block_slot`: the used blocks held by one device have distinct slots. `decode_holder`: the used blocks that one device sends, those it holds and the 4 new blocks of its own request, go to distinct decoding devices. `decode_slot`: no two used blocks share a decoding device and slot.
All inputs are finite; a program needn't handle non-finite values.
Results may differ from the reference program's by a relative error of at most 0.008.
Values may be sent and summed in bfloat16 or wider, within the bound.
No kernel may reach another device: no remote copies, remote signals or barrier semaphores. Data moves between devices by JAX's collectives and lax.ppermute only.
A program may use at most 128 MiB of HBM per device.

```python
import math
import jax
import jax.numpy as jnp
import numpy as np
from jax import lax

D = 2560
HD = 128
KVH = 4
QPK = 5
QH = 20
EXPERTS = 64
FF = 1536
TOP = 6
STRETCH = 64
BLOCK = 16
CAP = 8
REQS = 8
MAXB = 8
POOL = 4
NEWB = 4
DPOOL = 8
TOKENS = 512
N_BLK = 8


def draw_hidden_in(key, part):
    noise_key, row_key = jax.random.split(jax.random.fold_in(key, 5003))
    column = jnp.arange(D, dtype=jnp.float32) / (D - 1)
    base = jnp.clip(jax.random.normal(noise_key, (TOKENS, D), jnp.float32), -6.0, 6.0)
    ramp = 0.6 + 1.2 * column
    row_scale = jnp.exp(jax.random.uniform(row_key, (TOKENS, 1), jnp.float32, math.log(0.3), math.log(3.0)))
    return (base * ramp[None, :] * row_scale).astype(jnp.bfloat16)


def attention_inputs(key):
    query_key, pair_key = jax.random.split(jax.random.fold_in(key, 9001), 2)
    asked_rows = jnp.clip(jax.random.normal(query_key, (TOKENS, KVH, QPK, HD), jnp.float32), -6.0, 6.0)
    pair_rows = jnp.clip(jax.random.normal(pair_key, (TOKENS, KVH, 2, HD), jnp.float32), -6.0, 6.0)
    return (asked_rows.reshape(TOKENS, KVH * QPK * HD), pair_rows)


def draw_queries(key, part):
    return attention_inputs(key)[0].astype(jnp.bfloat16)


def draw_new_kv(key, part):
    return attention_inputs(key)[1].astype(jnp.bfloat16)


def cache_layout(key):
    subkeys = jax.random.split(jax.random.fold_in(key, 7001), 7)
    packing = jax.random.permutation(subkeys[0], REQS)
    order_rank = jnp.argsort(packing)
    block_counts = jax.random.randint(subkeys[1], (REQS,), 1, MAXB + 1)
    block_counts = jnp.where(order_rank == 0, MAXB, block_counts)
    continuing = order_rank < POOL
    block_counts = jnp.where(continuing, block_counts, 0)
    holders = jax.vmap(lambda subkey: jax.random.permutation(subkey, REQS))(jax.random.split(subkeys[2], REQS))[:, :MAXB]
    arrange = jax.vmap(lambda subkey: jax.random.permutation(subkey, POOL))(jax.random.split(subkeys[3], REQS))
    spare = jax.random.randint(subkeys[4], (REQS, MAXB), 0, POOL)
    slots = jnp.where(continuing[:, None], arrange[holders, jnp.minimum(order_rank, POOL - 1)[:, None]], spare)
    shifts = jax.random.permutation(subkeys[5], REQS)
    old_dest = (holders + shifts[slots]) % REQS
    fresh_index = POOL + jnp.arange(NEWB)
    new_dest = (jnp.arange(REQS)[:, None] + shifts[fresh_index][None, :]) % REQS
    destinations = jnp.concatenate([old_dest, new_dest], axis=1)
    local_index = jnp.concatenate([slots, jnp.broadcast_to(fresh_index[None, :], (REQS, NEWB))], axis=1)
    within = jax.vmap(lambda subkey: jax.random.permutation(subkey, DPOOL))(jax.random.split(subkeys[6], REQS))
    decode_slots = within[destinations, local_index]
    return (block_counts * BLOCK, holders, slots, destinations, decode_slots)


def draw_cache_len(key, part):
    return cache_layout(key)[0].astype(jnp.int32)


def draw_block_holder(key, part):
    return cache_layout(key)[1].astype(jnp.int32)


def draw_block_slot(key, part):
    return cache_layout(key)[2].astype(jnp.int32)


def draw_decode_holder(key, part):
    return cache_layout(key)[3].astype(jnp.int32)


def draw_decode_slot(key, part):
    return cache_layout(key)[4].astype(jnp.int32)


def steps_of(own_key, shape, cuts, least, largest):
    level = 1.0
    for dim, blocks in cuts:
        draws = jax.random.uniform(jax.random.fold_in(jax.random.fold_in(own_key, 6), dim), (blocks,), jnp.float32, least / len(cuts), largest / len(cuts))
        level = level * jnp.repeat(jnp.exp(draws), shape[dim] // blocks).reshape((-1,) + (1,) * (len(shape) - 1 - dim))
    return level


def shared_out(rng, own, number, rows, amount, top, limit, skew):
    ranking = jax.random.permutation(rng, amount)
    crowded, common = portions_of(amount, rows * top, limit, skew, True), portions_of(amount, rows * top, limit, skew, False)
    places = jnp.arange(amount)

    def named(lengths, rotation):
        used = int((lengths > 0).sum())
        fixed = max(1, used // 4)
        shifted = fixed + (places - fixed + rotation * (used - fixed)) % max(1, amount - fixed)
        return jnp.zeros((amount,), jnp.int32).at[ranking[jnp.where(places < fixed, places, shifted)]].set(jnp.asarray(lengths, jnp.int32))

    lengths = jnp.where(number % 4 == 0, named(crowded, number // 4), named(common, number - number // 4 - 1))
    mixed = jax.random.permutation(jax.random.fold_in(own, 3), amount)
    giver, taker = mixed[0:amount // 2 * 2:2], mixed[1:amount // 2 * 2:2]
    room = jnp.minimum(lengths[giver] - 1, limit - lengths[taker]) // 2
    room = jnp.where((giver == ranking[0]) | (taker == ranking[0]) | (lengths[taker] == 0), 0, jnp.maximum(room, 0))
    shifted = jax.random.randint(jax.random.fold_in(own, 4), (amount // 2,), 0, 1 << 20) % (room + 1)
    lengths = lengths.at[giver].add(-shifted).at[taker].add(shifted)
    items = jnp.searchsorted(jnp.cumsum(lengths), jnp.arange(rows * top), side="right").astype(jnp.int32)
    grid = items.reshape(top, rows).T
    grid = grid[jax.random.permutation(jax.random.fold_in(own, 1), rows)]
    rotation = jax.random.randint(jax.random.fold_in(own, 2), (rows, 1), 0, top)
    return jnp.take_along_axis(grid, (jnp.arange(top)[None, :] + rotation) % top, axis=1)


def portions_of(count, total, bound, slope, full):
    weights = [(1 << 20) // math.isqrt(standing ** slope) + 1 for standing in range(1, count + 1)]
    largest = bound if full else min(bound, max(-(-total // count), total * weights[0] // sum(weights)))
    least = 1 if total - largest >= count - 1 else 0
    counts, spare = [largest] + [least] * (count - 1), total - largest - least * (count - 1)
    while spare > 0:
        movable = [i for i in range(1, count) if counts[i] < largest] or [i for i in range(1, count) if counts[i] < bound]
        pool, left = sum([weights[i] for i in movable]), spare
        for i in movable:
            extra = min(bound - counts[i], max(1, left * weights[i] // pool), spare)
            counts[i] = counts[i] + extra
            spare = spare - extra
    return np.array(counts)


def bell_draw(own_key, shape, width, limit, pieces=(), held_as=jnp.bfloat16):
    factor_of = steps_of(own_key, shape, pieces, -0.22, 0.18) if pieces else 1.0
    drawn = jax.random.normal(own_key, shape, jnp.float32) * width * factor_of
    return jnp.minimum(jnp.maximum(drawn, -limit), limit).astype(held_as)


def setup_inputs(seed: int = 0) -> dict:
    key_list = jax.random.split(jax.random.key(seed), 17)
    hidden_in = draw_hidden_in(jax.random.fold_in(key_list[16], 71), 0)
    queries = draw_queries(jax.random.fold_in(key_list[16], 71), 0)
    new_kv = draw_new_kv(jax.random.fold_in(key_list[16], 71), 0)
    cache_pool = bell_draw(key_list[3], (N_BLK * POOL, BLOCK, KVH, 2, HD), 1.0, 6.0, ((0, 8), (2, 4)))
    cache_len = draw_cache_len(jax.random.fold_in(key_list[16], 71), 0)
    block_holder = draw_block_holder(jax.random.fold_in(key_list[16], 71), 0)
    block_slot = draw_block_slot(jax.random.fold_in(key_list[16], 71), 0)
    decode_holder = draw_decode_holder(jax.random.fold_in(key_list[16], 71), 0)
    decode_slot = draw_decode_slot(jax.random.fold_in(key_list[16], 71), 0)
    out_weight = bell_draw(key_list[9], (QH * HD, D), (QH * HD) ** -0.5, 0.125, ((0, 4), (1, 8)))
    norm_gain = jnp.clip(1.0 + 0.1 * jax.random.normal(key_list[10], (D,), jnp.float32), 0.5, 1.5).astype(jnp.bfloat16)
    router_weight = bell_draw(key_list[11], (D, EXPERTS), D ** -0.5, 0.125, ((0, 4),), jnp.float32)
    expert_routes_keys = jax.random.split(jax.random.fold_in(key_list[12], 1), TOKENS // STRETCH)
    expert_routes_turns = jax.random.permutation(jax.random.fold_in(key_list[12], 3), TOKENS // STRETCH)
    expert_routes = jax.vmap(lambda own, number: shared_out(jax.random.fold_in(key_list[12], 2), own, number, STRETCH, EXPERTS, TOP, CAP, 2))(expert_routes_keys, expert_routes_turns).reshape((TOKENS, TOP))
    w_gate = bell_draw(key_list[13], (2 * EXPERTS, D, FF // 2), D ** -0.5, 0.125, ((0, 8), (1, 4)))
    w_up = bell_draw(key_list[14], (2 * EXPERTS, D, FF // 2), D ** -0.5, 0.125, ((0, 8), (1, 4)))
    w_down = bell_draw(key_list[15], (2 * EXPERTS, FF // 2, D), FF ** -0.5, 0.15625, ((0, 8), (2, 4)))
    return {"hidden_in": hidden_in, "queries": queries, "new_kv": new_kv, "cache_pool": cache_pool, "cache_len": cache_len, "block_holder": block_holder, "block_slot": block_slot, "decode_holder": decode_holder, "decode_slot": decode_slot, "out_weight": out_weight, "norm_gain": norm_gain, "router_weight": router_weight, "expert_routes": expert_routes, "w_gate": w_gate, "w_up": w_up, "w_down": w_down}


EPSILON = 1e-05

def request_attention(queries, new_kv, cache_pool, cache_len, block_holder, block_slot, request):
    blocks = cache_len[request] // BLOCK
    row_ids = (block_holder[request] * POOL + block_slot[request]).astype(jnp.int32)
    cached = cache_pool[row_ids].reshape(MAXB * BLOCK, KVH, 2, HD)
    fresh_rows = lax.dynamic_slice_in_dim(new_kv, (request * STRETCH).astype(jnp.int32), STRETCH, 0)
    all_keys = jnp.concatenate([cached, fresh_rows], axis=0)
    asked_rows = lax.dynamic_slice_in_dim(queries, (request * STRETCH).astype(jnp.int32), STRETCH, 0).reshape(STRETCH, KVH, QPK, HD)
    scale = 1.0 / math.sqrt(HD)
    scores = jnp.einsum('cgqd,lgd->gqcl', asked_rows.astype(jnp.float32), all_keys[:, :, 0].astype(jnp.float32)) * scale
    stored = jnp.arange(MAXB * BLOCK) < blocks * BLOCK
    positions = jnp.arange(STRETCH)
    causal = positions[None, :] <= positions[:, None]
    allowed = jnp.concatenate([jnp.broadcast_to(stored[None, :], (STRETCH, MAXB * BLOCK)), causal], axis=1)
    scores = jnp.where(allowed, scores, -jnp.inf)
    row_max = lax.optimization_barrier(jnp.max(scores, axis=3, keepdims=True))
    raised = jnp.exp(scores - row_max)
    denominator = lax.optimization_barrier(jnp.sum(raised, axis=3))
    weights = lax.optimization_barrier(raised.astype(jnp.bfloat16))
    mixed_out = jnp.einsum('gqcl,lgd->gqcd', weights.astype(jnp.float32), all_keys[:, :, 1].astype(jnp.float32))
    mixed_out = mixed_out / denominator[..., None]
    return jnp.transpose(mixed_out, (2, 0, 1, 3)).reshape(STRETCH, KVH * QPK * HD).astype(jnp.bfloat16)

def expert_layer(normed, gates, expert_routes, w_gate, w_up, w_down):
    flat_routes = expert_routes.reshape(-1)
    gate_flat = gates.reshape(-1)
    rows_most = N_BLK * CAP
    groups = normed.reshape(TOKENS, KVH, D // KVH)

    def advance(carried, expert):
        is_hit = flat_routes == expert
        found_rows = jnp.nonzero(is_hit, size=rows_most, fill_value=0)[0].astype(jnp.int32)
        is_live = jnp.arange(rows_most) < jnp.sum(is_hit.astype(jnp.int32))
        token_ids = (found_rows // TOP).astype(jnp.int32)
        taken_rows = groups[token_ids].astype(jnp.float32)
        summed = jnp.zeros((rows_most, D), jnp.float32)
        for half_index in range(2):
            piece_id = 2 * expert + half_index
            gate_cast = w_gate[piece_id].reshape(KVH, D // KVH, FF // 2).astype(jnp.float32)
            up_cast = w_up[piece_id].reshape(KVH, D // KVH, FF // 2).astype(jnp.float32)
            gate_parts = lax.optimization_barrier(jnp.einsum('rgd,gdu->rgu', taken_rows, gate_cast).astype(jnp.bfloat16))
            up_parts = lax.optimization_barrier(jnp.einsum('rgd,gdu->rgu', taken_rows, up_cast).astype(jnp.bfloat16))
            gate_sum = lax.optimization_barrier(jnp.sum(gate_parts.astype(jnp.float32), axis=1))
            up_sum = lax.optimization_barrier(jnp.sum(up_parts.astype(jnp.float32), axis=1))
            hidden = (jax.nn.silu(gate_sum) * up_sum).astype(jnp.bfloat16)
            piece_out = jnp.dot(hidden, w_down[piece_id], preferred_element_type=jnp.float32).astype(jnp.bfloat16)
            summed = summed + piece_out.astype(jnp.float32)
        scaled = summed * jnp.where(is_live, gate_flat[found_rows], 0.0)[:, None]
        return (carried.at[token_ids].add(scaled), None)
    moe_out, _ = lax.scan(advance, jnp.zeros((TOKENS, D), jnp.float32), jnp.arange(EXPERTS).astype(jnp.int32))
    return moe_out

def relay_blocks(new_kv, cache_pool, cache_len, block_holder, block_slot, decode_holder, decode_slot):
    block_counts = cache_len // BLOCK
    in_use = jnp.arange(MAXB)[None, :] < block_counts[:, None]
    source_rows = (block_holder * POOL + block_slot).astype(jnp.int32)
    target_rows = jnp.where(in_use, decode_holder[:, :MAXB] * DPOOL + decode_slot[:, :MAXB], N_BLK * DPOOL).astype(jnp.int32)

    def advance(carried, request):
        moved = cache_pool[source_rows[request]]
        return (carried.at[target_rows[request]].set(moved, mode='drop'), None)
    start_pool = jnp.zeros((N_BLK * DPOOL, BLOCK, KVH, 2, HD), jnp.bfloat16)
    filled, _ = lax.scan(advance, start_pool, jnp.arange(REQS).astype(jnp.int32))
    fresh_blocks = new_kv.reshape(REQS * NEWB, BLOCK, KVH, 2, HD)
    fresh_target = (decode_holder[:, MAXB:] * DPOOL + decode_slot[:, MAXB:]).reshape(-1).astype(jnp.int32)
    return filled.at[fresh_target].set(fresh_blocks)

def reference(hidden_in, queries, new_kv, cache_pool, cache_len, block_holder, block_slot, decode_holder, decode_slot, out_weight, norm_gain, router_weight, expert_routes, w_gate, w_up, w_down):

    def one_request(request):
        return request_attention(queries, new_kv, cache_pool, cache_len, block_holder, block_slot, request)
    attended = lax.map(one_request, jnp.arange(REQS).astype(jnp.int32)).reshape(TOKENS, QH * HD)
    residual = (hidden_in.astype(jnp.float32) + jnp.dot(attended, out_weight, preferred_element_type=jnp.float32)).astype(jnp.bfloat16)
    resid_float = residual.astype(jnp.float32)
    scaled = resid_float * norm_gain.astype(jnp.float32)[None, :]
    inverse = lax.rsqrt(lax.optimization_barrier(jnp.mean(resid_float * resid_float, axis=1)) + EPSILON)
    logits = inverse[:, None] * jnp.dot(scaled, router_weight, precision=lax.Precision.HIGHEST)
    chosen_logit = jnp.take_along_axis(logits, expert_routes, axis=1)
    lifted = jnp.exp(chosen_logit)
    gates = lifted / lax.optimization_barrier(jnp.sum(lifted, axis=1, keepdims=True))
    normed = (scaled * inverse[:, None]).astype(jnp.bfloat16)
    moe_out = expert_layer(normed, gates, expert_routes, w_gate, w_up, w_down)
    layer_out = (resid_float + moe_out).astype(jnp.bfloat16)
    decode_pool = relay_blocks(new_kv, cache_pool, cache_len, block_holder, block_slot, decode_holder, decode_slot)
    return (layer_out, decode_pool)
```

```python
import math

import jax
import jax.numpy as jnp
from jax import lax
from jax.sharding import PartitionSpec as P

D = 2560
CAP = 8


EPSILON = 1e-05
MASKED = -1e30


def head_rows(asked_rows, head_count, head_dim):
    stretch_len = asked_rows.shape[0]
    return (
        asked_rows.reshape(stretch_len, head_count, head_dim)
        .transpose(1, 0, 2)
        .reshape(head_count * stretch_len, head_dim)
    )


def absorb(carried, scores, value_rows):
    running_max, denominator, accumulated = carried
    new_max = jnp.maximum(running_max, jnp.max(scores, axis=1))
    decay = jnp.exp(running_max - new_max)
    raised = jnp.exp(scores - new_max[:, None])
    denominator = denominator * decay + jnp.sum(raised, axis=1)
    accumulated = accumulated * decay[:, None] + jnp.dot(
        raised.astype(jnp.bfloat16), value_rows, preferred_element_type=jnp.float32
    )
    return (new_max, denominator, accumulated)


def attend_blocks(carried, query_rows, blocks, present, scale):
    block_count = blocks.shape[0]
    block_len = blocks.shape[1]
    head_dim = blocks.shape[3]
    tile_blocks = min(32, block_count)
    span = tile_blocks * block_len
    flags = present.astype(jnp.int32)
    live_count = jnp.sum(flags)
    order_rank = jnp.cumsum(flags) - 1
    positions = jnp.arange(block_count)
    chosen = present[None, :] & (order_rank[None, :] == positions[:, None])
    packing = jnp.sum(jnp.where(chosen, positions[None, :], 0), axis=1)
    packed = blocks[packing]

    def advance(turn, state_now):
        segment = lax.dynamic_slice_in_dim(packed, turn * tile_blocks, tile_blocks, 0)
        key_rows = segment[:, :, 0].reshape(span, head_dim)
        value_rows = segment[:, :, 1].reshape(span, head_dim)
        scores = (
            jnp.einsum("qd,kd->qk", query_rows, key_rows, preferred_element_type=jnp.float32)
            * scale
        )
        is_live = turn * tile_blocks + jnp.arange(span) // block_len < live_count
        scores = jnp.where(is_live[None, :], scores, MASKED)
        return absorb(state_now, scores, value_rows)

    return lax.fori_loop(0, (live_count + tile_blocks - 1) // tile_blocks, advance, carried)


def per_device(
    hidden_in,
    queries,
    new_kv,
    cache_pool,
    cache_len,
    block_holder,
    block_slot,
    decode_holder,
    decode_slot,
    out_weight,
    norm_gain,
    router_weight,
    expert_routes,
    w_gate,
    w_up,
    w_down,
):
    blk_count = lax.axis_size("blk")
    own_index = lax.axis_index("blk")
    stretch_len = queries.shape[0]
    head_dim = new_kv.shape[3]
    head_count = queries.shape[1] // head_dim
    pool_size = cache_pool.shape[0]
    block_len = cache_pool.shape[1]
    max_blocks = block_holder.shape[1]
    fresh_count = stretch_len // block_len
    scale = 1.0 / math.sqrt(head_dim)
    devices = jnp.arange(blk_count)
    in_use = jnp.arange(max_blocks)[None, :] < (cache_len // block_len)[:, None]
    pool_rows = cache_pool[:, :, 0]
    fresh_rows = new_kv[:, 0]
    sources = jnp.concatenate(
        [pool_rows, fresh_rows.reshape(fresh_count, block_len, 2, head_dim)], axis=0
    )
    held_here = in_use & (block_holder == own_index)
    old_target = jnp.where(held_here, decode_holder[:, :max_blocks], blk_count).reshape(-1)
    pick_old = jax.ops.segment_sum((block_slot + 1).reshape(-1), old_target, num_segments=blk_count)
    pick_new = jax.ops.segment_sum(
        pool_size + 1 + jnp.arange(fresh_count),
        decode_holder[own_index, max_blocks:],
        num_segments=blk_count,
    )
    picked = pick_old + pick_new
    sending = jnp.where(
        (picked > 0)[:, None, None, None],
        sources[jnp.maximum(picked - 1, 0)],
        jnp.zeros((), jnp.bfloat16),
    )
    landed = lax.all_to_all(sending, "blk", split_axis=0, concat_axis=0, tiled=True)
    source_request = jnp.zeros_like(devices) + own_index
    match_here = (block_holder[devices] == own_index) & in_use[devices]
    outgoing = pool_rows[jnp.sum(jnp.where(match_here, block_slot[devices], 0), axis=1)]
    arrived = lax.all_to_all(outgoing, "blk", split_axis=0, concat_axis=0, tiled=True)
    present = jnp.any(
        (block_holder[source_request] == devices[:, None]) & in_use[source_request], axis=1
    )
    own_rows = head_rows(queries, head_count, head_dim)
    row_count = head_count * stretch_len
    start_state = (
        jnp.full((row_count,), MASKED, jnp.float32),
        jnp.zeros((row_count,), jnp.float32),
        jnp.zeros((row_count, head_dim), jnp.float32),
    )
    query_pos = jnp.arange(row_count) % stretch_len
    allowed = jnp.arange(stretch_len)[None, :] <= query_pos[:, None]
    local_scores = (
        jnp.einsum("qd,kd->qk", own_rows, fresh_rows[:, 0], preferred_element_type=jnp.float32)
        * scale
    )
    carried = absorb(start_state, jnp.where(allowed, local_scores, MASKED), fresh_rows[:, 1])
    carried = attend_blocks(carried, own_rows, arrived, present, scale)
    running_max, denominator, accumulated = carried
    attended = (
        (accumulated / denominator[:, None])
        .reshape(head_count, stretch_len, head_dim)
        .transpose(1, 0, 2)
    )
    attended = attended.reshape(stretch_len, head_count * head_dim).astype(jnp.bfloat16)
    every_token = lax.all_gather(attended, "blk", axis=0, tiled=True)
    column_part = jnp.dot(
        every_token, out_weight, preferred_element_type=jnp.float32
    ).astype(jnp.bfloat16)
    projected = lax.all_to_all(column_part, "blk", split_axis=0, concat_axis=1, tiled=True)
    head_total = lax.psum_scatter(
        projected, "kv", scatter_dimension=1, tiled=True
    ).astype(jnp.float32)
    residual = (hidden_in.astype(jnp.float32) + head_total).astype(jnp.bfloat16)
    resid_float = residual.astype(jnp.float32)
    scaled = resid_float * norm_gain.astype(jnp.float32)[None, :]
    square_sum, raw_logits = lax.psum(
        (
            jnp.sum(resid_float * resid_float, axis=1),
            jnp.dot(scaled, router_weight, precision=lax.Precision.HIGHEST),
        ),
        "kv",
    )
    inverse = lax.rsqrt(square_sum / D + EPSILON)
    logits = raw_logits * inverse[:, None]
    normed = (scaled * inverse[:, None]).astype(jnp.bfloat16)
    expert_count = router_weight.shape[1]
    top_count = expert_routes.shape[1]
    chosen_logit = jnp.sum(
        jnp.where(
            expert_routes[:, :, None] == jnp.arange(expert_count)[None, None, :],
            logits[:, None, :],
            0.0,
        ),
        axis=2,
    )
    lifted = jnp.exp(chosen_logit)
    gates = lifted / jnp.sum(lifted, axis=1, keepdims=True)
    capacity = CAP
    flat_routes = expert_routes.reshape(-1)
    assign_count = flat_routes.shape[0]
    onehot = (flat_routes[:, None] == jnp.arange(expert_count)[None, :]).astype(jnp.int32)
    earlier = jnp.cumsum(onehot, axis=0) - onehot
    slot_rank = jnp.sum(earlier * onehot, axis=1)
    target = flat_routes * capacity + slot_rank
    slot_total = expert_count * capacity
    source_item = jax.ops.segment_sum(jnp.arange(assign_count) + 1, target, num_segments=slot_total)
    packed_rows = jnp.where(
        (source_item > 0)[:, None],
        normed[jnp.maximum(source_item - 1, 0) // top_count],
        jnp.zeros((), jnp.bfloat16),
    )
    pieces_here = w_gate.shape[0]
    feature_part = normed.shape[1]
    doubled = jnp.broadcast_to(
        packed_rows.reshape(expert_count, 1, capacity, feature_part),
        (expert_count, 2, capacity, feature_part),
    )
    doubled = doubled.reshape(blk_count, pieces_here, capacity, feature_part)
    rows_in = lax.all_to_all(doubled, "blk", split_axis=0, concat_axis=0, tiled=True)
    gate_part = jnp.einsum("spkd,pdu->spku", rows_in, w_gate, preferred_element_type=jnp.float32)
    up_part = jnp.einsum("spkd,pdu->spku", rows_in, w_up, preferred_element_type=jnp.float32)
    both_parts = jnp.stack([gate_part, up_part], axis=3)
    whole = lax.psum(both_parts.astype(jnp.bfloat16), "kv").astype(jnp.float32)
    hidden = (jax.nn.silu(whole[:, :, :, 0]) * whole[:, :, :, 1]).astype(jnp.bfloat16)
    piece_out = jnp.einsum(
        "spku,pud->spkd", hidden, w_down, preferred_element_type=jnp.float32
    ).astype(jnp.bfloat16)
    returned = lax.all_to_all(piece_out, "blk", split_axis=0, concat_axis=0, tiled=True)
    per_piece = returned.reshape(expert_count, 2, capacity, feature_part).astype(jnp.float32)
    per_slot = (per_piece[:, 0] + per_piece[:, 1]).reshape(slot_total, feature_part)
    routed = per_slot[target].reshape(stretch_len, top_count, feature_part)
    moe_out = jnp.sum(routed * gates[:, :, None], axis=1)
    layer_out = (resid_float + moe_out).astype(jnp.bfloat16)
    here_old = in_use & (decode_holder[:, :max_blocks] == own_index)
    from_old = jnp.where(here_old, block_holder, blk_count).reshape(-1)
    put_old = jax.ops.segment_sum(
        (decode_slot[:, :max_blocks] + 1).reshape(-1), from_old, num_segments=blk_count
    )
    here_new = decode_holder[:, max_blocks:] == own_index
    request_ids = jnp.broadcast_to(jnp.arange(decode_holder.shape[0])[:, None], here_new.shape)
    from_new = jnp.where(here_new, request_ids, blk_count).reshape(-1)
    put_new = jax.ops.segment_sum(
        (decode_slot[:, max_blocks:] + 1).reshape(-1), from_new, num_segments=blk_count
    )
    placing = put_old + put_new
    decode_size = pool_size + fresh_count
    placement = (placing[None, :] - 1 == jnp.arange(decode_size)[:, None]).astype(jnp.bfloat16)
    decoded = jnp.dot(
        placement, landed.reshape(blk_count, -1), preferred_element_type=jnp.float32
    ).astype(jnp.bfloat16)
    decode_pool = decoded.reshape(decode_size, block_len, 1, 2, head_dim)
    return (layer_out, decode_pool)


def solution(mesh):
    in_specs = (
        P("blk", "kv"),
        P("blk", "kv"),
        P("blk", "kv", None, None),
        P("blk", None, "kv", None, None),
        P(),
        P(),
        P(),
        P(),
        P(),
        P("kv", "blk"),
        P("kv"),
        P("kv", None),
        P("blk", None),
        P("blk", "kv", None),
        P("blk", "kv", None),
        P("blk", None, "kv"),
    )
    out_specs = (P("blk", "kv"), P("blk", None, "kv", None, None))
    return jax.shard_map(
        per_device, mesh=mesh, in_specs=in_specs, out_specs=out_specs, check_vma=False
    )
```

```python
import math

import jax
import jax.numpy as jnp
from jax import lax
from jax.sharding import PartitionSpec as P

D = 2560
CAP = 8


EPSILON = 1e-05
MASKED = -1e30


def head_rows(asked_rows, head_count, head_dim):
    stretch_len = asked_rows.shape[0]
    return (
        asked_rows.reshape(stretch_len, head_count, head_dim)
        .transpose(1, 0, 2)
        .reshape(head_count * stretch_len, head_dim)
    )


def absorb(carried, scores, value_rows):
    running_max, denominator, accumulated = carried
    new_max = jnp.maximum(running_max, jnp.max(scores, axis=1))
    decay = jnp.exp(running_max - new_max)
    raised = jnp.exp(scores - new_max[:, None])
    denominator = denominator * decay + jnp.sum(raised, axis=1)
    accumulated = accumulated * decay[:, None] + jnp.dot(
        raised.astype(jnp.bfloat16), value_rows, preferred_element_type=jnp.float32
    )
    return (new_max, denominator, accumulated)


def attend_blocks(carried, query_rows, blocks, present, scale):
    block_count = blocks.shape[0]
    block_len = blocks.shape[1]
    head_dim = blocks.shape[3]
    tile_blocks = min(32, block_count)
    span = tile_blocks * block_len
    flags = present.astype(jnp.int32)
    live_count = jnp.sum(flags)
    order_rank = jnp.cumsum(flags) - 1
    positions = jnp.arange(block_count)
    chosen = present[None, :] & (order_rank[None, :] == positions[:, None])
    packing = jnp.sum(jnp.where(chosen, positions[None, :], 0), axis=1)
    packed = blocks[packing]

    def advance(turn, state_now):
        segment = lax.dynamic_slice_in_dim(packed, turn * tile_blocks, tile_blocks, 0)
        key_rows = segment[:, :, 0].reshape(span, head_dim)
        value_rows = segment[:, :, 1].reshape(span, head_dim)
        scores = (
            jnp.einsum("qd,kd->qk", query_rows, key_rows, preferred_element_type=jnp.float32)
            * scale
        )
        is_live = turn * tile_blocks + jnp.arange(span) // block_len < live_count
        scores = jnp.where(is_live[None, :], scores, MASKED)
        return absorb(state_now, scores, value_rows)

    return lax.fori_loop(0, (live_count + tile_blocks - 1) // tile_blocks, advance, carried)


def per_device(
    hidden_in,
    queries,
    new_kv,
    cache_pool,
    cache_len,
    block_holder,
    block_slot,
    decode_holder,
    decode_slot,
    out_weight,
    norm_gain,
    router_weight,
    expert_routes,
    w_gate,
    w_up,
    w_down,
):
    blk_count = lax.axis_size("blk")
    own_index = lax.axis_index("blk")
    stretch_len = queries.shape[0]
    head_dim = new_kv.shape[3]
    head_count = queries.shape[1] // head_dim
    pool_size = cache_pool.shape[0]
    block_len = cache_pool.shape[1]
    max_blocks = block_holder.shape[1]
    fresh_count = stretch_len // block_len
    scale = 1.0 / math.sqrt(head_dim)
    devices = jnp.arange(blk_count)
    in_use = jnp.arange(max_blocks)[None, :] < (cache_len // block_len)[:, None]
    pool_rows = cache_pool[:, :, 0]
    fresh_rows = new_kv[:, 0]
    sources = jnp.concatenate(
        [pool_rows, fresh_rows.reshape(fresh_count, block_len, 2, head_dim)], axis=0
    )
    held_here = in_use & (block_holder == own_index)
    old_target = jnp.where(held_here, decode_holder[:, :max_blocks], blk_count).reshape(-1)
    pick_old = jax.ops.segment_sum((block_slot + 1).reshape(-1), old_target, num_segments=blk_count)
    pick_new = jax.ops.segment_sum(
        pool_size + 1 + jnp.arange(fresh_count),
        decode_holder[own_index, max_blocks:],
        num_segments=blk_count,
    )
    picked = pick_old + pick_new
    sending = jnp.where(
        (picked > 0)[:, None, None, None],
        sources[jnp.maximum(picked - 1, 0)],
        jnp.zeros((), jnp.bfloat16),
    )
    landed = lax.all_to_all(sending, "blk", split_axis=0, concat_axis=0, tiled=True)
    source_request = jnp.zeros_like(devices) + own_index
    match_here = (block_holder[devices] == own_index) & in_use[devices]
    outgoing = pool_rows[jnp.sum(jnp.where(match_here, block_slot[devices], 0), axis=1)]
    arrived = lax.all_to_all(outgoing, "blk", split_axis=0, concat_axis=0, tiled=True)
    present = jnp.any(
        (block_holder[source_request] == devices[:, None]) & in_use[source_request], axis=1
    )
    own_rows = head_rows(queries, head_count, head_dim)
    row_count = head_count * stretch_len
    start_state = (
        jnp.full((row_count,), MASKED, jnp.float32),
        jnp.zeros((row_count,), jnp.float32),
        jnp.zeros((row_count, head_dim), jnp.float32),
    )
    query_pos = jnp.arange(row_count) % stretch_len
    allowed = jnp.arange(stretch_len)[None, :] <= query_pos[:, None]
    local_scores = (
        jnp.einsum("qd,kd->qk", own_rows, fresh_rows[:, 0], preferred_element_type=jnp.float32)
        * scale
    )
    carried = absorb(start_state, jnp.where(allowed, local_scores, MASKED), fresh_rows[:, 1])
    carried = attend_blocks(carried, own_rows, arrived, present, scale)
    running_max, denominator, accumulated = carried
    attended = (
        (accumulated / denominator[:, None])
        .reshape(head_count, stretch_len, head_dim)
        .transpose(1, 0, 2)
    )
    attended = attended.reshape(stretch_len, head_count * head_dim).astype(jnp.bfloat16)
    every_token = lax.all_to_all(
        jnp.broadcast_to(attended[None], (blk_count,) + attended.shape), "blk", 0, 0, tiled=True
    ).reshape(-1, attended.shape[1])
    column_part = jnp.dot(
        every_token, out_weight, preferred_element_type=jnp.float32
    ).astype(jnp.bfloat16)
    projected = lax.all_to_all(column_part, "blk", split_axis=0, concat_axis=1, tiled=True)
    head_total = lax.psum_scatter(
        projected, "kv", scatter_dimension=1, tiled=True
    ).astype(jnp.float32)
    residual = (hidden_in.astype(jnp.float32) + head_total).astype(jnp.bfloat16)
    resid_float = residual.astype(jnp.float32)
    scaled = resid_float * norm_gain.astype(jnp.float32)[None, :]
    square_sum, raw_logits = lax.psum(
        (
            jnp.sum(resid_float * resid_float, axis=1),
            jnp.dot(scaled, router_weight, precision=lax.Precision.HIGHEST),
        ),
        "kv",
    )
    inverse = lax.rsqrt(square_sum / D + EPSILON)
    logits = raw_logits * inverse[:, None]
    normed = (scaled * inverse[:, None]).astype(jnp.bfloat16)
    expert_count = router_weight.shape[1]
    top_count = expert_routes.shape[1]
    chosen_logit = jnp.sum(
        jnp.where(
            expert_routes[:, :, None] == jnp.arange(expert_count)[None, None, :],
            logits[:, None, :],
            0.0,
        ),
        axis=2,
    )
    lifted = jnp.exp(chosen_logit)
    gates = lifted / jnp.sum(lifted, axis=1, keepdims=True)
    capacity = CAP
    flat_routes = expert_routes.reshape(-1)
    assign_count = flat_routes.shape[0]
    onehot = (flat_routes[:, None] == jnp.arange(expert_count)[None, :]).astype(jnp.int32)
    earlier = jnp.cumsum(onehot, axis=0) - onehot
    slot_rank = jnp.sum(earlier * onehot, axis=1)
    target = flat_routes * capacity + slot_rank
    slot_total = expert_count * capacity
    source_item = jax.ops.segment_sum(jnp.arange(assign_count) + 1, target, num_segments=slot_total)
    packed_rows = jnp.where(
        (source_item > 0)[:, None],
        normed[jnp.maximum(source_item - 1, 0) // top_count],
        jnp.zeros((), jnp.bfloat16),
    )
    pieces_here = w_gate.shape[0]
    feature_part = normed.shape[1]
    kv_count = lax.axis_size("kv")
    hidden_len = w_gate.shape[2]
    hidden_part = hidden_len // kv_count
    paired = pieces_here % 2 == 0
    if paired:
        experts_here = pieces_here // 2
        sent = packed_rows.reshape(blk_count, experts_here, capacity, feature_part)
        landed_rows = lax.all_to_all(sent, "blk", split_axis=0, concat_axis=0, tiled=True)
        rows_in = jnp.broadcast_to(
            landed_rows[:, :, None], (blk_count, experts_here, 2, capacity, feature_part)
        ).reshape(blk_count, pieces_here, capacity, feature_part)
    else:
        doubled = jnp.broadcast_to(
            packed_rows.reshape(expert_count, 1, capacity, feature_part),
            (expert_count, 2, capacity, feature_part),
        )
        doubled = doubled.reshape(blk_count, pieces_here, capacity, feature_part)
        rows_in = lax.all_to_all(doubled, "blk", split_axis=0, concat_axis=0, tiled=True)
    gate_w = w_gate.reshape(pieces_here, feature_part, kv_count, hidden_part)
    up_w = w_up.reshape(pieces_here, feature_part, kv_count, hidden_part)
    gate_part = jnp.einsum("spkd,pdcv->cspkv", rows_in, gate_w, preferred_element_type=jnp.float32)
    up_part = jnp.einsum("spkd,pdcv->cspkv", rows_in, up_w, preferred_element_type=jnp.float32)
    both_parts = jnp.stack([gate_part, up_part], axis=1).astype(jnp.bfloat16)
    share_shape = both_parts.shape[1:]
    own_share = lax.psum_scatter(
        both_parts.reshape(-1, hidden_part), "kv", scatter_dimension=0, tiled=True
    )
    own_share = own_share.reshape(share_shape).astype(jnp.float32)
    hidden_share = (jax.nn.silu(own_share[0]) * own_share[1]).astype(jnp.bfloat16)
    hidden = lax.all_gather(hidden_share, "kv", axis=0)
    down_w = w_down.reshape(pieces_here, kv_count, hidden_part, feature_part)
    piece_out = jnp.einsum(
        "cspkv,pcvd->spkd", hidden, down_w, preferred_element_type=jnp.float32
    ).astype(jnp.bfloat16)
    if paired:
        half_sum = piece_out.reshape(blk_count, experts_here, 2, capacity, feature_part)
        half_sum = jnp.sum(half_sum.astype(jnp.float32), axis=2).astype(jnp.bfloat16)
        returned = lax.all_to_all(half_sum, "blk", split_axis=0, concat_axis=0, tiled=True)
        per_slot = returned.reshape(slot_total, feature_part).astype(jnp.float32)
    else:
        returned = lax.all_to_all(piece_out, "blk", split_axis=0, concat_axis=0, tiled=True)
        per_piece = returned.reshape(expert_count, 2, capacity, feature_part).astype(jnp.float32)
        per_slot = (per_piece[:, 0] + per_piece[:, 1]).reshape(slot_total, feature_part)
    routed = per_slot[target].reshape(stretch_len, top_count, feature_part)
    moe_out = jnp.sum(routed * gates[:, :, None], axis=1)
    layer_out = (resid_float + moe_out).astype(jnp.bfloat16)
    here_old = in_use & (decode_holder[:, :max_blocks] == own_index)
    from_old = jnp.where(here_old, block_holder, blk_count).reshape(-1)
    put_old = jax.ops.segment_sum(
        (decode_slot[:, :max_blocks] + 1).reshape(-1), from_old, num_segments=blk_count
    )
    here_new = decode_holder[:, max_blocks:] == own_index
    request_ids = jnp.broadcast_to(jnp.arange(decode_holder.shape[0])[:, None], here_new.shape)
    from_new = jnp.where(here_new, request_ids, blk_count).reshape(-1)
    put_new = jax.ops.segment_sum(
        (decode_slot[:, max_blocks:] + 1).reshape(-1), from_new, num_segments=blk_count
    )
    placing = put_old + put_new
    decode_size = pool_size + fresh_count
    placement = (placing[None, :] - 1 == jnp.arange(decode_size)[:, None]).astype(jnp.bfloat16)
    decoded = jnp.dot(
        placement, landed.reshape(blk_count, -1), preferred_element_type=jnp.float32
    ).astype(jnp.bfloat16)
    decode_pool = decoded.reshape(decode_size, block_len, 1, 2, head_dim)
    return (layer_out, decode_pool)


def solution(mesh):
    in_specs = (
        P("blk", "kv"),
        P("blk", "kv"),
        P("blk", "kv", None, None),
        P("blk", None, "kv", None, None),
        P(),
        P(),
        P(),
        P(),
        P(),
        P("kv", "blk"),
        P("kv"),
        P("kv", None),
        P("blk", None),
        P("blk", "kv", None),
        P("blk", "kv", None),
        P("blk", None, "kv"),
    )
    out_specs = (P("blk", "kv"), P("blk", None, "kv", None, None))
    return jax.shard_map(
        per_device, mesh=mesh, in_specs=in_specs, out_specs=out_specs, check_vma=False
    )
```

```python
import math

import jax
import jax.numpy as jnp
from jax import lax
from jax.sharding import PartitionSpec as P

D = 2560
CAP = 8


EPSILON = 1e-05
MASKED = -1e30


def head_rows(asked_rows, head_count, head_dim):
    stretch_len = asked_rows.shape[0]
    return (
        asked_rows.reshape(stretch_len, head_count, head_dim)
        .transpose(1, 0, 2)
        .reshape(head_count * stretch_len, head_dim)
    )


def absorb(carried, scores, value_rows):
    running_max, denominator, accumulated = carried
    new_max = jnp.maximum(running_max, jnp.max(scores, axis=1))
    decay = jnp.exp(running_max - new_max)
    raised = jnp.exp(scores - new_max[:, None])
    denominator = denominator * decay + jnp.sum(raised, axis=1)
    accumulated = accumulated * decay[:, None] + jnp.dot(
        raised.astype(jnp.bfloat16), value_rows, preferred_element_type=jnp.float32
    )
    return (new_max, denominator, accumulated)


def attend_blocks(carried, query_rows, blocks, present, scale):
    block_count = blocks.shape[0]
    block_len = blocks.shape[1]
    head_dim = blocks.shape[3]
    tile_blocks = min(32, block_count)
    span = tile_blocks * block_len
    flags = present.astype(jnp.int32)
    live_count = jnp.sum(flags)
    order_rank = jnp.cumsum(flags) - 1
    positions = jnp.arange(block_count)
    chosen = present[None, :] & (order_rank[None, :] == positions[:, None])
    packing = jnp.sum(jnp.where(chosen, positions[None, :], 0), axis=1)
    packed = blocks[packing]

    def advance(turn, state_now):
        segment = lax.dynamic_slice_in_dim(packed, turn * tile_blocks, tile_blocks, 0)
        key_rows = segment[:, :, 0].reshape(span, head_dim)
        value_rows = segment[:, :, 1].reshape(span, head_dim)
        scores = (
            jnp.einsum("qd,kd->qk", query_rows, key_rows, preferred_element_type=jnp.float32)
            * scale
        )
        is_live = turn * tile_blocks + jnp.arange(span) // block_len < live_count
        scores = jnp.where(is_live[None, :], scores, MASKED)
        return absorb(state_now, scores, value_rows)

    return lax.fori_loop(0, (live_count + tile_blocks - 1) // tile_blocks, advance, carried)


def per_device(
    hidden_in,
    queries,
    new_kv,
    cache_pool,
    cache_len,
    block_holder,
    block_slot,
    decode_holder,
    decode_slot,
    out_weight,
    norm_gain,
    router_weight,
    expert_routes,
    w_gate,
    w_up,
    w_down,
):
    blk_count = lax.axis_size("blk")
    own_index = lax.axis_index("blk")
    stretch_len = queries.shape[0]
    head_dim = new_kv.shape[3]
    head_count = queries.shape[1] // head_dim
    pool_size = cache_pool.shape[0]
    block_len = cache_pool.shape[1]
    max_blocks = block_holder.shape[1]
    fresh_count = stretch_len // block_len
    scale = 1.0 / math.sqrt(head_dim)
    devices = jnp.arange(blk_count)
    in_use = jnp.arange(max_blocks)[None, :] < (cache_len // block_len)[:, None]
    pool_rows = cache_pool[:, :, 0]
    fresh_rows = new_kv[:, 0]
    sources = jnp.concatenate(
        [pool_rows, fresh_rows.reshape(fresh_count, block_len, 2, head_dim)], axis=0
    )
    held_here = in_use & (block_holder == own_index)
    old_target = jnp.where(held_here, decode_holder[:, :max_blocks], blk_count).reshape(-1)
    pick_old = jax.ops.segment_sum((block_slot + 1).reshape(-1), old_target, num_segments=blk_count)
    pick_new = jax.ops.segment_sum(
        pool_size + 1 + jnp.arange(fresh_count),
        decode_holder[own_index, max_blocks:],
        num_segments=blk_count,
    )
    picked = pick_old + pick_new
    sending = jnp.where(
        (picked > 0)[:, None, None, None],
        sources[jnp.maximum(picked - 1, 0)],
        jnp.zeros((), jnp.bfloat16),
    )
    landed = lax.all_to_all(sending, "blk", split_axis=0, concat_axis=0, tiled=True)
    source_request = jnp.zeros_like(devices) + own_index
    match_here = (block_holder[devices] == own_index) & in_use[devices]
    outgoing = pool_rows[jnp.sum(jnp.where(match_here, block_slot[devices], 0), axis=1)]
    arrived = lax.all_to_all(outgoing, "blk", split_axis=0, concat_axis=0, tiled=True)
    present = jnp.any(
        (block_holder[source_request] == devices[:, None]) & in_use[source_request], axis=1
    )
    own_rows = head_rows(queries, head_count, head_dim)
    row_count = head_count * stretch_len
    start_state = (
        jnp.full((row_count,), MASKED, jnp.float32),
        jnp.zeros((row_count,), jnp.float32),
        jnp.zeros((row_count, head_dim), jnp.float32),
    )
    query_pos = jnp.arange(row_count) % stretch_len
    allowed = jnp.arange(stretch_len)[None, :] <= query_pos[:, None]
    local_scores = (
        jnp.einsum("qd,kd->qk", own_rows, fresh_rows[:, 0], preferred_element_type=jnp.float32)
        * scale
    )
    carried = absorb(start_state, jnp.where(allowed, local_scores, MASKED), fresh_rows[:, 1])
    carried = attend_blocks(carried, own_rows, arrived, present, scale)
    running_max, denominator, accumulated = carried
    attended = (
        (accumulated / denominator[:, None])
        .reshape(head_count, stretch_len, head_dim)
        .transpose(1, 0, 2)
    )
    attended = attended.reshape(stretch_len, head_count * head_dim).astype(jnp.bfloat16)
    every_token = lax.all_to_all(
        jnp.broadcast_to(attended[None], (blk_count,) + attended.shape), "blk", 0, 0, tiled=True
    ).reshape(-1, attended.shape[1])
    column_part = jnp.dot(
        every_token, out_weight, preferred_element_type=jnp.float32
    ).astype(jnp.bfloat16)
    projected = lax.all_to_all(column_part, "blk", split_axis=0, concat_axis=1, tiled=True)
    head_total = lax.psum_scatter(
        projected, "kv", scatter_dimension=1, tiled=True
    ).astype(jnp.float32)
    residual = (hidden_in.astype(jnp.float32) + head_total).astype(jnp.bfloat16)
    resid_float = residual.astype(jnp.float32)
    scaled = resid_float * norm_gain.astype(jnp.float32)[None, :]
    square_sum, raw_logits = lax.psum(
        (
            jnp.sum(resid_float * resid_float, axis=1),
            jnp.dot(scaled, router_weight, precision=lax.Precision.HIGHEST),
        ),
        "kv",
    )
    inverse = lax.rsqrt(square_sum / D + EPSILON)
    logits = raw_logits * inverse[:, None]
    normed = (scaled * inverse[:, None]).astype(jnp.bfloat16)
    expert_count = router_weight.shape[1]
    top_count = expert_routes.shape[1]
    chosen_logit = jnp.sum(
        jnp.where(
            expert_routes[:, :, None] == jnp.arange(expert_count)[None, None, :],
            logits[:, None, :],
            0.0,
        ),
        axis=2,
    )
    lifted = jnp.exp(chosen_logit)
    gates = lifted / jnp.sum(lifted, axis=1, keepdims=True)
    capacity = CAP
    flat_routes = expert_routes.reshape(-1)
    assign_count = flat_routes.shape[0]
    onehot = (flat_routes[:, None] == jnp.arange(expert_count)[None, :]).astype(jnp.int32)
    earlier = jnp.cumsum(onehot, axis=0) - onehot
    slot_rank = jnp.sum(earlier * onehot, axis=1)
    target = flat_routes * capacity + slot_rank
    slot_total = expert_count * capacity
    source_item = jax.ops.segment_sum(jnp.arange(assign_count) + 1, target, num_segments=slot_total)
    packed_rows = jnp.where(
        (source_item > 0)[:, None],
        normed[jnp.maximum(source_item - 1, 0) // top_count],
        jnp.zeros((), jnp.bfloat16),
    )
    pieces_here = w_gate.shape[0]
    feature_part = normed.shape[1]
    paired = pieces_here % 2 == 0
    if paired:
        experts_here = pieces_here // 2
        sent = packed_rows.reshape(blk_count, experts_here, capacity, feature_part)
        landed_rows = lax.all_to_all(sent, "blk", split_axis=0, concat_axis=0, tiled=True)
        rows_in = jnp.broadcast_to(
            landed_rows[:, :, None], (blk_count, experts_here, 2, capacity, feature_part)
        ).reshape(blk_count, pieces_here, capacity, feature_part)
    else:
        doubled = jnp.broadcast_to(
            packed_rows.reshape(expert_count, 1, capacity, feature_part),
            (expert_count, 2, capacity, feature_part),
        )
        doubled = doubled.reshape(blk_count, pieces_here, capacity, feature_part)
        rows_in = lax.all_to_all(doubled, "blk", split_axis=0, concat_axis=0, tiled=True)
    gate_part = jnp.einsum("spkd,pdu->spku", rows_in, w_gate, preferred_element_type=jnp.float32)
    up_part = jnp.einsum("spkd,pdu->spku", rows_in, w_up, preferred_element_type=jnp.float32)
    both_parts = jnp.stack([gate_part, up_part], axis=3)
    whole = lax.psum(both_parts.astype(jnp.bfloat16), "kv").astype(jnp.float32)
    hidden = (jax.nn.silu(whole[:, :, :, 0]) * whole[:, :, :, 1]).astype(jnp.bfloat16)
    piece_out = jnp.einsum(
        "spku,pud->spkd", hidden, w_down, preferred_element_type=jnp.float32
    ).astype(jnp.bfloat16)
    if paired:
        half_sum = piece_out.reshape(blk_count, experts_here, 2, capacity, feature_part)
        half_sum = jnp.sum(half_sum.astype(jnp.float32), axis=2).astype(jnp.bfloat16)
        returned = lax.all_to_all(half_sum, "blk", split_axis=0, concat_axis=0, tiled=True)
        per_slot = returned.reshape(slot_total, feature_part).astype(jnp.float32)
    else:
        returned = lax.all_to_all(piece_out, "blk", split_axis=0, concat_axis=0, tiled=True)
        per_piece = returned.reshape(expert_count, 2, capacity, feature_part).astype(jnp.float32)
        per_slot = (per_piece[:, 0] + per_piece[:, 1]).reshape(slot_total, feature_part)
    routed = per_slot[target].reshape(stretch_len, top_count, feature_part)
    moe_out = jnp.sum(routed * gates[:, :, None], axis=1)
    layer_out = (resid_float + moe_out).astype(jnp.bfloat16)
    here_old = in_use & (decode_holder[:, :max_blocks] == own_index)
    from_old = jnp.where(here_old, block_holder, blk_count).reshape(-1)
    put_old = jax.ops.segment_sum(
        (decode_slot[:, :max_blocks] + 1).reshape(-1), from_old, num_segments=blk_count
    )
    here_new = decode_holder[:, max_blocks:] == own_index
    request_ids = jnp.broadcast_to(jnp.arange(decode_holder.shape[0])[:, None], here_new.shape)
    from_new = jnp.where(here_new, request_ids, blk_count).reshape(-1)
    put_new = jax.ops.segment_sum(
        (decode_slot[:, max_blocks:] + 1).reshape(-1), from_new, num_segments=blk_count
    )
    placing = put_old + put_new
    decode_size = pool_size + fresh_count
    placement = (placing[None, :] - 1 == jnp.arange(decode_size)[:, None]).astype(jnp.bfloat16)
    decoded = jnp.dot(
        placement, landed.reshape(blk_count, -1), preferred_element_type=jnp.float32
    ).astype(jnp.bfloat16)
    decode_pool = decoded.reshape(decode_size, block_len, 1, 2, head_dim)
    return (layer_out, decode_pool)


def solution(mesh):
    in_specs = (
        P("blk", "kv"),
        P("blk", "kv"),
        P("blk", "kv", None, None),
        P("blk", None, "kv", None, None),
        P(),
        P(),
        P(),
        P(),
        P(),
        P("kv", "blk"),
        P("kv"),
        P("kv", None),
        P("blk", None),
        P("blk", "kv", None),
        P("blk", "kv", None),
        P("blk", None, "kv"),
    )
    out_specs = (P("blk", "kv"), P("blk", None, "kv", None, None))
    return jax.shard_map(
        per_device, mesh=mesh, in_specs=in_specs, out_specs=out_specs, check_vma=False
    )
```

```python
import math

import jax
import jax.numpy as jnp
from jax import lax
from jax.sharding import PartitionSpec as P

D = 2560
CAP = 8


EPSILON = 1e-05
MASKED = -1e30


def head_rows(asked_rows, head_count, head_dim):
    stretch_len = asked_rows.shape[0]
    return (
        asked_rows.reshape(stretch_len, head_count, head_dim)
        .transpose(1, 0, 2)
        .reshape(head_count * stretch_len, head_dim)
    )


def absorb(carried, scores, value_rows):
    running_max, denominator, accumulated = carried
    new_max = jnp.maximum(running_max, jnp.max(scores, axis=1))
    decay = jnp.exp(running_max - new_max)
    raised = jnp.exp(scores - new_max[:, None])
    denominator = denominator * decay + jnp.sum(raised, axis=1)
    accumulated = accumulated * decay[:, None] + jnp.dot(
        raised.astype(jnp.bfloat16), value_rows, preferred_element_type=jnp.float32
    )
    return (new_max, denominator, accumulated)


def attend_blocks(carried, query_rows, blocks, present, scale):
    block_count = blocks.shape[0]
    block_len = blocks.shape[1]
    head_dim = blocks.shape[3]
    tile_blocks = min(32, block_count)
    span = tile_blocks * block_len
    flags = present.astype(jnp.int32)
    live_count = jnp.sum(flags)
    order_rank = jnp.cumsum(flags) - 1
    positions = jnp.arange(block_count)
    chosen = present[None, :] & (order_rank[None, :] == positions[:, None])
    packing = jnp.sum(jnp.where(chosen, positions[None, :], 0), axis=1)
    packed = blocks[packing]

    def advance(turn, state_now):
        segment = lax.dynamic_slice_in_dim(packed, turn * tile_blocks, tile_blocks, 0)
        key_rows = segment[:, :, 0].reshape(span, head_dim)
        value_rows = segment[:, :, 1].reshape(span, head_dim)
        scores = (
            jnp.einsum("qd,kd->qk", query_rows, key_rows, preferred_element_type=jnp.float32)
            * scale
        )
        is_live = turn * tile_blocks + jnp.arange(span) // block_len < live_count
        scores = jnp.where(is_live[None, :], scores, MASKED)
        return absorb(state_now, scores, value_rows)

    return lax.fori_loop(0, (live_count + tile_blocks - 1) // tile_blocks, advance, carried)


def per_device(
    hidden_in,
    queries,
    new_kv,
    cache_pool,
    cache_len,
    block_holder,
    block_slot,
    decode_holder,
    decode_slot,
    out_weight,
    norm_gain,
    router_weight,
    expert_routes,
    w_gate,
    w_up,
    w_down,
):
    blk_count = lax.axis_size("blk")
    own_index = lax.axis_index("blk")
    stretch_len = queries.shape[0]
    head_dim = new_kv.shape[3]
    head_count = queries.shape[1] // head_dim
    pool_size = cache_pool.shape[0]
    block_len = cache_pool.shape[1]
    max_blocks = block_holder.shape[1]
    fresh_count = stretch_len // block_len
    scale = 1.0 / math.sqrt(head_dim)
    devices = jnp.arange(blk_count)
    in_use = jnp.arange(max_blocks)[None, :] < (cache_len // block_len)[:, None]
    pool_rows = cache_pool[:, :, 0]
    fresh_rows = new_kv[:, 0]
    sources = jnp.concatenate(
        [pool_rows, fresh_rows.reshape(fresh_count, block_len, 2, head_dim)], axis=0
    )
    held_here = in_use & (block_holder == own_index)
    old_target = jnp.where(held_here, decode_holder[:, :max_blocks], blk_count).reshape(-1)
    pick_old = jax.ops.segment_sum((block_slot + 1).reshape(-1), old_target, num_segments=blk_count)
    pick_new = jax.ops.segment_sum(
        pool_size + 1 + jnp.arange(fresh_count),
        decode_holder[own_index, max_blocks:],
        num_segments=blk_count,
    )
    picked = pick_old + pick_new
    sending = jnp.where(
        (picked > 0)[:, None, None, None],
        sources[jnp.maximum(picked - 1, 0)],
        jnp.zeros((), jnp.bfloat16),
    )
    landed = lax.all_to_all(sending, "blk", split_axis=0, concat_axis=0, tiled=True)
    source_request = jnp.zeros_like(devices) + own_index
    match_here = (block_holder[devices] == own_index) & in_use[devices]
    outgoing = pool_rows[jnp.sum(jnp.where(match_here, block_slot[devices], 0), axis=1)]
    arrived = lax.all_to_all(outgoing, "blk", split_axis=0, concat_axis=0, tiled=True)
    present = jnp.any(
        (block_holder[source_request] == devices[:, None]) & in_use[source_request], axis=1
    )
    own_rows = head_rows(queries, head_count, head_dim)
    row_count = head_count * stretch_len
    start_state = (
        jnp.full((row_count,), MASKED, jnp.float32),
        jnp.zeros((row_count,), jnp.float32),
        jnp.zeros((row_count, head_dim), jnp.float32),
    )
    query_pos = jnp.arange(row_count) % stretch_len
    allowed = jnp.arange(stretch_len)[None, :] <= query_pos[:, None]
    local_scores = (
        jnp.einsum("qd,kd->qk", own_rows, fresh_rows[:, 0], preferred_element_type=jnp.float32)
        * scale
    )
    carried = absorb(start_state, jnp.where(allowed, local_scores, MASKED), fresh_rows[:, 1])
    carried = attend_blocks(carried, own_rows, arrived, present, scale)
    running_max, denominator, accumulated = carried
    attended = (
        (accumulated / denominator[:, None])
        .reshape(head_count, stretch_len, head_dim)
        .transpose(1, 0, 2)
    )
    attended = attended.reshape(stretch_len, head_count * head_dim).astype(jnp.bfloat16)
    every_token = lax.all_to_all(
        jnp.broadcast_to(attended[None], (blk_count,) + attended.shape), "blk", 0, 0, tiled=True
    ).reshape(-1, attended.shape[1])
    column_part = jnp.dot(
        every_token, out_weight, preferred_element_type=jnp.float32
    ).astype(jnp.bfloat16)
    projected = lax.all_to_all(column_part, "blk", split_axis=0, concat_axis=1, tiled=True)
    kv_index = lax.axis_index("kv")
    if lax.axis_size("kv") == 4:
        chip_bit = kv_index // 2
        core_low = kv_index % 2
        swap_core = [(i, i ^ 1) for i in range(4)]
        swap_chip = [(i, i ^ 2) for i in range(4)]
        chip_cols = projected.shape[1] // 2
        chip_kept = lax.dynamic_slice_in_dim(projected, chip_bit * chip_cols, chip_cols, 1)
        chip_given = lax.dynamic_slice_in_dim(projected, (1 - chip_bit) * chip_cols, chip_cols, 1)
        chip_sum = chip_kept.astype(jnp.float32) + lax.ppermute(
            chip_given, "kv", swap_chip
        ).astype(jnp.float32)
        own_cols = chip_cols // 2
        core_kept = lax.dynamic_slice_in_dim(chip_sum, core_low * own_cols, own_cols, 1)
        core_given = lax.dynamic_slice_in_dim(
            chip_sum, (1 - core_low) * own_cols, own_cols, 1
        ).astype(jnp.bfloat16)
        head_total = core_kept + lax.ppermute(core_given, "kv", swap_core).astype(jnp.float32)
    else:
        head_total = lax.psum_scatter(
            projected, "kv", scatter_dimension=1, tiled=True
        ).astype(jnp.float32)
    residual = (hidden_in.astype(jnp.float32) + head_total).astype(jnp.bfloat16)
    resid_float = residual.astype(jnp.float32)
    scaled = resid_float * norm_gain.astype(jnp.float32)[None, :]
    square_sum, raw_logits = lax.psum(
        (
            jnp.sum(resid_float * resid_float, axis=1),
            jnp.dot(scaled, router_weight, precision=lax.Precision.HIGHEST),
        ),
        "kv",
    )
    inverse = lax.rsqrt(square_sum / D + EPSILON)
    logits = raw_logits * inverse[:, None]
    normed = (scaled * inverse[:, None]).astype(jnp.bfloat16)
    expert_count = router_weight.shape[1]
    top_count = expert_routes.shape[1]
    chosen_logit = jnp.sum(
        jnp.where(
            expert_routes[:, :, None] == jnp.arange(expert_count)[None, None, :],
            logits[:, None, :],
            0.0,
        ),
        axis=2,
    )
    lifted = jnp.exp(chosen_logit)
    gates = lifted / jnp.sum(lifted, axis=1, keepdims=True)
    capacity = CAP
    flat_routes = expert_routes.reshape(-1)
    assign_count = flat_routes.shape[0]
    onehot = (flat_routes[:, None] == jnp.arange(expert_count)[None, :]).astype(jnp.int32)
    earlier = jnp.cumsum(onehot, axis=0) - onehot
    slot_rank = jnp.sum(earlier * onehot, axis=1)
    target = flat_routes * capacity + slot_rank
    slot_total = expert_count * capacity
    source_item = jax.ops.segment_sum(jnp.arange(assign_count) + 1, target, num_segments=slot_total)
    packed_rows = jnp.where(
        (source_item > 0)[:, None],
        normed[jnp.maximum(source_item - 1, 0) // top_count],
        jnp.zeros((), jnp.bfloat16),
    )
    pieces_here = w_gate.shape[0]
    feature_part = normed.shape[1]
    paired = pieces_here % 2 == 0
    if paired:
        experts_here = pieces_here // 2
        sent = packed_rows.reshape(blk_count, experts_here, capacity, feature_part)
        landed_rows = lax.all_to_all(sent, "blk", split_axis=0, concat_axis=0, tiled=True)
        rows_in = jnp.broadcast_to(
            landed_rows[:, :, None], (blk_count, experts_here, 2, capacity, feature_part)
        ).reshape(blk_count, pieces_here, capacity, feature_part)
    else:
        doubled = jnp.broadcast_to(
            packed_rows.reshape(expert_count, 1, capacity, feature_part),
            (expert_count, 2, capacity, feature_part),
        )
        doubled = doubled.reshape(blk_count, pieces_here, capacity, feature_part)
        rows_in = lax.all_to_all(doubled, "blk", split_axis=0, concat_axis=0, tiled=True)
    gate_part = jnp.einsum("spkd,pdu->spku", rows_in, w_gate, preferred_element_type=jnp.float32)
    up_part = jnp.einsum("spkd,pdu->spku", rows_in, w_up, preferred_element_type=jnp.float32)
    both_parts = jnp.stack([gate_part, up_part], axis=3).astype(jnp.bfloat16)
    kv_count = lax.axis_size("kv")
    core_bit = lax.axis_index("kv") % 2
    flip_core = [(i, i ^ 1) for i in range(kv_count)]
    flip_chip = [(i, i ^ 2) for i in range(kv_count)]
    half = both_parts.shape[0] // 2
    kept = lax.dynamic_slice_in_dim(both_parts, core_bit * half, half, 0)
    given = lax.dynamic_slice_in_dim(both_parts, (1 - core_bit) * half, half, 0)
    pair_sum = kept.astype(jnp.float32) + lax.ppermute(given, "kv", flip_core).astype(jnp.float32)
    pair_sum = pair_sum.astype(jnp.bfloat16)
    whole = pair_sum.astype(jnp.float32) + lax.ppermute(pair_sum, "kv", flip_chip).astype(jnp.float32)
    hidden_half = (jax.nn.silu(whole[:, :, :, 0]) * whole[:, :, :, 1]).astype(jnp.bfloat16)
    hidden_other = lax.ppermute(hidden_half, "kv", flip_core)
    hidden = jnp.where(
        core_bit == 0,
        jnp.concatenate([hidden_half, hidden_other], axis=0),
        jnp.concatenate([hidden_other, hidden_half], axis=0),
    )
    piece_out = jnp.einsum(
        "spku,pud->spkd", hidden, w_down, preferred_element_type=jnp.float32
    ).astype(jnp.bfloat16)
    if paired:
        half_sum = piece_out.reshape(blk_count, experts_here, 2, capacity, feature_part)
        half_sum = jnp.sum(half_sum.astype(jnp.float32), axis=2).astype(jnp.bfloat16)
        returned = lax.all_to_all(half_sum, "blk", split_axis=0, concat_axis=0, tiled=True)
        per_slot = returned.reshape(slot_total, feature_part).astype(jnp.float32)
    else:
        returned = lax.all_to_all(piece_out, "blk", split_axis=0, concat_axis=0, tiled=True)
        per_piece = returned.reshape(expert_count, 2, capacity, feature_part).astype(jnp.float32)
        per_slot = (per_piece[:, 0] + per_piece[:, 1]).reshape(slot_total, feature_part)
    routed = per_slot[target].reshape(stretch_len, top_count, feature_part)
    moe_out = jnp.sum(routed * gates[:, :, None], axis=1)
    layer_out = (resid_float + moe_out).astype(jnp.bfloat16)
    here_old = in_use & (decode_holder[:, :max_blocks] == own_index)
    from_old = jnp.where(here_old, block_holder, blk_count).reshape(-1)
    put_old = jax.ops.segment_sum(
        (decode_slot[:, :max_blocks] + 1).reshape(-1), from_old, num_segments=blk_count
    )
    here_new = decode_holder[:, max_blocks:] == own_index
    request_ids = jnp.broadcast_to(jnp.arange(decode_holder.shape[0])[:, None], here_new.shape)
    from_new = jnp.where(here_new, request_ids, blk_count).reshape(-1)
    put_new = jax.ops.segment_sum(
        (decode_slot[:, max_blocks:] + 1).reshape(-1), from_new, num_segments=blk_count
    )
    placing = put_old + put_new
    decode_size = pool_size + fresh_count
    placement = (placing[None, :] - 1 == jnp.arange(decode_size)[:, None]).astype(jnp.bfloat16)
    decoded = jnp.dot(
        placement, landed.reshape(blk_count, -1), preferred_element_type=jnp.float32
    ).astype(jnp.bfloat16)
    decode_pool = decoded.reshape(decode_size, block_len, 1, 2, head_dim)
    return (layer_out, decode_pool)


def solution(mesh):
    in_specs = (
        P("blk", "kv"),
        P("blk", "kv"),
        P("blk", "kv", None, None),
        P("blk", None, "kv", None, None),
        P(),
        P(),
        P(),
        P(),
        P(),
        P("kv", "blk"),
        P("kv"),
        P("kv", None),
        P("blk", None),
        P("blk", "kv", None),
        P("blk", "kv", None),
        P("blk", None, "kv"),
    )
    out_specs = (P("blk", "kv"), P("blk", None, "kv", None, None))
    return jax.shard_map(
        per_device, mesh=mesh, in_specs=in_specs, out_specs=out_specs, check_vma=False
    )
```

```python
import math

import jax
import jax.numpy as jnp
from jax import lax
from jax.sharding import PartitionSpec as P

D = 2560
CAP = 8


EPSILON = 1e-05
MASKED = -1e30


def head_rows(asked_rows, head_count, head_dim):
    stretch_len = asked_rows.shape[0]
    return (
        asked_rows.reshape(stretch_len, head_count, head_dim)
        .transpose(1, 0, 2)
        .reshape(head_count * stretch_len, head_dim)
    )


def absorb(carried, scores, value_rows):
    running_max, denominator, accumulated = carried
    new_max = jnp.maximum(running_max, jnp.max(scores, axis=1))
    decay = jnp.exp(running_max - new_max)
    raised = jnp.exp(scores - new_max[:, None])
    denominator = denominator * decay + jnp.sum(raised, axis=1)
    accumulated = accumulated * decay[:, None] + jnp.dot(
        raised.astype(jnp.bfloat16), value_rows, preferred_element_type=jnp.float32
    )
    return (new_max, denominator, accumulated)


def attend_blocks(carried, query_rows, blocks, present, scale):
    block_count = blocks.shape[0]
    block_len = blocks.shape[1]
    head_dim = blocks.shape[3]
    tile_blocks = min(32, block_count)
    span = tile_blocks * block_len
    flags = present.astype(jnp.int32)
    live_count = jnp.sum(flags)
    order_rank = jnp.cumsum(flags) - 1
    positions = jnp.arange(block_count)
    chosen = present[None, :] & (order_rank[None, :] == positions[:, None])
    packing = jnp.sum(jnp.where(chosen, positions[None, :], 0), axis=1)
    packed = blocks[packing]

    def advance(turn, state_now):
        segment = lax.dynamic_slice_in_dim(packed, turn * tile_blocks, tile_blocks, 0)
        key_rows = segment[:, :, 0].reshape(span, head_dim)
        value_rows = segment[:, :, 1].reshape(span, head_dim)
        scores = (
            jnp.einsum("qd,kd->qk", query_rows, key_rows, preferred_element_type=jnp.float32)
            * scale
        )
        is_live = turn * tile_blocks + jnp.arange(span) // block_len < live_count
        scores = jnp.where(is_live[None, :], scores, MASKED)
        return absorb(state_now, scores, value_rows)

    return lax.fori_loop(0, (live_count + tile_blocks - 1) // tile_blocks, advance, carried)


def per_device(
    hidden_in,
    queries,
    new_kv,
    cache_pool,
    cache_len,
    block_holder,
    block_slot,
    decode_holder,
    decode_slot,
    out_weight,
    norm_gain,
    router_weight,
    expert_routes,
    w_gate,
    w_up,
    w_down,
):
    blk_count = lax.axis_size("blk")
    own_index = lax.axis_index("blk")
    stretch_len = queries.shape[0]
    head_dim = new_kv.shape[3]
    head_count = queries.shape[1] // head_dim
    pool_size = cache_pool.shape[0]
    block_len = cache_pool.shape[1]
    max_blocks = block_holder.shape[1]
    fresh_count = stretch_len // block_len
    scale = 1.0 / math.sqrt(head_dim)
    devices = jnp.arange(blk_count)
    in_use = jnp.arange(max_blocks)[None, :] < (cache_len // block_len)[:, None]
    pool_rows = cache_pool[:, :, 0]
    fresh_rows = new_kv[:, 0]
    sources = jnp.concatenate(
        [pool_rows, fresh_rows.reshape(fresh_count, block_len, 2, head_dim)], axis=0
    )
    held_here = in_use & (block_holder == own_index)
    old_target = jnp.where(held_here, decode_holder[:, :max_blocks], blk_count).reshape(-1)
    pick_old = jax.ops.segment_sum((block_slot + 1).reshape(-1), old_target, num_segments=blk_count)
    pick_new = jax.ops.segment_sum(
        pool_size + 1 + jnp.arange(fresh_count),
        decode_holder[own_index, max_blocks:],
        num_segments=blk_count,
    )
    picked = pick_old + pick_new
    sending = jnp.where(
        (picked > 0)[:, None, None, None],
        sources[jnp.maximum(picked - 1, 0)],
        jnp.zeros((), jnp.bfloat16),
    )
    source_request = jnp.zeros_like(devices) + own_index
    match_here = (block_holder[devices] == own_index) & in_use[devices]
    outgoing = pool_rows[jnp.sum(jnp.where(match_here, block_slot[devices], 0), axis=1)]
    both_blocks = lax.all_to_all(
        jnp.stack([sending, outgoing], axis=1), "blk", split_axis=0, concat_axis=0, tiled=True
    )
    landed = both_blocks[:, 0]
    arrived = both_blocks[:, 1]
    present = jnp.any(
        (block_holder[source_request] == devices[:, None]) & in_use[source_request], axis=1
    )
    own_rows = head_rows(queries, head_count, head_dim)
    row_count = head_count * stretch_len
    start_state = (
        jnp.full((row_count,), MASKED, jnp.float32),
        jnp.zeros((row_count,), jnp.float32),
        jnp.zeros((row_count, head_dim), jnp.float32),
    )
    query_pos = jnp.arange(row_count) % stretch_len
    allowed = jnp.arange(stretch_len)[None, :] <= query_pos[:, None]
    local_scores = (
        jnp.einsum("qd,kd->qk", own_rows, fresh_rows[:, 0], preferred_element_type=jnp.float32)
        * scale
    )
    carried = absorb(start_state, jnp.where(allowed, local_scores, MASKED), fresh_rows[:, 1])
    carried = attend_blocks(carried, own_rows, arrived, present, scale)
    running_max, denominator, accumulated = carried
    attended = (
        (accumulated / denominator[:, None])
        .reshape(head_count, stretch_len, head_dim)
        .transpose(1, 0, 2)
    )
    attended = attended.reshape(stretch_len, head_count * head_dim).astype(jnp.bfloat16)
    every_token = lax.all_to_all(
        jnp.broadcast_to(attended[None], (blk_count,) + attended.shape), "blk", 0, 0, tiled=True
    ).reshape(-1, attended.shape[1])
    column_part = jnp.dot(
        every_token, out_weight, preferred_element_type=jnp.float32
    ).astype(jnp.bfloat16)
    projected = lax.all_to_all(column_part, "blk", split_axis=0, concat_axis=1, tiled=True)
    kv_index = lax.axis_index("kv")
    if lax.axis_size("kv") == 4:
        chip_bit = kv_index // 2
        core_low = kv_index % 2
        swap_core = [(i, i ^ 1) for i in range(4)]
        swap_chip = [(i, i ^ 2) for i in range(4)]
        chip_cols = projected.shape[1] // 2
        chip_kept = lax.dynamic_slice_in_dim(projected, chip_bit * chip_cols, chip_cols, 1)
        chip_given = lax.dynamic_slice_in_dim(projected, (1 - chip_bit) * chip_cols, chip_cols, 1)
        chip_sum = chip_kept.astype(jnp.float32) + lax.ppermute(
            chip_given, "kv", swap_chip
        ).astype(jnp.float32)
        own_cols = chip_cols // 2
        core_kept = lax.dynamic_slice_in_dim(chip_sum, core_low * own_cols, own_cols, 1)
        core_given = lax.dynamic_slice_in_dim(
            chip_sum, (1 - core_low) * own_cols, own_cols, 1
        ).astype(jnp.bfloat16)
        head_total = core_kept + lax.ppermute(core_given, "kv", swap_core).astype(jnp.float32)
    else:
        head_total = lax.psum_scatter(
            projected, "kv", scatter_dimension=1, tiled=True
        ).astype(jnp.float32)
    residual = (hidden_in.astype(jnp.float32) + head_total).astype(jnp.bfloat16)
    resid_float = residual.astype(jnp.float32)
    scaled = resid_float * norm_gain.astype(jnp.float32)[None, :]
    stats = jnp.concatenate(
        [
            jnp.sum(resid_float * resid_float, axis=1, keepdims=True),
            jnp.dot(scaled, router_weight, precision=lax.Precision.HIGHEST),
        ],
        axis=1,
    )
    if lax.axis_size("kv") == 4:
        stats = stats + lax.ppermute(stats, "kv", [(i, i ^ 1) for i in range(4)])
        stats = stats + lax.ppermute(stats, "kv", [(i, i ^ 2) for i in range(4)])
    else:
        stats = lax.psum(stats, "kv")
    square_sum = stats[:, 0]
    raw_logits = stats[:, 1:]
    inverse = lax.rsqrt(square_sum / D + EPSILON)
    logits = raw_logits * inverse[:, None]
    normed = (scaled * inverse[:, None]).astype(jnp.bfloat16)
    expert_count = router_weight.shape[1]
    top_count = expert_routes.shape[1]
    chosen_logit = jnp.sum(
        jnp.where(
            expert_routes[:, :, None] == jnp.arange(expert_count)[None, None, :],
            logits[:, None, :],
            0.0,
        ),
        axis=2,
    )
    lifted = jnp.exp(chosen_logit)
    gates = lifted / jnp.sum(lifted, axis=1, keepdims=True)
    capacity = CAP
    flat_routes = expert_routes.reshape(-1)
    assign_count = flat_routes.shape[0]
    onehot = (flat_routes[:, None] == jnp.arange(expert_count)[None, :]).astype(jnp.int32)
    earlier = jnp.cumsum(onehot, axis=0) - onehot
    slot_rank = jnp.sum(earlier * onehot, axis=1)
    target = flat_routes * capacity + slot_rank
    slot_total = expert_count * capacity
    source_item = jax.ops.segment_sum(jnp.arange(assign_count) + 1, target, num_segments=slot_total)
    packed_rows = jnp.where(
        (source_item > 0)[:, None],
        normed[jnp.maximum(source_item - 1, 0) // top_count],
        jnp.zeros((), jnp.bfloat16),
    )
    pieces_here = w_gate.shape[0]
    feature_part = normed.shape[1]
    paired = pieces_here % 2 == 0
    if paired:
        experts_here = pieces_here // 2
        sent = packed_rows.reshape(blk_count, experts_here, capacity, feature_part)
        landed_rows = lax.all_to_all(sent, "blk", split_axis=0, concat_axis=0, tiled=True)
        rows_in = jnp.broadcast_to(
            landed_rows[:, :, None], (blk_count, experts_here, 2, capacity, feature_part)
        ).reshape(blk_count, pieces_here, capacity, feature_part)
    else:
        doubled = jnp.broadcast_to(
            packed_rows.reshape(expert_count, 1, capacity, feature_part),
            (expert_count, 2, capacity, feature_part),
        )
        doubled = doubled.reshape(blk_count, pieces_here, capacity, feature_part)
        rows_in = lax.all_to_all(doubled, "blk", split_axis=0, concat_axis=0, tiled=True)
    gate_part = jnp.einsum("spkd,pdu->spku", rows_in, w_gate, preferred_element_type=jnp.float32)
    up_part = jnp.einsum("spkd,pdu->spku", rows_in, w_up, preferred_element_type=jnp.float32)
    both_parts = jnp.stack([gate_part, up_part], axis=3).astype(jnp.bfloat16)
    kv_count = lax.axis_size("kv")
    core_bit = lax.axis_index("kv") % 2
    flip_core = [(i, i ^ 1) for i in range(kv_count)]
    flip_chip = [(i, i ^ 2) for i in range(kv_count)]
    half = both_parts.shape[0] // 2
    kept = lax.dynamic_slice_in_dim(both_parts, core_bit * half, half, 0)
    given = lax.dynamic_slice_in_dim(both_parts, (1 - core_bit) * half, half, 0)
    pair_sum = kept.astype(jnp.float32) + lax.ppermute(given, "kv", flip_core).astype(jnp.float32)
    pair_sum = pair_sum.astype(jnp.bfloat16)
    whole = pair_sum.astype(jnp.float32) + lax.ppermute(pair_sum, "kv", flip_chip).astype(jnp.float32)
    hidden_half = (jax.nn.silu(whole[:, :, :, 0]) * whole[:, :, :, 1]).astype(jnp.bfloat16)
    hidden_other = lax.ppermute(hidden_half, "kv", flip_core)
    hidden = jnp.where(
        core_bit == 0,
        jnp.concatenate([hidden_half, hidden_other], axis=0),
        jnp.concatenate([hidden_other, hidden_half], axis=0),
    )
    piece_out = jnp.einsum(
        "spku,pud->spkd", hidden, w_down, preferred_element_type=jnp.float32
    ).astype(jnp.bfloat16)
    if paired:
        half_sum = piece_out.reshape(blk_count, experts_here, 2, capacity, feature_part)
        half_sum = jnp.sum(half_sum.astype(jnp.float32), axis=2).astype(jnp.bfloat16)
        returned = lax.all_to_all(half_sum, "blk", split_axis=0, concat_axis=0, tiled=True)
        per_slot = returned.reshape(slot_total, feature_part).astype(jnp.float32)
    else:
        returned = lax.all_to_all(piece_out, "blk", split_axis=0, concat_axis=0, tiled=True)
        per_piece = returned.reshape(expert_count, 2, capacity, feature_part).astype(jnp.float32)
        per_slot = (per_piece[:, 0] + per_piece[:, 1]).reshape(slot_total, feature_part)
    routed = per_slot[target].reshape(stretch_len, top_count, feature_part)
    moe_out = jnp.sum(routed * gates[:, :, None], axis=1)
    layer_out = (resid_float + moe_out).astype(jnp.bfloat16)
    here_old = in_use & (decode_holder[:, :max_blocks] == own_index)
    from_old = jnp.where(here_old, block_holder, blk_count).reshape(-1)
    put_old = jax.ops.segment_sum(
        (decode_slot[:, :max_blocks] + 1).reshape(-1), from_old, num_segments=blk_count
    )
    here_new = decode_holder[:, max_blocks:] == own_index
    request_ids = jnp.broadcast_to(jnp.arange(decode_holder.shape[0])[:, None], here_new.shape)
    from_new = jnp.where(here_new, request_ids, blk_count).reshape(-1)
    put_new = jax.ops.segment_sum(
        (decode_slot[:, max_blocks:] + 1).reshape(-1), from_new, num_segments=blk_count
    )
    placing = put_old + put_new
    decode_size = pool_size + fresh_count
    placement = (placing[None, :] - 1 == jnp.arange(decode_size)[:, None]).astype(jnp.bfloat16)
    decoded = jnp.dot(
        placement, landed.reshape(blk_count, -1), preferred_element_type=jnp.float32
    ).astype(jnp.bfloat16)
    decode_pool = decoded.reshape(decode_size, block_len, 1, 2, head_dim)
    return (layer_out, decode_pool)


def solution(mesh):
    in_specs = (
        P("blk", "kv"),
        P("blk", "kv"),
        P("blk", "kv", None, None),
        P("blk", None, "kv", None, None),
        P(),
        P(),
        P(),
        P(),
        P(),
        P("kv", "blk"),
        P("kv"),
        P("kv", None),
        P("blk", None),
        P("blk", "kv", None),
        P("blk", "kv", None),
        P("blk", None, "kv"),
    )
    out_specs = (P("blk", "kv"), P("blk", None, "kv", None, None))
    return jax.shard_map(
        per_device, mesh=mesh, in_specs=in_specs, out_specs=out_specs, check_vma=False
    )
```

```python
import math

import jax
import jax.numpy as jnp
from jax import lax
from jax.sharding import PartitionSpec as P

D = 2560
CAP = 8
CHUNKS = 2


EPSILON = 1e-05
MASKED = -1e30


def head_rows(asked_rows, head_count, head_dim):
    stretch_len = asked_rows.shape[0]
    return (
        asked_rows.reshape(stretch_len, head_count, head_dim)
        .transpose(1, 0, 2)
        .reshape(head_count * stretch_len, head_dim)
    )


def absorb(carried, scores, value_rows):
    running_max, denominator, accumulated = carried
    new_max = jnp.maximum(running_max, jnp.max(scores, axis=1))
    decay = jnp.exp(running_max - new_max)
    raised = jnp.exp(scores - new_max[:, None])
    denominator = denominator * decay + jnp.sum(raised, axis=1)
    accumulated = accumulated * decay[:, None] + jnp.dot(
        raised.astype(jnp.bfloat16), value_rows, preferred_element_type=jnp.float32
    )
    return (new_max, denominator, accumulated)


def attend_blocks(carried, query_rows, blocks, present, scale):
    block_count = blocks.shape[0]
    block_len = blocks.shape[1]
    head_dim = blocks.shape[3]
    tile_blocks = min(32, block_count)
    span = tile_blocks * block_len
    flags = present.astype(jnp.int32)
    live_count = jnp.sum(flags)
    order_rank = jnp.cumsum(flags) - 1
    positions = jnp.arange(block_count)
    chosen = present[None, :] & (order_rank[None, :] == positions[:, None])
    packing = jnp.sum(jnp.where(chosen, positions[None, :], 0), axis=1)
    packed = blocks[packing]

    def advance(turn, state_now):
        segment = lax.dynamic_slice_in_dim(packed, turn * tile_blocks, tile_blocks, 0)
        key_rows = segment[:, :, 0].reshape(span, head_dim)
        value_rows = segment[:, :, 1].reshape(span, head_dim)
        scores = (
            jnp.einsum("qd,kd->qk", query_rows, key_rows, preferred_element_type=jnp.float32)
            * scale
        )
        is_live = turn * tile_blocks + jnp.arange(span) // block_len < live_count
        scores = jnp.where(is_live[None, :], scores, MASKED)
        return absorb(state_now, scores, value_rows)

    return lax.fori_loop(0, (live_count + tile_blocks - 1) // tile_blocks, advance, carried)


def per_device(
    hidden_in,
    queries,
    new_kv,
    cache_pool,
    cache_len,
    block_holder,
    block_slot,
    decode_holder,
    decode_slot,
    out_weight,
    norm_gain,
    router_weight,
    expert_routes,
    w_gate,
    w_up,
    w_down,
):
    blk_count = lax.axis_size("blk")
    own_index = lax.axis_index("blk")
    stretch_len = queries.shape[0]
    head_dim = new_kv.shape[3]
    head_count = queries.shape[1] // head_dim
    pool_size = cache_pool.shape[0]
    block_len = cache_pool.shape[1]
    max_blocks = block_holder.shape[1]
    fresh_count = stretch_len // block_len
    scale = 1.0 / math.sqrt(head_dim)
    devices = jnp.arange(blk_count)
    in_use = jnp.arange(max_blocks)[None, :] < (cache_len // block_len)[:, None]
    pool_rows = cache_pool[:, :, 0]
    fresh_rows = new_kv[:, 0]
    sources = jnp.concatenate(
        [pool_rows, fresh_rows.reshape(fresh_count, block_len, 2, head_dim)], axis=0
    )
    held_here = in_use & (block_holder == own_index)
    old_target = jnp.where(held_here, decode_holder[:, :max_blocks], blk_count).reshape(-1)
    pick_old = jax.ops.segment_sum((block_slot + 1).reshape(-1), old_target, num_segments=blk_count)
    pick_new = jax.ops.segment_sum(
        pool_size + 1 + jnp.arange(fresh_count),
        decode_holder[own_index, max_blocks:],
        num_segments=blk_count,
    )
    picked = pick_old + pick_new
    sending = jnp.where(
        (picked > 0)[:, None, None, None],
        sources[jnp.maximum(picked - 1, 0)],
        jnp.zeros((), jnp.bfloat16),
    )
    source_request = jnp.zeros_like(devices) + own_index
    match_here = (block_holder[devices] == own_index) & in_use[devices]
    outgoing = pool_rows[jnp.sum(jnp.where(match_here, block_slot[devices], 0), axis=1)]
    both_blocks = lax.all_to_all(
        jnp.stack([sending, outgoing], axis=1), "blk", split_axis=0, concat_axis=0, tiled=True
    )
    landed = both_blocks[:, 0]
    arrived = both_blocks[:, 1]
    present = jnp.any(
        (block_holder[source_request] == devices[:, None]) & in_use[source_request], axis=1
    )
    own_rows = head_rows(queries, head_count, head_dim)
    row_count = head_count * stretch_len
    start_state = (
        jnp.full((row_count,), MASKED, jnp.float32),
        jnp.zeros((row_count,), jnp.float32),
        jnp.zeros((row_count, head_dim), jnp.float32),
    )
    query_pos = jnp.arange(row_count) % stretch_len
    allowed = jnp.arange(stretch_len)[None, :] <= query_pos[:, None]
    local_scores = (
        jnp.einsum("qd,kd->qk", own_rows, fresh_rows[:, 0], preferred_element_type=jnp.float32)
        * scale
    )
    carried = absorb(start_state, jnp.where(allowed, local_scores, MASKED), fresh_rows[:, 1])
    carried = attend_blocks(carried, own_rows, arrived, present, scale)
    running_max, denominator, accumulated = carried
    attended = (
        (accumulated / denominator[:, None])
        .reshape(head_count, stretch_len, head_dim)
        .transpose(1, 0, 2)
    )
    attended = attended.reshape(stretch_len, head_count * head_dim).astype(jnp.bfloat16)
    every_token = lax.all_to_all(
        jnp.broadcast_to(attended[None], (blk_count,) + attended.shape), "blk", 0, 0, tiled=True
    ).reshape(-1, attended.shape[1])
    column_part = jnp.dot(
        every_token, out_weight, preferred_element_type=jnp.float32
    ).astype(jnp.bfloat16)
    projected = lax.all_to_all(column_part, "blk", split_axis=0, concat_axis=1, tiled=True)
    kv_index = lax.axis_index("kv")
    if lax.axis_size("kv") == 4:
        chip_bit = kv_index // 2
        core_low = kv_index % 2
        swap_core = [(i, i ^ 1) for i in range(4)]
        swap_chip = [(i, i ^ 2) for i in range(4)]
        chip_cols = projected.shape[1] // 2
        chip_kept = lax.dynamic_slice_in_dim(projected, chip_bit * chip_cols, chip_cols, 1)
        chip_given = lax.dynamic_slice_in_dim(projected, (1 - chip_bit) * chip_cols, chip_cols, 1)
        chip_sum = chip_kept.astype(jnp.float32) + lax.ppermute(
            chip_given, "kv", swap_chip
        ).astype(jnp.float32)
        own_cols = chip_cols // 2
        core_kept = lax.dynamic_slice_in_dim(chip_sum, core_low * own_cols, own_cols, 1)
        core_given = lax.dynamic_slice_in_dim(
            chip_sum, (1 - core_low) * own_cols, own_cols, 1
        ).astype(jnp.bfloat16)
        head_total = core_kept + lax.ppermute(core_given, "kv", swap_core).astype(jnp.float32)
    else:
        head_total = lax.psum_scatter(
            projected, "kv", scatter_dimension=1, tiled=True
        ).astype(jnp.float32)
    residual = (hidden_in.astype(jnp.float32) + head_total).astype(jnp.bfloat16)
    resid_float = residual.astype(jnp.float32)
    scaled = resid_float * norm_gain.astype(jnp.float32)[None, :]
    stats = jnp.concatenate(
        [
            jnp.sum(resid_float * resid_float, axis=1, keepdims=True),
            jnp.dot(scaled, router_weight, precision=lax.Precision.HIGHEST),
        ],
        axis=1,
    )
    if lax.axis_size("kv") == 4:
        stats = stats + lax.ppermute(stats, "kv", [(i, i ^ 1) for i in range(4)])
        stats = stats + lax.ppermute(stats, "kv", [(i, i ^ 2) for i in range(4)])
    else:
        stats = lax.psum(stats, "kv")
    square_sum = stats[:, 0]
    raw_logits = stats[:, 1:]
    inverse = lax.rsqrt(square_sum / D + EPSILON)
    logits = raw_logits * inverse[:, None]
    normed = (scaled * inverse[:, None]).astype(jnp.bfloat16)
    expert_count = router_weight.shape[1]
    top_count = expert_routes.shape[1]
    chosen_logit = jnp.sum(
        jnp.where(
            expert_routes[:, :, None] == jnp.arange(expert_count)[None, None, :],
            logits[:, None, :],
            0.0,
        ),
        axis=2,
    )
    lifted = jnp.exp(chosen_logit)
    gates = lifted / jnp.sum(lifted, axis=1, keepdims=True)
    capacity = CAP
    flat_routes = expert_routes.reshape(-1)
    assign_count = flat_routes.shape[0]
    onehot = (flat_routes[:, None] == jnp.arange(expert_count)[None, :]).astype(jnp.int32)
    earlier = jnp.cumsum(onehot, axis=0) - onehot
    slot_rank = jnp.sum(earlier * onehot, axis=1)
    target = flat_routes * capacity + slot_rank
    slot_total = expert_count * capacity
    source_item = jax.ops.segment_sum(jnp.arange(assign_count) + 1, target, num_segments=slot_total)
    packed_rows = jnp.where(
        (source_item > 0)[:, None],
        normed[jnp.maximum(source_item - 1, 0) // top_count],
        jnp.zeros((), jnp.bfloat16),
    )
    pieces_here = w_gate.shape[0]
    feature_part = normed.shape[1]
    paired = pieces_here % 2 == 0
    kv_count = lax.axis_size("kv")
    core_bit = lax.axis_index("kv") % 2
    flip_core = [(i, i ^ 1) for i in range(kv_count)]
    flip_chip = [(i, i ^ 2) for i in range(kv_count)]
    if paired:
        experts_here = pieces_here // 2
        outgoing_rows = packed_rows.reshape(blk_count, experts_here, capacity, feature_part)
    else:
        outgoing_rows = jnp.broadcast_to(
            packed_rows.reshape(expert_count, 1, capacity, feature_part),
            (expert_count, 2, capacity, feature_part),
        ).reshape(blk_count, pieces_here, capacity, feature_part)

    def expert_chunk(chunk_rows):
        chunk_len = chunk_rows.shape[2]
        landed_rows = lax.all_to_all(chunk_rows, "blk", split_axis=0, concat_axis=0, tiled=True)
        if paired:
            rows_in = jnp.broadcast_to(
                landed_rows[:, :, None], (blk_count, experts_here, 2, chunk_len, feature_part)
            ).reshape(blk_count, pieces_here, chunk_len, feature_part)
        else:
            rows_in = landed_rows
        gate_part = jnp.einsum("spkd,pdu->spku", rows_in, w_gate, preferred_element_type=jnp.float32)
        up_part = jnp.einsum("spkd,pdu->spku", rows_in, w_up, preferred_element_type=jnp.float32)
        both_parts = jnp.stack([gate_part, up_part], axis=3).astype(jnp.bfloat16)
        half = both_parts.shape[0] // 2
        kept = lax.dynamic_slice_in_dim(both_parts, core_bit * half, half, 0)
        given = lax.dynamic_slice_in_dim(both_parts, (1 - core_bit) * half, half, 0)
        pair_sum = kept.astype(jnp.float32) + lax.ppermute(given, "kv", flip_core).astype(jnp.float32)
        pair_sum = pair_sum.astype(jnp.bfloat16)
        whole = pair_sum.astype(jnp.float32) + lax.ppermute(pair_sum, "kv", flip_chip).astype(jnp.float32)
        hidden_half = (jax.nn.silu(whole[:, :, :, 0]) * whole[:, :, :, 1]).astype(jnp.bfloat16)
        hidden_other = lax.ppermute(hidden_half, "kv", flip_core)
        hidden = jnp.where(
            core_bit == 0,
            jnp.concatenate([hidden_half, hidden_other], axis=0),
            jnp.concatenate([hidden_other, hidden_half], axis=0),
        )
        piece_out = jnp.einsum(
            "spku,pud->spkd", hidden, w_down, preferred_element_type=jnp.float32
        ).astype(jnp.bfloat16)
        if paired:
            half_sum = piece_out.reshape(blk_count, experts_here, 2, chunk_len, feature_part)
            half_sum = jnp.sum(half_sum.astype(jnp.float32), axis=2).astype(jnp.bfloat16)
            returned = lax.all_to_all(half_sum, "blk", split_axis=0, concat_axis=0, tiled=True)
            return returned.reshape(expert_count, chunk_len, feature_part).astype(jnp.float32)
        returned = lax.all_to_all(piece_out, "blk", split_axis=0, concat_axis=0, tiled=True)
        per_piece = returned.reshape(expert_count, 2, chunk_len, feature_part).astype(jnp.float32)
        return per_piece[:, 0] + per_piece[:, 1]

    chunk_count = CHUNKS if capacity % CHUNKS == 0 else 1
    chunk_len = capacity // chunk_count
    per_chunk = [
        expert_chunk(outgoing_rows[:, :, i * chunk_len : (i + 1) * chunk_len])
        for i in range(chunk_count)
    ]
    per_slot = jnp.concatenate(per_chunk, axis=1).reshape(slot_total, feature_part)
    routed = per_slot[target].reshape(stretch_len, top_count, feature_part)
    moe_out = jnp.sum(routed * gates[:, :, None], axis=1)
    layer_out = (resid_float + moe_out).astype(jnp.bfloat16)
    here_old = in_use & (decode_holder[:, :max_blocks] == own_index)
    from_old = jnp.where(here_old, block_holder, blk_count).reshape(-1)
    put_old = jax.ops.segment_sum(
        (decode_slot[:, :max_blocks] + 1).reshape(-1), from_old, num_segments=blk_count
    )
    here_new = decode_holder[:, max_blocks:] == own_index
    request_ids = jnp.broadcast_to(jnp.arange(decode_holder.shape[0])[:, None], here_new.shape)
    from_new = jnp.where(here_new, request_ids, blk_count).reshape(-1)
    put_new = jax.ops.segment_sum(
        (decode_slot[:, max_blocks:] + 1).reshape(-1), from_new, num_segments=blk_count
    )
    placing = put_old + put_new
    decode_size = pool_size + fresh_count
    placement = (placing[None, :] - 1 == jnp.arange(decode_size)[:, None]).astype(jnp.bfloat16)
    decoded = jnp.dot(
        placement, landed.reshape(blk_count, -1), preferred_element_type=jnp.float32
    ).astype(jnp.bfloat16)
    decode_pool = decoded.reshape(decode_size, block_len, 1, 2, head_dim)
    return (layer_out, decode_pool)


def solution(mesh):
    in_specs = (
        P("blk", "kv"),
        P("blk", "kv"),
        P("blk", "kv", None, None),
        P("blk", None, "kv", None, None),
        P(),
        P(),
        P(),
        P(),
        P(),
        P("kv", "blk"),
        P("kv"),
        P("kv", None),
        P("blk", None),
        P("blk", "kv", None),
        P("blk", "kv", None),
        P("blk", None, "kv"),
    )
    out_specs = (P("blk", "kv"), P("blk", None, "kv", None, None))
    return jax.shard_map(
        per_device, mesh=mesh, in_specs=in_specs, out_specs=out_specs, check_vma=False
    )
```

```python
import math

import jax
import jax.numpy as jnp
from jax import lax
from jax.sharding import PartitionSpec as P

D = 2560
CAP = 8
CHUNKS = 2


EPSILON = 1e-05
MASKED = -1e30


def head_rows(asked_rows, head_count, head_dim):
    stretch_len = asked_rows.shape[0]
    return (
        asked_rows.reshape(stretch_len, head_count, head_dim)
        .transpose(1, 0, 2)
        .reshape(head_count * stretch_len, head_dim)
    )


def absorb(carried, scores, value_rows):
    running_max, denominator, accumulated = carried
    new_max = jnp.maximum(running_max, jnp.max(scores, axis=1))
    decay = jnp.exp(running_max - new_max)
    raised = jnp.exp(scores - new_max[:, None])
    denominator = denominator * decay + jnp.sum(raised, axis=1)
    accumulated = accumulated * decay[:, None] + jnp.dot(
        raised.astype(jnp.bfloat16), value_rows, preferred_element_type=jnp.float32
    )
    return (new_max, denominator, accumulated)


def attend_blocks(carried, query_rows, blocks, present, scale):
    block_count = blocks.shape[0]
    block_len = blocks.shape[1]
    head_dim = blocks.shape[3]
    tile_blocks = min(32, block_count)
    span = tile_blocks * block_len
    flags = present.astype(jnp.int32)
    live_count = jnp.sum(flags)
    order_rank = jnp.cumsum(flags) - 1
    positions = jnp.arange(block_count)
    chosen = present[None, :] & (order_rank[None, :] == positions[:, None])
    packing = jnp.sum(jnp.where(chosen, positions[None, :], 0), axis=1)
    packed = blocks[packing]

    def advance(turn, state_now):
        segment = lax.dynamic_slice_in_dim(packed, turn * tile_blocks, tile_blocks, 0)
        key_rows = segment[:, :, 0].reshape(span, head_dim)
        value_rows = segment[:, :, 1].reshape(span, head_dim)
        scores = (
            jnp.einsum("qd,kd->qk", query_rows, key_rows, preferred_element_type=jnp.float32)
            * scale
        )
        is_live = turn * tile_blocks + jnp.arange(span) // block_len < live_count
        scores = jnp.where(is_live[None, :], scores, MASKED)
        return absorb(state_now, scores, value_rows)

    return lax.fori_loop(0, (live_count + tile_blocks - 1) // tile_blocks, advance, carried)


def per_device(
    hidden_in,
    queries,
    new_kv,
    cache_pool,
    cache_len,
    block_holder,
    block_slot,
    decode_holder,
    decode_slot,
    out_weight,
    norm_gain,
    router_weight,
    expert_routes,
    w_gate,
    w_up,
    w_down,
):
    blk_count = lax.axis_size("blk")
    own_index = lax.axis_index("blk")
    stretch_len = queries.shape[0]
    head_dim = new_kv.shape[3]
    head_count = queries.shape[1] // head_dim
    pool_size = cache_pool.shape[0]
    block_len = cache_pool.shape[1]
    max_blocks = block_holder.shape[1]
    fresh_count = stretch_len // block_len
    scale = 1.0 / math.sqrt(head_dim)
    devices = jnp.arange(blk_count)
    in_use = jnp.arange(max_blocks)[None, :] < (cache_len // block_len)[:, None]
    pool_rows = cache_pool[:, :, 0]
    fresh_rows = new_kv[:, 0]
    sources = jnp.concatenate(
        [pool_rows, fresh_rows.reshape(fresh_count, block_len, 2, head_dim)], axis=0
    )
    held_here = in_use & (block_holder == own_index)
    old_target = jnp.where(held_here, decode_holder[:, :max_blocks], blk_count).reshape(-1)
    pick_old = jax.ops.segment_sum((block_slot + 1).reshape(-1), old_target, num_segments=blk_count)
    pick_new = jax.ops.segment_sum(
        pool_size + 1 + jnp.arange(fresh_count),
        decode_holder[own_index, max_blocks:],
        num_segments=blk_count,
    )
    picked = pick_old + pick_new
    sending = jnp.where(
        (picked > 0)[:, None, None, None],
        sources[jnp.maximum(picked - 1, 0)],
        jnp.zeros((), jnp.bfloat16),
    )
    source_request = jnp.zeros_like(devices) + own_index
    match_here = (block_holder[devices] == own_index) & in_use[devices]
    outgoing = pool_rows[jnp.sum(jnp.where(match_here, block_slot[devices], 0), axis=1)]
    both_blocks = lax.all_to_all(
        jnp.stack([sending, outgoing], axis=1), "blk", split_axis=0, concat_axis=0, tiled=True
    )
    landed = both_blocks[:, 0]
    arrived = both_blocks[:, 1]
    present = jnp.any(
        (block_holder[source_request] == devices[:, None]) & in_use[source_request], axis=1
    )
    own_rows = head_rows(queries, head_count, head_dim)
    row_count = head_count * stretch_len
    start_state = (
        jnp.full((row_count,), MASKED, jnp.float32),
        jnp.zeros((row_count,), jnp.float32),
        jnp.zeros((row_count, head_dim), jnp.float32),
    )
    query_pos = jnp.arange(row_count) % stretch_len
    allowed = jnp.arange(stretch_len)[None, :] <= query_pos[:, None]
    local_scores = (
        jnp.einsum("qd,kd->qk", own_rows, fresh_rows[:, 0], preferred_element_type=jnp.float32)
        * scale
    )
    carried = absorb(start_state, jnp.where(allowed, local_scores, MASKED), fresh_rows[:, 1])
    carried = attend_blocks(carried, own_rows, arrived, present, scale)
    running_max, denominator, accumulated = carried
    attended = (
        (accumulated / denominator[:, None])
        .reshape(head_count, stretch_len, head_dim)
        .transpose(1, 0, 2)
    )
    attended = attended.reshape(stretch_len, head_count * head_dim).astype(jnp.bfloat16)
    every_token = lax.all_to_all(
        jnp.broadcast_to(attended[None], (blk_count,) + attended.shape), "blk", 0, 0, tiled=True
    ).reshape(-1, attended.shape[1])
    column_part = jnp.dot(
        every_token, out_weight, preferred_element_type=jnp.float32
    ).astype(jnp.bfloat16)
    projected = lax.all_to_all(column_part, "blk", split_axis=0, concat_axis=1, tiled=True)
    kv_index = lax.axis_index("kv")
    if lax.axis_size("kv") == 4:
        chip_bit = kv_index // 2
        core_low = kv_index % 2
        swap_core = [(i, i ^ 1) for i in range(4)]
        swap_chip = [(i, i ^ 2) for i in range(4)]
        chip_cols = projected.shape[1] // 2
        chip_kept = lax.dynamic_slice_in_dim(projected, chip_bit * chip_cols, chip_cols, 1)
        chip_given = lax.dynamic_slice_in_dim(projected, (1 - chip_bit) * chip_cols, chip_cols, 1)
        chip_sum = chip_kept.astype(jnp.float32) + lax.ppermute(
            chip_given, "kv", swap_chip
        ).astype(jnp.float32)
        own_cols = chip_cols // 2
        core_kept = lax.dynamic_slice_in_dim(chip_sum, core_low * own_cols, own_cols, 1)
        core_given = lax.dynamic_slice_in_dim(
            chip_sum, (1 - core_low) * own_cols, own_cols, 1
        ).astype(jnp.bfloat16)
        head_total = core_kept + lax.ppermute(core_given, "kv", swap_core).astype(jnp.float32)
    else:
        head_total = lax.psum_scatter(
            projected, "kv", scatter_dimension=1, tiled=True
        ).astype(jnp.float32)
    residual = (hidden_in.astype(jnp.float32) + head_total).astype(jnp.bfloat16)
    resid_float = residual.astype(jnp.float32)
    scaled = resid_float * norm_gain.astype(jnp.float32)[None, :]
    stats = jnp.concatenate(
        [
            jnp.sum(resid_float * resid_float, axis=1, keepdims=True),
            jnp.dot(scaled, router_weight, precision=lax.Precision.HIGHEST),
        ],
        axis=1,
    )
    if lax.axis_size("kv") == 4:
        stats = stats + lax.ppermute(stats, "kv", [(i, i ^ 1) for i in range(4)])
        stats = stats + lax.ppermute(stats, "kv", [(i, i ^ 2) for i in range(4)])
    else:
        stats = lax.psum(stats, "kv")
    square_sum = stats[:, 0]
    raw_logits = stats[:, 1:]
    inverse = lax.rsqrt(square_sum / D + EPSILON)
    logits = raw_logits * inverse[:, None]
    normed = (scaled * inverse[:, None]).astype(jnp.bfloat16)
    expert_count = router_weight.shape[1]
    top_count = expert_routes.shape[1]
    chosen_logit = jnp.sum(
        jnp.where(
            expert_routes[:, :, None] == jnp.arange(expert_count)[None, None, :],
            logits[:, None, :],
            0.0,
        ),
        axis=2,
    )
    lifted = jnp.exp(chosen_logit)
    gates = lifted / jnp.sum(lifted, axis=1, keepdims=True)
    capacity = CAP
    flat_routes = expert_routes.reshape(-1)
    assign_count = flat_routes.shape[0]
    onehot = (flat_routes[:, None] == jnp.arange(expert_count)[None, :]).astype(jnp.int32)
    earlier = jnp.cumsum(onehot, axis=0) - onehot
    slot_rank = jnp.sum(earlier * onehot, axis=1)
    target = flat_routes * capacity + slot_rank
    slot_total = expert_count * capacity
    source_item = jax.ops.segment_sum(jnp.arange(assign_count) + 1, target, num_segments=slot_total)
    packed_rows = jnp.where(
        (source_item > 0)[:, None],
        normed[jnp.maximum(source_item - 1, 0) // top_count],
        jnp.zeros((), jnp.bfloat16),
    )
    pieces_here = w_gate.shape[0]
    feature_part = normed.shape[1]
    paired = pieces_here % 2 == 0
    kv_count = lax.axis_size("kv")
    core_bit = lax.axis_index("kv") % 2
    flip_core = [(i, i ^ 1) for i in range(kv_count)]
    flip_chip = [(i, i ^ 2) for i in range(kv_count)]
    if paired:
        experts_here = pieces_here // 2
        outgoing_rows = packed_rows.reshape(blk_count, experts_here, capacity, feature_part)
    else:
        experts_here = 1
        outgoing_rows = jnp.broadcast_to(
            packed_rows.reshape(expert_count, 1, capacity, feature_part),
            (expert_count, 2, capacity, feature_part),
        ).reshape(blk_count, pieces_here, capacity, feature_part)

    def expert_chunk(chunk_rows, gate_w, up_w, down_w):
        chunk_pieces = gate_w.shape[0]
        landed_rows = lax.all_to_all(chunk_rows, "blk", split_axis=0, concat_axis=0, tiled=True)
        if paired:
            rows_in = jnp.broadcast_to(
                landed_rows[:, :, None],
                (blk_count, chunk_pieces // 2, 2, capacity, feature_part),
            ).reshape(blk_count, chunk_pieces, capacity, feature_part)
        else:
            rows_in = landed_rows
        gate_part = jnp.einsum("spkd,pdu->spku", rows_in, gate_w, preferred_element_type=jnp.float32)
        up_part = jnp.einsum("spkd,pdu->spku", rows_in, up_w, preferred_element_type=jnp.float32)
        both_parts = jnp.stack([gate_part, up_part], axis=3).astype(jnp.bfloat16)
        half = both_parts.shape[0] // 2
        kept = lax.dynamic_slice_in_dim(both_parts, core_bit * half, half, 0)
        given = lax.dynamic_slice_in_dim(both_parts, (1 - core_bit) * half, half, 0)
        pair_sum = kept.astype(jnp.float32) + lax.ppermute(given, "kv", flip_core).astype(jnp.float32)
        pair_sum = pair_sum.astype(jnp.bfloat16)
        whole = pair_sum.astype(jnp.float32) + lax.ppermute(pair_sum, "kv", flip_chip).astype(jnp.float32)
        hidden_half = (jax.nn.silu(whole[:, :, :, 0]) * whole[:, :, :, 1]).astype(jnp.bfloat16)
        hidden_other = lax.ppermute(hidden_half, "kv", flip_core)
        hidden = jnp.where(
            core_bit == 0,
            jnp.concatenate([hidden_half, hidden_other], axis=0),
            jnp.concatenate([hidden_other, hidden_half], axis=0),
        )
        piece_out = jnp.einsum(
            "spku,pud->spkd", hidden, down_w, preferred_element_type=jnp.float32
        ).astype(jnp.bfloat16)
        if paired:
            half_sum = piece_out.reshape(blk_count, chunk_pieces // 2, 2, capacity, feature_part)
            half_sum = jnp.sum(half_sum.astype(jnp.float32), axis=2).astype(jnp.bfloat16)
            return lax.all_to_all(half_sum, "blk", split_axis=0, concat_axis=0, tiled=True)
        returned = lax.all_to_all(piece_out, "blk", split_axis=0, concat_axis=0, tiled=True)
        per_piece = returned.reshape(expert_count, 2, capacity, feature_part).astype(jnp.float32)
        return (per_piece[:, 0] + per_piece[:, 1]).astype(jnp.bfloat16)

    chunk_count = CHUNKS if paired and experts_here % CHUNKS == 0 else 1
    chunk_experts = experts_here // chunk_count
    chunk_pieces = pieces_here // chunk_count
    per_chunk = []
    for i in range(chunk_count):
        pieces_of = slice(i * chunk_pieces, (i + 1) * chunk_pieces)
        per_chunk.append(
            expert_chunk(
                outgoing_rows[:, i * chunk_experts : (i + 1) * chunk_experts],
                w_gate[pieces_of],
                w_up[pieces_of],
                w_down[pieces_of],
            )
        )
    if paired:
        per_slot = jnp.concatenate(per_chunk, axis=1).reshape(slot_total, feature_part)
    else:
        per_slot = per_chunk[0].reshape(slot_total, feature_part)
    per_slot = per_slot.astype(jnp.float32)
    routed = per_slot[target].reshape(stretch_len, top_count, feature_part)
    moe_out = jnp.sum(routed * gates[:, :, None], axis=1)
    layer_out = (resid_float + moe_out).astype(jnp.bfloat16)
    here_old = in_use & (decode_holder[:, :max_blocks] == own_index)
    from_old = jnp.where(here_old, block_holder, blk_count).reshape(-1)
    put_old = jax.ops.segment_sum(
        (decode_slot[:, :max_blocks] + 1).reshape(-1), from_old, num_segments=blk_count
    )
    here_new = decode_holder[:, max_blocks:] == own_index
    request_ids = jnp.broadcast_to(jnp.arange(decode_holder.shape[0])[:, None], here_new.shape)
    from_new = jnp.where(here_new, request_ids, blk_count).reshape(-1)
    put_new = jax.ops.segment_sum(
        (decode_slot[:, max_blocks:] + 1).reshape(-1), from_new, num_segments=blk_count
    )
    placing = put_old + put_new
    decode_size = pool_size + fresh_count
    placement = (placing[None, :] - 1 == jnp.arange(decode_size)[:, None]).astype(jnp.bfloat16)
    decoded = jnp.dot(
        placement, landed.reshape(blk_count, -1), preferred_element_type=jnp.float32
    ).astype(jnp.bfloat16)
    decode_pool = decoded.reshape(decode_size, block_len, 1, 2, head_dim)
    return (layer_out, decode_pool)


def solution(mesh):
    in_specs = (
        P("blk", "kv"),
        P("blk", "kv"),
        P("blk", "kv", None, None),
        P("blk", None, "kv", None, None),
        P(),
        P(),
        P(),
        P(),
        P(),
        P("kv", "blk"),
        P("kv"),
        P("kv", None),
        P("blk", None),
        P("blk", "kv", None),
        P("blk", "kv", None),
        P("blk", None, "kv"),
    )
    out_specs = (P("blk", "kv"), P("blk", None, "kv", None, None))
    return jax.shard_map(
        per_device, mesh=mesh, in_specs=in_specs, out_specs=out_specs, check_vma=False
    )
```

```python
import math

import jax
import jax.numpy as jnp
from jax import lax
from jax.sharding import PartitionSpec as P

D = 2560
CAP = 8
CHUNKS = 1


EPSILON = 1e-05
MASKED = -1e30


def head_rows(asked_rows, head_count, head_dim):
    stretch_len = asked_rows.shape[0]
    return (
        asked_rows.reshape(stretch_len, head_count, head_dim)
        .transpose(1, 0, 2)
        .reshape(head_count * stretch_len, head_dim)
    )


def absorb(carried, scores, value_rows):
    running_max, denominator, accumulated = carried
    new_max = jnp.maximum(running_max, jnp.max(scores, axis=1))
    decay = jnp.exp(running_max - new_max)
    raised = jnp.exp(scores - new_max[:, None])
    denominator = denominator * decay + jnp.sum(raised, axis=1)
    accumulated = accumulated * decay[:, None] + jnp.dot(
        raised.astype(jnp.bfloat16), value_rows, preferred_element_type=jnp.float32
    )
    return (new_max, denominator, accumulated)


def attend_blocks(carried, query_rows, blocks, present, scale):
    block_count = blocks.shape[0]
    block_len = blocks.shape[1]
    head_dim = blocks.shape[3]
    tile_blocks = min(32, block_count)
    span = tile_blocks * block_len
    flags = present.astype(jnp.int32)
    live_count = jnp.sum(flags)
    order_rank = jnp.cumsum(flags) - 1
    positions = jnp.arange(block_count)
    chosen = present[None, :] & (order_rank[None, :] == positions[:, None])
    packing = jnp.sum(jnp.where(chosen, positions[None, :], 0), axis=1)
    packed = blocks[packing]

    def advance(turn, state_now):
        segment = lax.dynamic_slice_in_dim(packed, turn * tile_blocks, tile_blocks, 0)
        key_rows = segment[:, :, 0].reshape(span, head_dim)
        value_rows = segment[:, :, 1].reshape(span, head_dim)
        scores = (
            jnp.einsum("qd,kd->qk", query_rows, key_rows, preferred_element_type=jnp.float32)
            * scale
        )
        is_live = turn * tile_blocks + jnp.arange(span) // block_len < live_count
        scores = jnp.where(is_live[None, :], scores, MASKED)
        return absorb(state_now, scores, value_rows)

    return lax.fori_loop(0, (live_count + tile_blocks - 1) // tile_blocks, advance, carried)


def per_device(
    hidden_in,
    queries,
    new_kv,
    cache_pool,
    cache_len,
    block_holder,
    block_slot,
    decode_holder,
    decode_slot,
    out_weight,
    norm_gain,
    router_weight,
    expert_routes,
    w_gate,
    w_up,
    w_down,
):
    blk_count = lax.axis_size("blk")
    own_index = lax.axis_index("blk")
    stretch_len = queries.shape[0]
    head_dim = new_kv.shape[3]
    head_count = queries.shape[1] // head_dim
    pool_size = cache_pool.shape[0]
    block_len = cache_pool.shape[1]
    max_blocks = block_holder.shape[1]
    fresh_count = stretch_len // block_len
    scale = 1.0 / math.sqrt(head_dim)
    devices = jnp.arange(blk_count)
    in_use = jnp.arange(max_blocks)[None, :] < (cache_len // block_len)[:, None]
    pool_rows = cache_pool[:, :, 0]
    fresh_rows = new_kv[:, 0]
    sources = jnp.concatenate(
        [pool_rows, fresh_rows.reshape(fresh_count, block_len, 2, head_dim)], axis=0
    )
    held_here = in_use & (block_holder == own_index)
    old_target = jnp.where(held_here, decode_holder[:, :max_blocks], blk_count).reshape(-1)
    pick_old = jax.ops.segment_sum((block_slot + 1).reshape(-1), old_target, num_segments=blk_count)
    pick_new = jax.ops.segment_sum(
        pool_size + 1 + jnp.arange(fresh_count),
        decode_holder[own_index, max_blocks:],
        num_segments=blk_count,
    )
    picked = pick_old + pick_new
    sending = jnp.where(
        (picked > 0)[:, None, None, None],
        sources[jnp.maximum(picked - 1, 0)],
        jnp.zeros((), jnp.bfloat16),
    )
    source_request = jnp.zeros_like(devices) + own_index
    match_here = (block_holder[devices] == own_index) & in_use[devices]
    outgoing = pool_rows[jnp.sum(jnp.where(match_here, block_slot[devices], 0), axis=1)]
    both_blocks = lax.all_to_all(
        jnp.stack([sending, outgoing], axis=1), "blk", split_axis=0, concat_axis=0, tiled=True
    )
    landed = both_blocks[:, 0]
    arrived = both_blocks[:, 1]
    present = jnp.any(
        (block_holder[source_request] == devices[:, None]) & in_use[source_request], axis=1
    )
    own_rows = head_rows(queries, head_count, head_dim)
    row_count = head_count * stretch_len
    start_state = (
        jnp.full((row_count,), MASKED, jnp.float32),
        jnp.zeros((row_count,), jnp.float32),
        jnp.zeros((row_count, head_dim), jnp.float32),
    )
    query_pos = jnp.arange(row_count) % stretch_len
    allowed = jnp.arange(stretch_len)[None, :] <= query_pos[:, None]
    local_scores = (
        jnp.einsum("qd,kd->qk", own_rows, fresh_rows[:, 0], preferred_element_type=jnp.float32)
        * scale
    )
    carried = absorb(start_state, jnp.where(allowed, local_scores, MASKED), fresh_rows[:, 1])
    carried = attend_blocks(carried, own_rows, arrived, present, scale)
    running_max, denominator, accumulated = carried
    attended = (
        (accumulated / denominator[:, None])
        .reshape(head_count, stretch_len, head_dim)
        .transpose(1, 0, 2)
    )
    attended = attended.reshape(stretch_len, head_count * head_dim).astype(jnp.bfloat16)
    every_token = lax.all_to_all(
        jnp.broadcast_to(attended[None], (blk_count,) + attended.shape), "blk", 0, 0, tiled=True
    ).reshape(-1, attended.shape[1])
    column_part = jnp.dot(
        every_token, out_weight, preferred_element_type=jnp.float32
    ).astype(jnp.bfloat16)
    projected = lax.all_to_all(column_part, "blk", split_axis=0, concat_axis=1, tiled=True)
    kv_index = lax.axis_index("kv")
    if lax.axis_size("kv") == 4:
        chip_bit = kv_index // 2
        core_low = kv_index % 2
        swap_core = [(i, i ^ 1) for i in range(4)]
        swap_chip = [(i, i ^ 2) for i in range(4)]
        chip_cols = projected.shape[1] // 2
        chip_kept = lax.dynamic_slice_in_dim(projected, chip_bit * chip_cols, chip_cols, 1)
        chip_given = lax.dynamic_slice_in_dim(projected, (1 - chip_bit) * chip_cols, chip_cols, 1)
        chip_sum = chip_kept.astype(jnp.float32) + lax.ppermute(
            chip_given, "kv", swap_chip
        ).astype(jnp.float32)
        own_cols = chip_cols // 2
        core_kept = lax.dynamic_slice_in_dim(chip_sum, core_low * own_cols, own_cols, 1)
        core_given = lax.dynamic_slice_in_dim(
            chip_sum, (1 - core_low) * own_cols, own_cols, 1
        ).astype(jnp.bfloat16)
        head_total = core_kept + lax.ppermute(core_given, "kv", swap_core).astype(jnp.float32)
    else:
        head_total = lax.psum_scatter(
            projected, "kv", scatter_dimension=1, tiled=True
        ).astype(jnp.float32)
    residual = (hidden_in.astype(jnp.float32) + head_total).astype(jnp.bfloat16)
    resid_float = residual.astype(jnp.float32)
    scaled = resid_float * norm_gain.astype(jnp.float32)[None, :]
    stats = jnp.concatenate(
        [
            jnp.sum(resid_float * resid_float, axis=1, keepdims=True),
            jnp.dot(scaled, router_weight, precision=lax.Precision.HIGHEST),
        ],
        axis=1,
    )
    if lax.axis_size("kv") == 4:
        stats = stats + lax.ppermute(stats, "kv", [(i, i ^ 1) for i in range(4)])
        stats = stats + lax.ppermute(stats, "kv", [(i, i ^ 2) for i in range(4)])
    else:
        stats = lax.psum(stats, "kv")
    square_sum = stats[:, 0]
    raw_logits = stats[:, 1:]
    inverse = lax.rsqrt(square_sum / D + EPSILON)
    logits = raw_logits * inverse[:, None]
    normed = (scaled * inverse[:, None]).astype(jnp.bfloat16)
    expert_count = router_weight.shape[1]
    top_count = expert_routes.shape[1]
    chosen_logit = jnp.sum(
        jnp.where(
            expert_routes[:, :, None] == jnp.arange(expert_count)[None, None, :],
            logits[:, None, :],
            0.0,
        ),
        axis=2,
    )
    lifted = jnp.exp(chosen_logit)
    gates = lifted / jnp.sum(lifted, axis=1, keepdims=True)
    capacity = CAP
    flat_routes = expert_routes.reshape(-1)
    assign_count = flat_routes.shape[0]
    onehot = (flat_routes[:, None] == jnp.arange(expert_count)[None, :]).astype(jnp.int32)
    earlier = jnp.cumsum(onehot, axis=0) - onehot
    slot_rank = jnp.sum(earlier * onehot, axis=1)
    target = flat_routes * capacity + slot_rank
    slot_total = expert_count * capacity
    source_item = jax.ops.segment_sum(jnp.arange(assign_count) + 1, target, num_segments=slot_total)
    packed_rows = jnp.where(
        (source_item > 0)[:, None],
        normed[jnp.maximum(source_item - 1, 0) // top_count],
        jnp.zeros((), jnp.bfloat16),
    )
    pieces_here = w_gate.shape[0]
    feature_part = normed.shape[1]
    paired = pieces_here % 2 == 0
    kv_count = lax.axis_size("kv")
    core_bit = lax.axis_index("kv") % 2
    chip_bit = lax.axis_index("kv") // 2
    flip_core = [(i, i ^ 1) for i in range(kv_count)]
    flip_chip = [(i, i ^ 2) for i in range(kv_count)]
    if paired:
        experts_here = pieces_here // 2
        outgoing_rows = packed_rows.reshape(blk_count, experts_here, capacity, feature_part)
    else:
        experts_here = 1
        outgoing_rows = jnp.broadcast_to(
            packed_rows.reshape(expert_count, 1, capacity, feature_part),
            (expert_count, 2, capacity, feature_part),
        ).reshape(blk_count, pieces_here, capacity, feature_part)

    def pair_stage(landed_rows, gate_w, up_w):
        chunk_pieces = gate_w.shape[0]
        if paired:
            rows_in = jnp.broadcast_to(
                landed_rows[:, :, None],
                (blk_count, chunk_pieces // 2, 2, capacity, feature_part),
            ).reshape(blk_count, chunk_pieces, capacity, feature_part)
        else:
            rows_in = landed_rows
        gate_part = jnp.einsum("spkd,pdu->spku", rows_in, gate_w, preferred_element_type=jnp.float32)
        up_part = jnp.einsum("spkd,pdu->spku", rows_in, up_w, preferred_element_type=jnp.float32)
        both_parts = jnp.stack([gate_part, up_part], axis=3).astype(jnp.bfloat16)
        half = both_parts.shape[0] // 2
        kept = lax.dynamic_slice_in_dim(both_parts, core_bit * half, half, 0)
        given = lax.dynamic_slice_in_dim(both_parts, (1 - core_bit) * half, half, 0)
        pair_sum = kept.astype(jnp.float32) + lax.ppermute(given, "kv", flip_core).astype(jnp.float32)
        return pair_sum.astype(jnp.bfloat16)

    def out_stage(pair_sum, down_w):
        chunk_pieces = down_w.shape[0]
        quarter = pair_sum.shape[0] // 2
        chip_kept = lax.dynamic_slice_in_dim(pair_sum, chip_bit * quarter, quarter, 0)
        chip_given = lax.dynamic_slice_in_dim(pair_sum, (1 - chip_bit) * quarter, quarter, 0)
        whole = chip_kept.astype(jnp.float32) + lax.ppermute(
            chip_given, "kv", flip_chip
        ).astype(jnp.float32)
        hidden_quarter = (jax.nn.silu(whole[:, :, :, 0]) * whole[:, :, :, 1]).astype(jnp.bfloat16)
        hidden_far = lax.ppermute(hidden_quarter, "kv", flip_chip)
        hidden_half = jnp.where(
            chip_bit == 0,
            jnp.concatenate([hidden_quarter, hidden_far], axis=0),
            jnp.concatenate([hidden_far, hidden_quarter], axis=0),
        )
        hidden_other = lax.ppermute(hidden_half, "kv", flip_core)
        hidden = jnp.where(
            core_bit == 0,
            jnp.concatenate([hidden_half, hidden_other], axis=0),
            jnp.concatenate([hidden_other, hidden_half], axis=0),
        )
        piece_out = jnp.einsum(
            "spku,pud->spkd", hidden, down_w, preferred_element_type=jnp.float32
        ).astype(jnp.bfloat16)
        if paired:
            half_sum = piece_out.reshape(blk_count, chunk_pieces // 2, 2, capacity, feature_part)
            half_sum = jnp.sum(half_sum.astype(jnp.float32), axis=2).astype(jnp.bfloat16)
            return lax.all_to_all(half_sum, "blk", split_axis=0, concat_axis=0, tiled=True)
        returned = lax.all_to_all(piece_out, "blk", split_axis=0, concat_axis=0, tiled=True)
        per_piece = returned.reshape(expert_count, 2, capacity, feature_part).astype(jnp.float32)
        return (per_piece[:, 0] + per_piece[:, 1]).astype(jnp.bfloat16)

    chunk_count = CHUNKS if paired and experts_here % CHUNKS == 0 else 1
    chunk_experts = experts_here // chunk_count
    chunk_pieces = pieces_here // chunk_count
    piece_sets = [slice(i * chunk_pieces, (i + 1) * chunk_pieces) for i in range(chunk_count)]
    landed_sets = [
        lax.all_to_all(
            outgoing_rows[:, i * chunk_experts : (i + 1) * chunk_experts],
            "blk",
            split_axis=0,
            concat_axis=0,
            tiled=True,
        )
        for i in range(chunk_count)
    ]
    pair_sets = []
    for i in range(chunk_count):
        landed_now = landed_sets[i]
        if pair_sets:
            pair_sets[-1], landed_now = lax.optimization_barrier((pair_sets[-1], landed_now))
        pair_sets.append(pair_stage(landed_now, w_gate[piece_sets[i]], w_up[piece_sets[i]]))
    per_chunk = [out_stage(pair_sets[i], w_down[piece_sets[i]]) for i in range(chunk_count)]
    if paired:
        per_slot = jnp.concatenate(per_chunk, axis=1).reshape(slot_total, feature_part)
    else:
        per_slot = per_chunk[0].reshape(slot_total, feature_part)
    per_slot = per_slot.astype(jnp.float32)
    routed = per_slot[target].reshape(stretch_len, top_count, feature_part)
    moe_out = jnp.sum(routed * gates[:, :, None], axis=1)
    layer_out = (resid_float + moe_out).astype(jnp.bfloat16)
    here_old = in_use & (decode_holder[:, :max_blocks] == own_index)
    from_old = jnp.where(here_old, block_holder, blk_count).reshape(-1)
    put_old = jax.ops.segment_sum(
        (decode_slot[:, :max_blocks] + 1).reshape(-1), from_old, num_segments=blk_count
    )
    here_new = decode_holder[:, max_blocks:] == own_index
    request_ids = jnp.broadcast_to(jnp.arange(decode_holder.shape[0])[:, None], here_new.shape)
    from_new = jnp.where(here_new, request_ids, blk_count).reshape(-1)
    put_new = jax.ops.segment_sum(
        (decode_slot[:, max_blocks:] + 1).reshape(-1), from_new, num_segments=blk_count
    )
    placing = put_old + put_new
    decode_size = pool_size + fresh_count
    placement = (placing[None, :] - 1 == jnp.arange(decode_size)[:, None]).astype(jnp.bfloat16)
    decoded = jnp.dot(
        placement, landed.reshape(blk_count, -1), preferred_element_type=jnp.float32
    ).astype(jnp.bfloat16)
    decode_pool = decoded.reshape(decode_size, block_len, 1, 2, head_dim)
    return (layer_out, decode_pool)


def solution(mesh):
    in_specs = (
        P("blk", "kv"),
        P("blk", "kv"),
        P("blk", "kv", None, None),
        P("blk", None, "kv", None, None),
        P(),
        P(),
        P(),
        P(),
        P(),
        P("kv", "blk"),
        P("kv"),
        P("kv", None),
        P("blk", None),
        P("blk", "kv", None),
        P("blk", "kv", None),
        P("blk", None, "kv"),
    )
    out_specs = (P("blk", "kv"), P("blk", None, "kv", None, None))
    return jax.shard_map(
        per_device, mesh=mesh, in_specs=in_specs, out_specs=out_specs, check_vma=False
    )
```

```python
import math

import jax
import jax.numpy as jnp
from jax import lax
from jax.sharding import PartitionSpec as P

D = 2560
CAP = 8
CHUNKS = 2


EPSILON = 1e-05
MASKED = -1e30


def head_rows(asked_rows, head_count, head_dim):
    stretch_len = asked_rows.shape[0]
    return (
        asked_rows.reshape(stretch_len, head_count, head_dim)
        .transpose(1, 0, 2)
        .reshape(head_count * stretch_len, head_dim)
    )


def absorb(carried, scores, value_rows):
    running_max, denominator, accumulated = carried
    new_max = jnp.maximum(running_max, jnp.max(scores, axis=1))
    decay = jnp.exp(running_max - new_max)
    raised = jnp.exp(scores - new_max[:, None])
    denominator = denominator * decay + jnp.sum(raised, axis=1)
    accumulated = accumulated * decay[:, None] + jnp.dot(
        raised.astype(jnp.bfloat16), value_rows, preferred_element_type=jnp.float32
    )
    return (new_max, denominator, accumulated)


def attend_blocks(carried, query_rows, blocks, present, scale):
    block_count = blocks.shape[0]
    block_len = blocks.shape[1]
    head_dim = blocks.shape[3]
    tile_blocks = min(32, block_count)
    span = tile_blocks * block_len
    flags = present.astype(jnp.int32)
    live_count = jnp.sum(flags)
    order_rank = jnp.cumsum(flags) - 1
    positions = jnp.arange(block_count)
    chosen = present[None, :] & (order_rank[None, :] == positions[:, None])
    packing = jnp.sum(jnp.where(chosen, positions[None, :], 0), axis=1)
    packed = blocks[packing]

    def advance(turn, state_now):
        segment = lax.dynamic_slice_in_dim(packed, turn * tile_blocks, tile_blocks, 0)
        key_rows = segment[:, :, 0].reshape(span, head_dim)
        value_rows = segment[:, :, 1].reshape(span, head_dim)
        scores = (
            jnp.einsum("qd,kd->qk", query_rows, key_rows, preferred_element_type=jnp.float32)
            * scale
        )
        is_live = turn * tile_blocks + jnp.arange(span) // block_len < live_count
        scores = jnp.where(is_live[None, :], scores, MASKED)
        return absorb(state_now, scores, value_rows)

    return lax.fori_loop(0, (live_count + tile_blocks - 1) // tile_blocks, advance, carried)


def per_device(
    hidden_in,
    queries,
    new_kv,
    cache_pool,
    cache_len,
    block_holder,
    block_slot,
    decode_holder,
    decode_slot,
    out_weight,
    norm_gain,
    router_weight,
    expert_routes,
    w_gate,
    w_up,
    w_down,
):
    blk_count = lax.axis_size("blk")
    own_index = lax.axis_index("blk")
    stretch_len = queries.shape[0]
    head_dim = new_kv.shape[3]
    head_count = queries.shape[1] // head_dim
    pool_size = cache_pool.shape[0]
    block_len = cache_pool.shape[1]
    max_blocks = block_holder.shape[1]
    fresh_count = stretch_len // block_len
    scale = 1.0 / math.sqrt(head_dim)
    devices = jnp.arange(blk_count)
    in_use = jnp.arange(max_blocks)[None, :] < (cache_len // block_len)[:, None]
    pool_rows = cache_pool[:, :, 0]
    fresh_rows = new_kv[:, 0]
    sources = jnp.concatenate(
        [pool_rows, fresh_rows.reshape(fresh_count, block_len, 2, head_dim)], axis=0
    )
    held_here = in_use & (block_holder == own_index)
    old_target = jnp.where(held_here, decode_holder[:, :max_blocks], blk_count).reshape(-1)
    pick_old = jax.ops.segment_sum((block_slot + 1).reshape(-1), old_target, num_segments=blk_count)
    pick_new = jax.ops.segment_sum(
        pool_size + 1 + jnp.arange(fresh_count),
        decode_holder[own_index, max_blocks:],
        num_segments=blk_count,
    )
    picked = pick_old + pick_new
    sending = jnp.where(
        (picked > 0)[:, None, None, None],
        sources[jnp.maximum(picked - 1, 0)],
        jnp.zeros((), jnp.bfloat16),
    )
    source_request = jnp.zeros_like(devices) + own_index
    match_here = (block_holder[devices] == own_index) & in_use[devices]
    outgoing = pool_rows[jnp.sum(jnp.where(match_here, block_slot[devices], 0), axis=1)]
    both_blocks = lax.all_to_all(
        jnp.stack([sending, outgoing], axis=1), "blk", split_axis=0, concat_axis=0, tiled=True
    )
    landed = both_blocks[:, 0]
    arrived = both_blocks[:, 1]
    present = jnp.any(
        (block_holder[source_request] == devices[:, None]) & in_use[source_request], axis=1
    )
    own_rows = head_rows(queries, head_count, head_dim)
    row_count = head_count * stretch_len
    start_state = (
        jnp.full((row_count,), MASKED, jnp.float32),
        jnp.zeros((row_count,), jnp.float32),
        jnp.zeros((row_count, head_dim), jnp.float32),
    )
    query_pos = jnp.arange(row_count) % stretch_len
    allowed = jnp.arange(stretch_len)[None, :] <= query_pos[:, None]
    local_scores = (
        jnp.einsum("qd,kd->qk", own_rows, fresh_rows[:, 0], preferred_element_type=jnp.float32)
        * scale
    )
    carried = absorb(start_state, jnp.where(allowed, local_scores, MASKED), fresh_rows[:, 1])
    carried = attend_blocks(carried, own_rows, arrived, present, scale)
    running_max, denominator, accumulated = carried
    attended = (
        (accumulated / denominator[:, None])
        .reshape(head_count, stretch_len, head_dim)
        .transpose(1, 0, 2)
    )
    attended = attended.reshape(stretch_len, head_count * head_dim).astype(jnp.bfloat16)
    every_token = lax.all_to_all(
        jnp.broadcast_to(attended[None], (blk_count,) + attended.shape), "blk", 0, 0, tiled=True
    ).reshape(-1, attended.shape[1])
    column_part = jnp.dot(
        every_token, out_weight, preferred_element_type=jnp.float32
    ).astype(jnp.bfloat16)
    projected = lax.all_to_all(column_part, "blk", split_axis=0, concat_axis=1, tiled=True)
    kv_index = lax.axis_index("kv")
    if lax.axis_size("kv") == 4:
        chip_bit = kv_index // 2
        core_low = kv_index % 2
        swap_core = [(i, i ^ 1) for i in range(4)]
        swap_chip = [(i, i ^ 2) for i in range(4)]
        chip_cols = projected.shape[1] // 2
        chip_kept = lax.dynamic_slice_in_dim(projected, chip_bit * chip_cols, chip_cols, 1)
        chip_given = lax.dynamic_slice_in_dim(projected, (1 - chip_bit) * chip_cols, chip_cols, 1)
        chip_sum = chip_kept.astype(jnp.float32) + lax.ppermute(
            chip_given, "kv", swap_chip
        ).astype(jnp.float32)
        own_cols = chip_cols // 2
        core_kept = lax.dynamic_slice_in_dim(chip_sum, core_low * own_cols, own_cols, 1)
        core_given = lax.dynamic_slice_in_dim(
            chip_sum, (1 - core_low) * own_cols, own_cols, 1
        ).astype(jnp.bfloat16)
        head_total = core_kept + lax.ppermute(core_given, "kv", swap_core).astype(jnp.float32)
    else:
        head_total = lax.psum_scatter(
            projected, "kv", scatter_dimension=1, tiled=True
        ).astype(jnp.float32)
    residual = (hidden_in.astype(jnp.float32) + head_total).astype(jnp.bfloat16)
    resid_float = residual.astype(jnp.float32)
    scaled = resid_float * norm_gain.astype(jnp.float32)[None, :]
    stats = jnp.concatenate(
        [
            jnp.sum(resid_float * resid_float, axis=1, keepdims=True),
            jnp.dot(scaled, router_weight, precision=lax.Precision.HIGHEST),
        ],
        axis=1,
    )
    if lax.axis_size("kv") == 4:
        stats = stats + lax.ppermute(stats, "kv", [(i, i ^ 1) for i in range(4)])
        stats = stats + lax.ppermute(stats, "kv", [(i, i ^ 2) for i in range(4)])
    else:
        stats = lax.psum(stats, "kv")
    square_sum = stats[:, 0]
    raw_logits = stats[:, 1:]
    inverse = lax.rsqrt(square_sum / D + EPSILON)
    logits = raw_logits * inverse[:, None]
    normed = (scaled * inverse[:, None]).astype(jnp.bfloat16)
    expert_count = router_weight.shape[1]
    top_count = expert_routes.shape[1]
    chosen_logit = jnp.sum(
        jnp.where(
            expert_routes[:, :, None] == jnp.arange(expert_count)[None, None, :],
            logits[:, None, :],
            0.0,
        ),
        axis=2,
    )
    lifted = jnp.exp(chosen_logit)
    gates = lifted / jnp.sum(lifted, axis=1, keepdims=True)
    capacity = CAP
    flat_routes = expert_routes.reshape(-1)
    assign_count = flat_routes.shape[0]
    onehot = (flat_routes[:, None] == jnp.arange(expert_count)[None, :]).astype(jnp.int32)
    earlier = jnp.cumsum(onehot, axis=0) - onehot
    slot_rank = jnp.sum(earlier * onehot, axis=1)
    target = flat_routes * capacity + slot_rank
    slot_total = expert_count * capacity
    source_item = jax.ops.segment_sum(jnp.arange(assign_count) + 1, target, num_segments=slot_total)
    packed_rows = jnp.where(
        (source_item > 0)[:, None],
        normed[jnp.maximum(source_item - 1, 0) // top_count],
        jnp.zeros((), jnp.bfloat16),
    )
    pieces_here = w_gate.shape[0]
    feature_part = normed.shape[1]
    paired = pieces_here % 2 == 0
    kv_count = lax.axis_size("kv")
    core_bit = lax.axis_index("kv") % 2
    chip_bit = lax.axis_index("kv") // 2
    flip_core = [(i, i ^ 1) for i in range(kv_count)]
    flip_chip = [(i, i ^ 2) for i in range(kv_count)]
    if paired:
        experts_here = pieces_here // 2
        outgoing_rows = packed_rows.reshape(blk_count, experts_here, capacity, feature_part)
    else:
        experts_here = 1
        outgoing_rows = jnp.broadcast_to(
            packed_rows.reshape(expert_count, 1, capacity, feature_part),
            (expert_count, 2, capacity, feature_part),
        ).reshape(blk_count, pieces_here, capacity, feature_part)

    def pair_stage(landed_rows, gate_w, up_w):
        chunk_pieces = gate_w.shape[0]
        if paired:
            rows_in = jnp.broadcast_to(
                landed_rows[:, :, None],
                (blk_count, chunk_pieces // 2, 2, capacity, feature_part),
            ).reshape(blk_count, chunk_pieces, capacity, feature_part)
        else:
            rows_in = landed_rows
        gate_part = jnp.einsum("spkd,pdu->spku", rows_in, gate_w, preferred_element_type=jnp.float32)
        up_part = jnp.einsum("spkd,pdu->spku", rows_in, up_w, preferred_element_type=jnp.float32)
        both_parts = jnp.stack([gate_part, up_part], axis=3).astype(jnp.bfloat16)
        half = both_parts.shape[0] // 2
        kept = lax.dynamic_slice_in_dim(both_parts, core_bit * half, half, 0)
        given = lax.dynamic_slice_in_dim(both_parts, (1 - core_bit) * half, half, 0)
        pair_sum = kept.astype(jnp.float32) + lax.ppermute(given, "kv", flip_core).astype(jnp.float32)
        return pair_sum.astype(jnp.bfloat16)

    def chip_split(pair_sum):
        quarter = pair_sum.shape[0] // 2
        chip_kept = lax.dynamic_slice_in_dim(pair_sum, chip_bit * quarter, quarter, 0)
        chip_given = lax.dynamic_slice_in_dim(pair_sum, (1 - chip_bit) * quarter, quarter, 0)
        return chip_kept, chip_given

    def out_stage(chip_kept, chip_given, down_w):
        chunk_pieces = down_w.shape[0]
        whole = chip_kept.astype(jnp.float32) + lax.ppermute(
            chip_given, "kv", flip_chip
        ).astype(jnp.float32)
        hidden_quarter = (jax.nn.silu(whole[:, :, :, 0]) * whole[:, :, :, 1]).astype(jnp.bfloat16)
        hidden_far = lax.ppermute(hidden_quarter, "kv", flip_chip)
        hidden_half = jnp.where(
            chip_bit == 0,
            jnp.concatenate([hidden_quarter, hidden_far], axis=0),
            jnp.concatenate([hidden_far, hidden_quarter], axis=0),
        )
        hidden_other = lax.ppermute(hidden_half, "kv", flip_core)
        hidden = jnp.where(
            core_bit == 0,
            jnp.concatenate([hidden_half, hidden_other], axis=0),
            jnp.concatenate([hidden_other, hidden_half], axis=0),
        )
        piece_out = jnp.einsum(
            "spku,pud->spkd", hidden, down_w, preferred_element_type=jnp.float32
        ).astype(jnp.bfloat16)
        if paired:
            half_sum = piece_out.reshape(blk_count, chunk_pieces // 2, 2, capacity, feature_part)
            half_sum = jnp.sum(half_sum.astype(jnp.float32), axis=2).astype(jnp.bfloat16)
            return lax.all_to_all(half_sum, "blk", split_axis=0, concat_axis=0, tiled=True)
        returned = lax.all_to_all(piece_out, "blk", split_axis=0, concat_axis=0, tiled=True)
        per_piece = returned.reshape(expert_count, 2, capacity, feature_part).astype(jnp.float32)
        return (per_piece[:, 0] + per_piece[:, 1]).astype(jnp.bfloat16)

    chunk_count = CHUNKS if paired and experts_here % CHUNKS == 0 else 1
    chunk_experts = experts_here // chunk_count
    chunk_pieces = pieces_here // chunk_count
    piece_sets = [slice(i * chunk_pieces, (i + 1) * chunk_pieces) for i in range(chunk_count)]
    split_sets = []
    for i in range(chunk_count):
        rows_now = outgoing_rows[:, i * chunk_experts : (i + 1) * chunk_experts]
        if split_sets:
            last_kept, last_given = split_sets[-1]
            last_given, rows_now = lax.optimization_barrier((last_given, rows_now))
            split_sets[-1] = (last_kept, last_given)
        landed_now = lax.all_to_all(rows_now, "blk", split_axis=0, concat_axis=0, tiled=True)
        pair_now = pair_stage(landed_now, w_gate[piece_sets[i]], w_up[piece_sets[i]])
        split_sets.append(chip_split(pair_now))
    per_chunk = [
        out_stage(split_sets[i][0], split_sets[i][1], w_down[piece_sets[i]])
        for i in range(chunk_count)
    ]
    if paired:
        per_slot = jnp.concatenate(per_chunk, axis=1).reshape(slot_total, feature_part)
    else:
        per_slot = per_chunk[0].reshape(slot_total, feature_part)
    per_slot = per_slot.astype(jnp.float32)
    routed = per_slot[target].reshape(stretch_len, top_count, feature_part)
    moe_out = jnp.sum(routed * gates[:, :, None], axis=1)
    layer_out = (resid_float + moe_out).astype(jnp.bfloat16)
    here_old = in_use & (decode_holder[:, :max_blocks] == own_index)
    from_old = jnp.where(here_old, block_holder, blk_count).reshape(-1)
    put_old = jax.ops.segment_sum(
        (decode_slot[:, :max_blocks] + 1).reshape(-1), from_old, num_segments=blk_count
    )
    here_new = decode_holder[:, max_blocks:] == own_index
    request_ids = jnp.broadcast_to(jnp.arange(decode_holder.shape[0])[:, None], here_new.shape)
    from_new = jnp.where(here_new, request_ids, blk_count).reshape(-1)
    put_new = jax.ops.segment_sum(
        (decode_slot[:, max_blocks:] + 1).reshape(-1), from_new, num_segments=blk_count
    )
    placing = put_old + put_new
    decode_size = pool_size + fresh_count
    placement = (placing[None, :] - 1 == jnp.arange(decode_size)[:, None]).astype(jnp.bfloat16)
    decoded = jnp.dot(
        placement, landed.reshape(blk_count, -1), preferred_element_type=jnp.float32
    ).astype(jnp.bfloat16)
    decode_pool = decoded.reshape(decode_size, block_len, 1, 2, head_dim)
    return (layer_out, decode_pool)


def solution(mesh):
    in_specs = (
        P("blk", "kv"),
        P("blk", "kv"),
        P("blk", "kv", None, None),
        P("blk", None, "kv", None, None),
        P(),
        P(),
        P(),
        P(),
        P(),
        P("kv", "blk"),
        P("kv"),
        P("kv", None),
        P("blk", None),
        P("blk", "kv", None),
        P("blk", "kv", None),
        P("blk", None, "kv"),
    )
    out_specs = (P("blk", "kv"), P("blk", None, "kv", None, None))
    return jax.shard_map(
        per_device, mesh=mesh, in_specs=in_specs, out_specs=out_specs, check_vma=False
    )
```

```python
import math

import jax
import jax.numpy as jnp
from jax import lax
from jax.sharding import PartitionSpec as P

D = 2560
CAP = 8
CHUNKS = 1


EPSILON = 1e-05
MASKED = -1e30


def head_rows(asked_rows, head_count, head_dim):
    stretch_len = asked_rows.shape[0]
    return (
        asked_rows.reshape(stretch_len, head_count, head_dim)
        .transpose(1, 0, 2)
        .reshape(head_count * stretch_len, head_dim)
    )


def absorb(carried, scores, value_rows):
    running_max, denominator, accumulated = carried
    new_max = jnp.maximum(running_max, jnp.max(scores, axis=1))
    decay = jnp.exp(running_max - new_max)
    raised = jnp.exp(scores - new_max[:, None])
    denominator = denominator * decay + jnp.sum(raised, axis=1)
    accumulated = accumulated * decay[:, None] + jnp.dot(
        raised.astype(jnp.bfloat16), value_rows, preferred_element_type=jnp.float32
    )
    return (new_max, denominator, accumulated)


def attend_blocks(carried, query_rows, blocks, present, scale):
    block_count = blocks.shape[0]
    block_len = blocks.shape[1]
    head_dim = blocks.shape[3]
    tile_blocks = min(32, block_count)
    span = tile_blocks * block_len
    flags = present.astype(jnp.int32)
    live_count = jnp.sum(flags)
    order_rank = jnp.cumsum(flags) - 1
    positions = jnp.arange(block_count)
    chosen = present[None, :] & (order_rank[None, :] == positions[:, None])
    packing = jnp.sum(jnp.where(chosen, positions[None, :], 0), axis=1)
    packed = blocks[packing]

    def advance(turn, state_now):
        segment = lax.dynamic_slice_in_dim(packed, turn * tile_blocks, tile_blocks, 0)
        key_rows = segment[:, :, 0].reshape(span, head_dim)
        value_rows = segment[:, :, 1].reshape(span, head_dim)
        scores = (
            jnp.einsum("qd,kd->qk", query_rows, key_rows, preferred_element_type=jnp.float32)
            * scale
        )
        is_live = turn * tile_blocks + jnp.arange(span) // block_len < live_count
        scores = jnp.where(is_live[None, :], scores, MASKED)
        return absorb(state_now, scores, value_rows)

    return lax.fori_loop(0, (live_count + tile_blocks - 1) // tile_blocks, advance, carried)


def per_device(
    hidden_in,
    queries,
    new_kv,
    cache_pool,
    cache_len,
    block_holder,
    block_slot,
    decode_holder,
    decode_slot,
    out_weight,
    norm_gain,
    router_weight,
    expert_routes,
    w_gate,
    w_up,
    w_down,
):
    blk_count = lax.axis_size("blk")
    own_index = lax.axis_index("blk")
    stretch_len = queries.shape[0]
    head_dim = new_kv.shape[3]
    head_count = queries.shape[1] // head_dim
    pool_size = cache_pool.shape[0]
    block_len = cache_pool.shape[1]
    max_blocks = block_holder.shape[1]
    fresh_count = stretch_len // block_len
    scale = 1.0 / math.sqrt(head_dim)
    devices = jnp.arange(blk_count)
    in_use = jnp.arange(max_blocks)[None, :] < (cache_len // block_len)[:, None]
    pool_rows = cache_pool[:, :, 0]
    fresh_rows = new_kv[:, 0]
    sources = jnp.concatenate(
        [pool_rows, fresh_rows.reshape(fresh_count, block_len, 2, head_dim)], axis=0
    )
    held_here = in_use & (block_holder == own_index)
    old_target = jnp.where(held_here, decode_holder[:, :max_blocks], blk_count).reshape(-1)
    pick_old = jax.ops.segment_sum((block_slot + 1).reshape(-1), old_target, num_segments=blk_count)
    pick_new = jax.ops.segment_sum(
        pool_size + 1 + jnp.arange(fresh_count),
        decode_holder[own_index, max_blocks:],
        num_segments=blk_count,
    )
    picked = pick_old + pick_new
    sending = jnp.where(
        (picked > 0)[:, None, None, None],
        sources[jnp.maximum(picked - 1, 0)],
        jnp.zeros((), jnp.bfloat16),
    )
    source_request = jnp.zeros_like(devices) + own_index
    match_here = (block_holder[devices] == own_index) & in_use[devices]
    outgoing = pool_rows[jnp.sum(jnp.where(match_here, block_slot[devices], 0), axis=1)]
    block_shape = sending.shape[1:]
    both_blocks = lax.all_to_all(
        jnp.stack(
            [sending.reshape(blk_count, -1, head_dim), outgoing.reshape(blk_count, -1, head_dim)],
            axis=1,
        ),
        "blk",
        split_axis=0,
        concat_axis=0,
        tiled=True,
    )
    landed = both_blocks[:, 0].reshape((blk_count,) + block_shape)
    arrived = both_blocks[:, 1].reshape((blk_count,) + block_shape)
    present = jnp.any(
        (block_holder[source_request] == devices[:, None]) & in_use[source_request], axis=1
    )
    own_rows = head_rows(queries, head_count, head_dim)
    row_count = head_count * stretch_len
    start_state = (
        jnp.full((row_count,), MASKED, jnp.float32),
        jnp.zeros((row_count,), jnp.float32),
        jnp.zeros((row_count, head_dim), jnp.float32),
    )
    query_pos = jnp.arange(row_count) % stretch_len
    allowed = jnp.arange(stretch_len)[None, :] <= query_pos[:, None]
    local_scores = (
        jnp.einsum("qd,kd->qk", own_rows, fresh_rows[:, 0], preferred_element_type=jnp.float32)
        * scale
    )
    carried = absorb(start_state, jnp.where(allowed, local_scores, MASKED), fresh_rows[:, 1])
    carried = attend_blocks(carried, own_rows, arrived, present, scale)
    running_max, denominator, accumulated = carried
    attended = (
        (accumulated / denominator[:, None])
        .reshape(head_count, stretch_len, head_dim)
        .transpose(1, 0, 2)
    )
    attended = attended.reshape(stretch_len, head_count * head_dim).astype(jnp.bfloat16)
    every_token = lax.all_to_all(
        jnp.broadcast_to(attended[None], (blk_count,) + attended.shape), "blk", 0, 0, tiled=True
    ).reshape(-1, attended.shape[1])
    column_part = jnp.dot(
        every_token, out_weight, preferred_element_type=jnp.float32
    ).astype(jnp.bfloat16)
    projected = lax.all_to_all(column_part, "blk", split_axis=0, concat_axis=1, tiled=True)
    kv_index = lax.axis_index("kv")
    if lax.axis_size("kv") == 4:
        chip_bit = kv_index // 2
        core_low = kv_index % 2
        swap_core = [(i, i ^ 1) for i in range(4)]
        swap_chip = [(i, i ^ 2) for i in range(4)]
        chip_cols = projected.shape[1] // 2
        chip_kept = lax.dynamic_slice_in_dim(projected, chip_bit * chip_cols, chip_cols, 1)
        chip_given = lax.dynamic_slice_in_dim(projected, (1 - chip_bit) * chip_cols, chip_cols, 1)
        chip_sum = chip_kept.astype(jnp.float32) + lax.ppermute(
            chip_given, "kv", swap_chip
        ).astype(jnp.float32)
        own_cols = chip_cols // 2
        core_kept = lax.dynamic_slice_in_dim(chip_sum, core_low * own_cols, own_cols, 1)
        core_given = lax.dynamic_slice_in_dim(
            chip_sum, (1 - core_low) * own_cols, own_cols, 1
        ).astype(jnp.bfloat16)
        head_total = core_kept + lax.ppermute(core_given, "kv", swap_core).astype(jnp.float32)
    else:
        head_total = lax.psum_scatter(
            projected, "kv", scatter_dimension=1, tiled=True
        ).astype(jnp.float32)
    residual = (hidden_in.astype(jnp.float32) + head_total).astype(jnp.bfloat16)
    resid_float = residual.astype(jnp.float32)
    scaled = resid_float * norm_gain.astype(jnp.float32)[None, :]
    stats = jnp.concatenate(
        [
            jnp.sum(resid_float * resid_float, axis=1, keepdims=True),
            jnp.dot(scaled, router_weight, precision=lax.Precision.HIGHEST),
        ],
        axis=1,
    )
    if lax.axis_size("kv") == 4:
        stats = stats + lax.ppermute(stats, "kv", [(i, i ^ 1) for i in range(4)])
        stats = stats + lax.ppermute(stats, "kv", [(i, i ^ 2) for i in range(4)])
    else:
        stats = lax.psum(stats, "kv")
    square_sum = stats[:, 0]
    raw_logits = stats[:, 1:]
    inverse = lax.rsqrt(square_sum / D + EPSILON)
    logits = raw_logits * inverse[:, None]
    normed = (scaled * inverse[:, None]).astype(jnp.bfloat16)
    expert_count = router_weight.shape[1]
    top_count = expert_routes.shape[1]
    chosen_logit = jnp.sum(
        jnp.where(
            expert_routes[:, :, None] == jnp.arange(expert_count)[None, None, :],
            logits[:, None, :],
            0.0,
        ),
        axis=2,
    )
    lifted = jnp.exp(chosen_logit)
    gates = lifted / jnp.sum(lifted, axis=1, keepdims=True)
    capacity = CAP
    flat_routes = expert_routes.reshape(-1)
    assign_count = flat_routes.shape[0]
    onehot = (flat_routes[:, None] == jnp.arange(expert_count)[None, :]).astype(jnp.int32)
    earlier = jnp.cumsum(onehot, axis=0) - onehot
    slot_rank = jnp.sum(earlier * onehot, axis=1)
    target = flat_routes * capacity + slot_rank
    slot_total = expert_count * capacity
    source_item = jax.ops.segment_sum(jnp.arange(assign_count) + 1, target, num_segments=slot_total)
    packed_rows = jnp.where(
        (source_item > 0)[:, None],
        normed[jnp.maximum(source_item - 1, 0) // top_count],
        jnp.zeros((), jnp.bfloat16),
    )
    pieces_here = w_gate.shape[0]
    feature_part = normed.shape[1]
    paired = pieces_here % 2 == 0
    kv_count = lax.axis_size("kv")
    core_bit = lax.axis_index("kv") % 2
    chip_bit = lax.axis_index("kv") // 2
    flip_core = [(i, i ^ 1) for i in range(kv_count)]
    flip_chip = [(i, i ^ 2) for i in range(kv_count)]
    if paired:
        experts_here = pieces_here // 2
        outgoing_rows = packed_rows.reshape(blk_count, experts_here, capacity, feature_part)
    else:
        experts_here = 1
        outgoing_rows = jnp.broadcast_to(
            packed_rows.reshape(expert_count, 1, capacity, feature_part),
            (expert_count, 2, capacity, feature_part),
        ).reshape(blk_count, pieces_here, capacity, feature_part)

    def pair_stage(landed_rows, gate_w, up_w):
        chunk_pieces = gate_w.shape[0]
        if paired:
            rows_in = jnp.broadcast_to(
                landed_rows[:, :, None],
                (blk_count, chunk_pieces // 2, 2, capacity, feature_part),
            ).reshape(blk_count, chunk_pieces, capacity, feature_part)
        else:
            rows_in = landed_rows
        gate_part = jnp.einsum("spkd,pdu->spku", rows_in, gate_w, preferred_element_type=jnp.float32)
        up_part = jnp.einsum("spkd,pdu->spku", rows_in, up_w, preferred_element_type=jnp.float32)
        both_parts = jnp.stack([gate_part, up_part], axis=3).astype(jnp.bfloat16)
        half = both_parts.shape[0] // 2
        kept = lax.dynamic_slice_in_dim(both_parts, core_bit * half, half, 0)
        given = lax.dynamic_slice_in_dim(both_parts, (1 - core_bit) * half, half, 0)
        pair_sum = kept.astype(jnp.float32) + lax.ppermute(given, "kv", flip_core).astype(jnp.float32)
        return pair_sum.astype(jnp.bfloat16)

    def out_stage(pair_sum, down_w):
        chunk_pieces = down_w.shape[0]
        quarter = pair_sum.shape[0] // 2
        chip_kept = lax.dynamic_slice_in_dim(pair_sum, chip_bit * quarter, quarter, 0)
        chip_given = lax.dynamic_slice_in_dim(pair_sum, (1 - chip_bit) * quarter, quarter, 0)
        whole = chip_kept.astype(jnp.float32) + lax.ppermute(
            chip_given, "kv", flip_chip
        ).astype(jnp.float32)
        hidden_quarter = (jax.nn.silu(whole[:, :, :, 0]) * whole[:, :, :, 1]).astype(jnp.bfloat16)
        hidden_far = lax.ppermute(hidden_quarter, "kv", flip_chip)
        hidden_half = jnp.where(
            chip_bit == 0,
            jnp.concatenate([hidden_quarter, hidden_far], axis=0),
            jnp.concatenate([hidden_far, hidden_quarter], axis=0),
        )
        hidden_other = lax.ppermute(hidden_half, "kv", flip_core)
        hidden = jnp.where(
            core_bit == 0,
            jnp.concatenate([hidden_half, hidden_other], axis=0),
            jnp.concatenate([hidden_other, hidden_half], axis=0),
        )
        piece_out = jnp.einsum(
            "spku,pud->spkd", hidden, down_w, preferred_element_type=jnp.float32
        ).astype(jnp.bfloat16)
        if paired:
            half_sum = piece_out.reshape(blk_count, chunk_pieces // 2, 2, capacity, feature_part)
            half_sum = jnp.sum(half_sum.astype(jnp.float32), axis=2).astype(jnp.bfloat16)
            return lax.all_to_all(half_sum, "blk", split_axis=0, concat_axis=0, tiled=True)
        returned = lax.all_to_all(piece_out, "blk", split_axis=0, concat_axis=0, tiled=True)
        per_piece = returned.reshape(expert_count, 2, capacity, feature_part).astype(jnp.float32)
        return (per_piece[:, 0] + per_piece[:, 1]).astype(jnp.bfloat16)

    chunk_count = CHUNKS if paired and experts_here % CHUNKS == 0 else 1
    chunk_experts = experts_here // chunk_count
    chunk_pieces = pieces_here // chunk_count
    piece_sets = [slice(i * chunk_pieces, (i + 1) * chunk_pieces) for i in range(chunk_count)]
    landed_sets = [
        lax.all_to_all(
            outgoing_rows[:, i * chunk_experts : (i + 1) * chunk_experts],
            "blk",
            split_axis=0,
            concat_axis=0,
            tiled=True,
        )
        for i in range(chunk_count)
    ]
    pair_sets = []
    for i in range(chunk_count):
        landed_now = landed_sets[i]
        if pair_sets:
            pair_sets[-1], landed_now = lax.optimization_barrier((pair_sets[-1], landed_now))
        pair_sets.append(pair_stage(landed_now, w_gate[piece_sets[i]], w_up[piece_sets[i]]))
    per_chunk = [out_stage(pair_sets[i], w_down[piece_sets[i]]) for i in range(chunk_count)]
    if paired:
        per_slot = jnp.concatenate(per_chunk, axis=1).reshape(slot_total, feature_part)
    else:
        per_slot = per_chunk[0].reshape(slot_total, feature_part)
    per_slot = per_slot.astype(jnp.float32)
    routed = per_slot[target].reshape(stretch_len, top_count, feature_part)
    moe_out = jnp.sum(routed * gates[:, :, None], axis=1)
    layer_out = (resid_float + moe_out).astype(jnp.bfloat16)
    here_old = in_use & (decode_holder[:, :max_blocks] == own_index)
    from_old = jnp.where(here_old, block_holder, blk_count).reshape(-1)
    put_old = jax.ops.segment_sum(
        (decode_slot[:, :max_blocks] + 1).reshape(-1), from_old, num_segments=blk_count
    )
    here_new = decode_holder[:, max_blocks:] == own_index
    request_ids = jnp.broadcast_to(jnp.arange(decode_holder.shape[0])[:, None], here_new.shape)
    from_new = jnp.where(here_new, request_ids, blk_count).reshape(-1)
    put_new = jax.ops.segment_sum(
        (decode_slot[:, max_blocks:] + 1).reshape(-1), from_new, num_segments=blk_count
    )
    placing = put_old + put_new
    decode_size = pool_size + fresh_count
    placement = (placing[None, :] - 1 == jnp.arange(decode_size)[:, None]).astype(jnp.bfloat16)
    decoded = jnp.dot(
        placement, landed.reshape(blk_count, -1), preferred_element_type=jnp.float32
    ).astype(jnp.bfloat16)
    decode_pool = decoded.reshape(decode_size, block_len, 1, 2, head_dim)
    return (layer_out, decode_pool)


def solution(mesh):
    in_specs = (
        P("blk", "kv"),
        P("blk", "kv"),
        P("blk", "kv", None, None),
        P("blk", None, "kv", None, None),
        P(),
        P(),
        P(),
        P(),
        P(),
        P("kv", "blk"),
        P("kv"),
        P("kv", None),
        P("blk", None),
        P("blk", "kv", None),
        P("blk", "kv", None),
        P("blk", None, "kv"),
    )
    out_specs = (P("blk", "kv"), P("blk", None, "kv", None, None))
    return jax.shard_map(
        per_device, mesh=mesh, in_specs=in_specs, out_specs=out_specs, check_vma=False
    )
```

```python
import math

import jax
import jax.numpy as jnp
from jax import lax
from jax.sharding import PartitionSpec as P

D = 2560
CAP = 8
CHUNKS = 1


EPSILON = 1e-05
MASKED = -1e30


def head_rows(asked_rows, head_count, head_dim):
    stretch_len = asked_rows.shape[0]
    return (
        asked_rows.reshape(stretch_len, head_count, head_dim)
        .transpose(1, 0, 2)
        .reshape(head_count * stretch_len, head_dim)
    )


def absorb(carried, scores, value_rows):
    running_max, denominator, accumulated = carried
    new_max = jnp.maximum(running_max, jnp.max(scores, axis=1))
    decay = jnp.exp(running_max - new_max)
    raised = jnp.exp(scores - new_max[:, None])
    denominator = denominator * decay + jnp.sum(raised, axis=1)
    accumulated = accumulated * decay[:, None] + jnp.dot(
        raised.astype(jnp.bfloat16), value_rows, preferred_element_type=jnp.float32
    )
    return (new_max, denominator, accumulated)


def attend_blocks(carried, query_rows, blocks, present, scale):
    block_count = blocks.shape[0]
    block_len = blocks.shape[1]
    head_dim = blocks.shape[3]
    tile_blocks = min(32, block_count)
    span = tile_blocks * block_len
    flags = present.astype(jnp.int32)
    live_count = jnp.sum(flags)
    order_rank = jnp.cumsum(flags) - 1
    positions = jnp.arange(block_count)
    chosen = present[None, :] & (order_rank[None, :] == positions[:, None])
    packing = jnp.sum(jnp.where(chosen, positions[None, :], 0), axis=1)
    packed = blocks[packing]

    def advance(turn, state_now):
        segment = lax.dynamic_slice_in_dim(packed, turn * tile_blocks, tile_blocks, 0)
        key_rows = segment[:, :, 0].reshape(span, head_dim)
        value_rows = segment[:, :, 1].reshape(span, head_dim)
        scores = (
            jnp.einsum("qd,kd->qk", query_rows, key_rows, preferred_element_type=jnp.float32)
            * scale
        )
        is_live = turn * tile_blocks + jnp.arange(span) // block_len < live_count
        scores = jnp.where(is_live[None, :], scores, MASKED)
        return absorb(state_now, scores, value_rows)

    return lax.fori_loop(0, (live_count + tile_blocks - 1) // tile_blocks, advance, carried)


def per_device(
    hidden_in,
    queries,
    new_kv,
    cache_pool,
    cache_len,
    block_holder,
    block_slot,
    decode_holder,
    decode_slot,
    out_weight,
    norm_gain,
    router_weight,
    expert_routes,
    w_gate,
    w_up,
    w_down,
):
    blk_count = lax.axis_size("blk")
    own_index = lax.axis_index("blk")
    stretch_len = queries.shape[0]
    head_dim = new_kv.shape[3]
    head_count = queries.shape[1] // head_dim
    pool_size = cache_pool.shape[0]
    block_len = cache_pool.shape[1]
    max_blocks = block_holder.shape[1]
    fresh_count = stretch_len // block_len
    scale = 1.0 / math.sqrt(head_dim)
    devices = jnp.arange(blk_count)
    in_use = jnp.arange(max_blocks)[None, :] < (cache_len // block_len)[:, None]
    pool_rows = cache_pool[:, :, 0]
    fresh_rows = new_kv[:, 0]
    sources = jnp.concatenate(
        [pool_rows, fresh_rows.reshape(fresh_count, block_len, 2, head_dim)], axis=0
    )
    held_here = in_use & (block_holder == own_index)
    old_target = jnp.where(held_here, decode_holder[:, :max_blocks], blk_count).reshape(-1)
    pick_old = jax.ops.segment_sum((block_slot + 1).reshape(-1), old_target, num_segments=blk_count)
    pick_new = jax.ops.segment_sum(
        pool_size + 1 + jnp.arange(fresh_count),
        decode_holder[own_index, max_blocks:],
        num_segments=blk_count,
    )
    picked = pick_old + pick_new
    source_count = sources.shape[0]
    send_pick = (jnp.arange(source_count)[None, :] == (picked - 1)[:, None]).astype(jnp.bfloat16)
    sending = (
        jnp.dot(send_pick, sources.reshape(source_count, -1), preferred_element_type=jnp.float32)
        .astype(jnp.bfloat16)
        .reshape((blk_count,) + sources.shape[1:])
    )
    source_request = jnp.zeros_like(devices) + own_index
    match_here = (block_holder[devices] == own_index) & in_use[devices]
    out_slot = jnp.sum(jnp.where(match_here, block_slot[devices], 0), axis=1)
    out_pick = (jnp.arange(pool_size)[None, :] == out_slot[:, None]).astype(jnp.bfloat16)
    outgoing = (
        jnp.dot(out_pick, pool_rows.reshape(pool_size, -1), preferred_element_type=jnp.float32)
        .astype(jnp.bfloat16)
        .reshape((blk_count,) + pool_rows.shape[1:])
    )
    block_shape = sending.shape[1:]
    both_blocks = lax.all_to_all(
        jnp.stack(
            [sending.reshape(blk_count, -1, head_dim), outgoing.reshape(blk_count, -1, head_dim)],
            axis=1,
        ),
        "blk",
        split_axis=0,
        concat_axis=0,
        tiled=True,
    )
    landed = both_blocks[:, 0].reshape((blk_count,) + block_shape)
    arrived = both_blocks[:, 1].reshape((blk_count,) + block_shape)
    present = jnp.any(
        (block_holder[source_request] == devices[:, None]) & in_use[source_request], axis=1
    )
    own_rows = head_rows(queries, head_count, head_dim)
    row_count = head_count * stretch_len
    start_state = (
        jnp.full((row_count,), MASKED, jnp.float32),
        jnp.zeros((row_count,), jnp.float32),
        jnp.zeros((row_count, head_dim), jnp.float32),
    )
    query_pos = jnp.arange(row_count) % stretch_len
    allowed = jnp.arange(stretch_len)[None, :] <= query_pos[:, None]
    local_scores = (
        jnp.einsum("qd,kd->qk", own_rows, fresh_rows[:, 0], preferred_element_type=jnp.float32)
        * scale
    )
    carried = absorb(start_state, jnp.where(allowed, local_scores, MASKED), fresh_rows[:, 1])
    carried = attend_blocks(carried, own_rows, arrived, present, scale)
    running_max, denominator, accumulated = carried
    attended = (
        (accumulated / denominator[:, None])
        .reshape(head_count, stretch_len, head_dim)
        .transpose(1, 0, 2)
    )
    attended = attended.reshape(stretch_len, head_count * head_dim).astype(jnp.bfloat16)
    every_token = lax.all_to_all(
        jnp.broadcast_to(attended[None], (blk_count,) + attended.shape), "blk", 0, 0, tiled=True
    ).reshape(-1, attended.shape[1])
    column_part = jnp.dot(
        every_token, out_weight, preferred_element_type=jnp.float32
    ).astype(jnp.bfloat16)
    projected = lax.all_to_all(column_part, "blk", split_axis=0, concat_axis=1, tiled=True)
    kv_index = lax.axis_index("kv")
    if lax.axis_size("kv") == 4:
        chip_bit = kv_index // 2
        core_low = kv_index % 2
        swap_core = [(i, i ^ 1) for i in range(4)]
        swap_chip = [(i, i ^ 2) for i in range(4)]
        chip_cols = projected.shape[1] // 2
        chip_kept = lax.dynamic_slice_in_dim(projected, chip_bit * chip_cols, chip_cols, 1)
        chip_given = lax.dynamic_slice_in_dim(projected, (1 - chip_bit) * chip_cols, chip_cols, 1)
        chip_sum = chip_kept.astype(jnp.float32) + lax.ppermute(
            chip_given, "kv", swap_chip
        ).astype(jnp.float32)
        own_cols = chip_cols // 2
        core_kept = lax.dynamic_slice_in_dim(chip_sum, core_low * own_cols, own_cols, 1)
        core_given = lax.dynamic_slice_in_dim(
            chip_sum, (1 - core_low) * own_cols, own_cols, 1
        ).astype(jnp.bfloat16)
        head_total = core_kept + lax.ppermute(core_given, "kv", swap_core).astype(jnp.float32)
    else:
        head_total = lax.psum_scatter(
            projected, "kv", scatter_dimension=1, tiled=True
        ).astype(jnp.float32)
    residual = (hidden_in.astype(jnp.float32) + head_total).astype(jnp.bfloat16)
    resid_float = residual.astype(jnp.float32)
    scaled = resid_float * norm_gain.astype(jnp.float32)[None, :]
    stats = jnp.concatenate(
        [
            jnp.sum(resid_float * resid_float, axis=1, keepdims=True),
            jnp.dot(scaled, router_weight, precision=lax.Precision.HIGHEST),
        ],
        axis=1,
    )
    if lax.axis_size("kv") == 4:
        stats = stats + lax.ppermute(stats, "kv", [(i, i ^ 1) for i in range(4)])
        stats = stats + lax.ppermute(stats, "kv", [(i, i ^ 2) for i in range(4)])
    else:
        stats = lax.psum(stats, "kv")
    square_sum = stats[:, 0]
    raw_logits = stats[:, 1:]
    inverse = lax.rsqrt(square_sum / D + EPSILON)
    logits = raw_logits * inverse[:, None]
    normed = (scaled * inverse[:, None]).astype(jnp.bfloat16)
    expert_count = router_weight.shape[1]
    top_count = expert_routes.shape[1]
    chosen_logit = jnp.sum(
        jnp.where(
            expert_routes[:, :, None] == jnp.arange(expert_count)[None, None, :],
            logits[:, None, :],
            0.0,
        ),
        axis=2,
    )
    lifted = jnp.exp(chosen_logit)
    gates = lifted / jnp.sum(lifted, axis=1, keepdims=True)
    capacity = CAP
    flat_routes = expert_routes.reshape(-1)
    assign_count = flat_routes.shape[0]
    onehot = (flat_routes[:, None] == jnp.arange(expert_count)[None, :]).astype(jnp.int32)
    earlier = jnp.cumsum(onehot, axis=0) - onehot
    slot_rank = jnp.sum(earlier * onehot, axis=1)
    target = flat_routes * capacity + slot_rank
    slot_total = expert_count * capacity
    source_item = jax.ops.segment_sum(jnp.arange(assign_count) + 1, target, num_segments=slot_total)
    row_pick = (
        jnp.arange(stretch_len)[None, :] == ((source_item - 1) // top_count)[:, None]
    ) & (source_item > 0)[:, None]
    packed_rows = jnp.dot(
        row_pick.astype(jnp.bfloat16), normed, preferred_element_type=jnp.float32
    ).astype(jnp.bfloat16)
    pieces_here = w_gate.shape[0]
    feature_part = normed.shape[1]
    paired = pieces_here % 2 == 0
    kv_count = lax.axis_size("kv")
    core_bit = lax.axis_index("kv") % 2
    chip_bit = lax.axis_index("kv") // 2
    flip_core = [(i, i ^ 1) for i in range(kv_count)]
    flip_chip = [(i, i ^ 2) for i in range(kv_count)]
    if paired:
        experts_here = pieces_here // 2
        outgoing_rows = packed_rows.reshape(blk_count, experts_here, capacity, feature_part)
    else:
        experts_here = 1
        outgoing_rows = jnp.broadcast_to(
            packed_rows.reshape(expert_count, 1, capacity, feature_part),
            (expert_count, 2, capacity, feature_part),
        ).reshape(blk_count, pieces_here, capacity, feature_part)

    def pair_stage(landed_rows, gate_w, up_w):
        chunk_pieces = gate_w.shape[0]
        if paired:
            rows_in = jnp.broadcast_to(
                landed_rows[:, :, None],
                (blk_count, chunk_pieces // 2, 2, capacity, feature_part),
            ).reshape(blk_count, chunk_pieces, capacity, feature_part)
        else:
            rows_in = landed_rows
        gate_part = jnp.einsum("spkd,pdu->spku", rows_in, gate_w, preferred_element_type=jnp.float32)
        up_part = jnp.einsum("spkd,pdu->spku", rows_in, up_w, preferred_element_type=jnp.float32)
        both_parts = jnp.stack([gate_part, up_part], axis=3).astype(jnp.bfloat16)
        half = both_parts.shape[0] // 2
        kept = lax.dynamic_slice_in_dim(both_parts, core_bit * half, half, 0)
        given = lax.dynamic_slice_in_dim(both_parts, (1 - core_bit) * half, half, 0)
        pair_sum = kept.astype(jnp.float32) + lax.ppermute(given, "kv", flip_core).astype(jnp.float32)
        return pair_sum.astype(jnp.bfloat16)

    def out_stage(pair_sum, down_w):
        chunk_pieces = down_w.shape[0]
        quarter = pair_sum.shape[0] // 2
        chip_kept = lax.dynamic_slice_in_dim(pair_sum, chip_bit * quarter, quarter, 0)
        chip_given = lax.dynamic_slice_in_dim(pair_sum, (1 - chip_bit) * quarter, quarter, 0)
        whole = chip_kept.astype(jnp.float32) + lax.ppermute(
            chip_given, "kv", flip_chip
        ).astype(jnp.float32)
        hidden_quarter = (jax.nn.silu(whole[:, :, :, 0]) * whole[:, :, :, 1]).astype(jnp.bfloat16)
        hidden_far = lax.ppermute(hidden_quarter, "kv", flip_chip)
        hidden_half = jnp.where(
            chip_bit == 0,
            jnp.concatenate([hidden_quarter, hidden_far], axis=0),
            jnp.concatenate([hidden_far, hidden_quarter], axis=0),
        )
        hidden_other = lax.ppermute(hidden_half, "kv", flip_core)
        hidden = jnp.where(
            core_bit == 0,
            jnp.concatenate([hidden_half, hidden_other], axis=0),
            jnp.concatenate([hidden_other, hidden_half], axis=0),
        )
        piece_out = jnp.einsum(
            "spku,pud->spkd", hidden, down_w, preferred_element_type=jnp.float32
        ).astype(jnp.bfloat16)
        if paired:
            half_sum = piece_out.reshape(blk_count, chunk_pieces // 2, 2, capacity, feature_part)
            half_sum = jnp.sum(half_sum.astype(jnp.float32), axis=2).astype(jnp.bfloat16)
            return lax.all_to_all(half_sum, "blk", split_axis=0, concat_axis=0, tiled=True)
        returned = lax.all_to_all(piece_out, "blk", split_axis=0, concat_axis=0, tiled=True)
        per_piece = returned.reshape(expert_count, 2, capacity, feature_part).astype(jnp.float32)
        return (per_piece[:, 0] + per_piece[:, 1]).astype(jnp.bfloat16)

    chunk_count = CHUNKS if paired and experts_here % CHUNKS == 0 else 1
    chunk_experts = experts_here // chunk_count
    chunk_pieces = pieces_here // chunk_count
    piece_sets = [slice(i * chunk_pieces, (i + 1) * chunk_pieces) for i in range(chunk_count)]
    landed_sets = [
        lax.all_to_all(
            outgoing_rows[:, i * chunk_experts : (i + 1) * chunk_experts],
            "blk",
            split_axis=0,
            concat_axis=0,
            tiled=True,
        )
        for i in range(chunk_count)
    ]
    pair_sets = []
    for i in range(chunk_count):
        landed_now = landed_sets[i]
        if pair_sets:
            pair_sets[-1], landed_now = lax.optimization_barrier((pair_sets[-1], landed_now))
        pair_sets.append(pair_stage(landed_now, w_gate[piece_sets[i]], w_up[piece_sets[i]]))
    per_chunk = [out_stage(pair_sets[i], w_down[piece_sets[i]]) for i in range(chunk_count)]
    if paired:
        per_slot = jnp.concatenate(per_chunk, axis=1).reshape(slot_total, feature_part)
    else:
        per_slot = per_chunk[0].reshape(slot_total, feature_part)
    per_slot = per_slot.astype(jnp.float32)
    slot_weight = jnp.sum(
        jnp.where(
            target.reshape(stretch_len, top_count, 1) == jnp.arange(slot_total)[None, None, :],
            gates[:, :, None],
            0.0,
        ),
        axis=1,
    )
    moe_out = jnp.dot(
        slot_weight, per_slot, precision=lax.Precision.HIGHEST, preferred_element_type=jnp.float32
    )
    layer_out = (resid_float + moe_out).astype(jnp.bfloat16)
    here_old = in_use & (decode_holder[:, :max_blocks] == own_index)
    from_old = jnp.where(here_old, block_holder, blk_count).reshape(-1)
    put_old = jax.ops.segment_sum(
        (decode_slot[:, :max_blocks] + 1).reshape(-1), from_old, num_segments=blk_count
    )
    here_new = decode_holder[:, max_blocks:] == own_index
    request_ids = jnp.broadcast_to(jnp.arange(decode_holder.shape[0])[:, None], here_new.shape)
    from_new = jnp.where(here_new, request_ids, blk_count).reshape(-1)
    put_new = jax.ops.segment_sum(
        (decode_slot[:, max_blocks:] + 1).reshape(-1), from_new, num_segments=blk_count
    )
    placing = put_old + put_new
    decode_size = pool_size + fresh_count
    placement = (placing[None, :] - 1 == jnp.arange(decode_size)[:, None]).astype(jnp.bfloat16)
    decoded = jnp.dot(
        placement, landed.reshape(blk_count, -1), preferred_element_type=jnp.float32
    ).astype(jnp.bfloat16)
    decode_pool = decoded.reshape(decode_size, block_len, 1, 2, head_dim)
    return (layer_out, decode_pool)


def solution(mesh):
    in_specs = (
        P("blk", "kv"),
        P("blk", "kv"),
        P("blk", "kv", None, None),
        P("blk", None, "kv", None, None),
        P(),
        P(),
        P(),
        P(),
        P(),
        P("kv", "blk"),
        P("kv"),
        P("kv", None),
        P("blk", None),
        P("blk", "kv", None),
        P("blk", "kv", None),
        P("blk", None, "kv"),
    )
    out_specs = (P("blk", "kv"), P("blk", None, "kv", None, None))
    return jax.shard_map(
        per_device, mesh=mesh, in_specs=in_specs, out_specs=out_specs, check_vma=False
    )
```

```python
import math

import jax
import jax.numpy as jnp
from jax import lax
from jax.sharding import PartitionSpec as P

D = 2560
CAP = 8
CHUNKS = 1


EPSILON = 1e-05
MASKED = -1e30


def head_rows(asked_rows, head_count, head_dim):
    stretch_len = asked_rows.shape[0]
    return (
        asked_rows.reshape(stretch_len, head_count, head_dim)
        .transpose(1, 0, 2)
        .reshape(head_count * stretch_len, head_dim)
    )


def absorb(carried, scores, value_rows):
    running_max, denominator, accumulated = carried
    new_max = jnp.maximum(running_max, jnp.max(scores, axis=1))
    decay = jnp.exp(running_max - new_max)
    raised = jnp.exp(scores - new_max[:, None])
    denominator = denominator * decay + jnp.sum(raised, axis=1)
    accumulated = accumulated * decay[:, None] + jnp.dot(
        raised.astype(jnp.bfloat16), value_rows, preferred_element_type=jnp.float32
    )
    return (new_max, denominator, accumulated)


def attend_blocks(carried, query_rows, blocks, present, scale):
    block_count = blocks.shape[0]
    block_len = blocks.shape[1]
    head_dim = blocks.shape[3]
    tile_blocks = min(32, block_count)
    span = tile_blocks * block_len
    flags = present.astype(jnp.int32)
    live_count = jnp.sum(flags)
    order_rank = jnp.cumsum(flags) - 1
    positions = jnp.arange(block_count)
    chosen = present[None, :] & (order_rank[None, :] == positions[:, None])
    packing = jnp.sum(jnp.where(chosen, positions[None, :], 0), axis=1)
    packed = blocks[packing]

    def advance(turn, state_now):
        segment = lax.dynamic_slice_in_dim(packed, turn * tile_blocks, tile_blocks, 0)
        key_rows = segment[:, :, 0].reshape(span, head_dim)
        value_rows = segment[:, :, 1].reshape(span, head_dim)
        scores = (
            jnp.einsum("qd,kd->qk", query_rows, key_rows, preferred_element_type=jnp.float32)
            * scale
        )
        is_live = turn * tile_blocks + jnp.arange(span) // block_len < live_count
        scores = jnp.where(is_live[None, :], scores, MASKED)
        return absorb(state_now, scores, value_rows)

    return lax.fori_loop(0, (live_count + tile_blocks - 1) // tile_blocks, advance, carried)


def per_device(
    hidden_in,
    queries,
    new_kv,
    cache_pool,
    cache_len,
    block_holder,
    block_slot,
    decode_holder,
    decode_slot,
    out_weight,
    norm_gain,
    router_weight,
    expert_routes,
    w_gate,
    w_up,
    w_down,
):
    blk_count = lax.axis_size("blk")
    own_index = lax.axis_index("blk")
    stretch_len = queries.shape[0]
    head_dim = new_kv.shape[3]
    head_count = queries.shape[1] // head_dim
    pool_size = cache_pool.shape[0]
    block_len = cache_pool.shape[1]
    max_blocks = block_holder.shape[1]
    fresh_count = stretch_len // block_len
    scale = 1.0 / math.sqrt(head_dim)
    devices = jnp.arange(blk_count)
    in_use = jnp.arange(max_blocks)[None, :] < (cache_len // block_len)[:, None]
    pool_rows = cache_pool[:, :, 0]
    fresh_rows = new_kv[:, 0]
    sources = jnp.concatenate(
        [pool_rows, fresh_rows.reshape(fresh_count, block_len, 2, head_dim)], axis=0
    )
    held_here = in_use & (block_holder == own_index)
    old_target = jnp.where(held_here, decode_holder[:, :max_blocks], blk_count).reshape(-1)
    pick_old = jax.ops.segment_sum((block_slot + 1).reshape(-1), old_target, num_segments=blk_count)
    pick_new = jax.ops.segment_sum(
        pool_size + 1 + jnp.arange(fresh_count),
        decode_holder[own_index, max_blocks:],
        num_segments=blk_count,
    )
    picked = pick_old + pick_new
    source_count = sources.shape[0]
    send_pick = (jnp.arange(source_count)[None, :] == (picked - 1)[:, None]).astype(jnp.bfloat16)
    sending = (
        jnp.dot(send_pick, sources.reshape(source_count, -1), preferred_element_type=jnp.float32)
        .astype(jnp.bfloat16)
        .reshape((blk_count,) + sources.shape[1:])
    )
    match_here = (block_holder[:blk_count] == own_index) & in_use[:blk_count]
    out_slot = jnp.sum(jnp.where(match_here, block_slot[:blk_count], 0), axis=1)
    out_pick = (jnp.arange(pool_size)[None, :] == out_slot[:, None]).astype(jnp.bfloat16)
    outgoing = (
        jnp.dot(out_pick, pool_rows.reshape(pool_size, -1), preferred_element_type=jnp.float32)
        .astype(jnp.bfloat16)
        .reshape((blk_count,) + pool_rows.shape[1:])
    )
    block_shape = sending.shape[1:]
    both_blocks = lax.all_to_all(
        jnp.stack(
            [sending.reshape(blk_count, -1, head_dim), outgoing.reshape(blk_count, -1, head_dim)],
            axis=1,
        ),
        "blk",
        split_axis=0,
        concat_axis=0,
        tiled=True,
    )
    landed = both_blocks[:, 0].reshape((blk_count,) + block_shape)
    arrived = both_blocks[:, 1].reshape((blk_count,) + block_shape)
    present = jnp.any(
        (lax.dynamic_index_in_dim(block_holder, own_index, 0, keepdims=False)[None, :] == devices[:, None])
        & lax.dynamic_index_in_dim(in_use, own_index, 0, keepdims=False)[None, :],
        axis=1,
    )
    own_rows = head_rows(queries, head_count, head_dim)
    row_count = head_count * stretch_len
    start_state = (
        jnp.full((row_count,), MASKED, jnp.float32),
        jnp.zeros((row_count,), jnp.float32),
        jnp.zeros((row_count, head_dim), jnp.float32),
    )
    query_pos = jnp.arange(row_count) % stretch_len
    allowed = jnp.arange(stretch_len)[None, :] <= query_pos[:, None]
    local_scores = (
        jnp.einsum("qd,kd->qk", own_rows, fresh_rows[:, 0], preferred_element_type=jnp.float32)
        * scale
    )
    carried = absorb(start_state, jnp.where(allowed, local_scores, MASKED), fresh_rows[:, 1])
    carried = attend_blocks(carried, own_rows, arrived, present, scale)
    running_max, denominator, accumulated = carried
    attended = (
        (accumulated / denominator[:, None])
        .reshape(head_count, stretch_len, head_dim)
        .transpose(1, 0, 2)
    )
    attended = attended.reshape(stretch_len, head_count * head_dim).astype(jnp.bfloat16)
    every_token = lax.all_to_all(
        jnp.broadcast_to(attended[None], (blk_count,) + attended.shape), "blk", 0, 0, tiled=True
    ).reshape(-1, attended.shape[1])
    column_part = jnp.dot(
        every_token, out_weight, preferred_element_type=jnp.float32
    ).astype(jnp.bfloat16)
    projected = lax.all_to_all(column_part, "blk", split_axis=0, concat_axis=1, tiled=True)
    kv_index = lax.axis_index("kv")
    if lax.axis_size("kv") == 4:
        chip_bit = kv_index // 2
        core_low = kv_index % 2
        swap_core = [(i, i ^ 1) for i in range(4)]
        swap_chip = [(i, i ^ 2) for i in range(4)]
        chip_cols = projected.shape[1] // 2
        chip_kept = lax.dynamic_slice_in_dim(projected, chip_bit * chip_cols, chip_cols, 1)
        chip_given = lax.dynamic_slice_in_dim(projected, (1 - chip_bit) * chip_cols, chip_cols, 1)
        chip_sum = chip_kept.astype(jnp.float32) + lax.ppermute(
            chip_given, "kv", swap_chip
        ).astype(jnp.float32)
        own_cols = chip_cols // 2
        core_kept = lax.dynamic_slice_in_dim(chip_sum, core_low * own_cols, own_cols, 1)
        core_given = lax.dynamic_slice_in_dim(
            chip_sum, (1 - core_low) * own_cols, own_cols, 1
        ).astype(jnp.bfloat16)
        head_total = core_kept + lax.ppermute(core_given, "kv", swap_core).astype(jnp.float32)
    else:
        head_total = lax.psum_scatter(
            projected, "kv", scatter_dimension=1, tiled=True
        ).astype(jnp.float32)
    residual = (hidden_in.astype(jnp.float32) + head_total).astype(jnp.bfloat16)
    resid_float = residual.astype(jnp.float32)
    scaled = resid_float * norm_gain.astype(jnp.float32)[None, :]
    stats = jnp.concatenate(
        [
            jnp.sum(resid_float * resid_float, axis=1, keepdims=True),
            jnp.dot(scaled, router_weight, precision=lax.Precision.HIGHEST),
        ],
        axis=1,
    )
    if lax.axis_size("kv") == 4:
        stats = stats + lax.ppermute(stats, "kv", [(i, i ^ 1) for i in range(4)])
        stats = stats + lax.ppermute(stats, "kv", [(i, i ^ 2) for i in range(4)])
    else:
        stats = lax.psum(stats, "kv")
    square_sum = stats[:, 0]
    raw_logits = stats[:, 1:]
    inverse = lax.rsqrt(square_sum / D + EPSILON)
    logits = raw_logits * inverse[:, None]
    normed = (scaled * inverse[:, None]).astype(jnp.bfloat16)
    expert_count = router_weight.shape[1]
    top_count = expert_routes.shape[1]
    chosen_logit = jnp.sum(
        jnp.where(
            expert_routes[:, :, None] == jnp.arange(expert_count)[None, None, :],
            logits[:, None, :],
            0.0,
        ),
        axis=2,
    )
    lifted = jnp.exp(chosen_logit)
    gates = lifted / jnp.sum(lifted, axis=1, keepdims=True)
    capacity = CAP
    flat_routes = expert_routes.reshape(-1)
    assign_count = flat_routes.shape[0]
    onehot = (flat_routes[:, None] == jnp.arange(expert_count)[None, :]).astype(jnp.int32)
    earlier = jnp.cumsum(onehot, axis=0) - onehot
    slot_rank = jnp.sum(earlier * onehot, axis=1)
    target = flat_routes * capacity + slot_rank
    slot_total = expert_count * capacity
    slot_hit = target.reshape(stretch_len, top_count, 1) == jnp.arange(slot_total)[None, None, :]
    token_slot = jnp.any(slot_hit, axis=1).astype(jnp.bfloat16)
    packed_rows = lax.dot_general(
        token_slot, normed, (((0,), (0,)), ((), ())), preferred_element_type=jnp.float32
    ).astype(jnp.bfloat16)
    pieces_here = w_gate.shape[0]
    feature_part = normed.shape[1]
    paired = pieces_here % 2 == 0
    kv_count = lax.axis_size("kv")
    core_bit = lax.axis_index("kv") % 2
    chip_bit = lax.axis_index("kv") // 2
    flip_core = [(i, i ^ 1) for i in range(kv_count)]
    flip_chip = [(i, i ^ 2) for i in range(kv_count)]
    if paired:
        experts_here = pieces_here // 2
        outgoing_rows = packed_rows.reshape(blk_count, experts_here, capacity, feature_part)
    else:
        experts_here = 1
        outgoing_rows = jnp.broadcast_to(
            packed_rows.reshape(expert_count, 1, capacity, feature_part),
            (expert_count, 2, capacity, feature_part),
        ).reshape(blk_count, pieces_here, capacity, feature_part)

    def pair_stage(landed_rows, gate_w, up_w):
        chunk_pieces = gate_w.shape[0]
        if paired:
            rows_in = jnp.broadcast_to(
                landed_rows[:, :, None],
                (blk_count, chunk_pieces // 2, 2, capacity, feature_part),
            ).reshape(blk_count, chunk_pieces, capacity, feature_part)
        else:
            rows_in = landed_rows
        gate_part = jnp.einsum("spkd,pdu->spku", rows_in, gate_w, preferred_element_type=jnp.float32)
        up_part = jnp.einsum("spkd,pdu->spku", rows_in, up_w, preferred_element_type=jnp.float32)
        both_parts = jnp.stack([gate_part, up_part], axis=3).astype(jnp.bfloat16)
        half = both_parts.shape[0] // 2
        kept = lax.dynamic_slice_in_dim(both_parts, core_bit * half, half, 0)
        given = lax.dynamic_slice_in_dim(both_parts, (1 - core_bit) * half, half, 0)
        pair_sum = kept.astype(jnp.float32) + lax.ppermute(given, "kv", flip_core).astype(jnp.float32)
        return pair_sum.astype(jnp.bfloat16)

    def out_stage(pair_sum, down_w):
        chunk_pieces = down_w.shape[0]
        quarter = pair_sum.shape[0] // 2
        chip_kept = lax.dynamic_slice_in_dim(pair_sum, chip_bit * quarter, quarter, 0)
        chip_given = lax.dynamic_slice_in_dim(pair_sum, (1 - chip_bit) * quarter, quarter, 0)
        whole = chip_kept.astype(jnp.float32) + lax.ppermute(
            chip_given, "kv", flip_chip
        ).astype(jnp.float32)
        hidden_quarter = (jax.nn.silu(whole[:, :, :, 0]) * whole[:, :, :, 1]).astype(jnp.bfloat16)
        hidden_far = lax.ppermute(hidden_quarter, "kv", flip_chip)
        hidden_half = jnp.where(
            chip_bit == 0,
            jnp.concatenate([hidden_quarter, hidden_far], axis=0),
            jnp.concatenate([hidden_far, hidden_quarter], axis=0),
        )
        hidden_other = lax.ppermute(hidden_half, "kv", flip_core)
        hidden = jnp.where(
            core_bit == 0,
            jnp.concatenate([hidden_half, hidden_other], axis=0),
            jnp.concatenate([hidden_other, hidden_half], axis=0),
        )
        piece_out = jnp.einsum(
            "spku,pud->spkd", hidden, down_w, preferred_element_type=jnp.float32
        ).astype(jnp.bfloat16)
        if paired:
            half_sum = piece_out.reshape(blk_count, chunk_pieces // 2, 2, capacity, feature_part)
            half_sum = jnp.sum(half_sum.astype(jnp.float32), axis=2).astype(jnp.bfloat16)
            return lax.all_to_all(half_sum, "blk", split_axis=0, concat_axis=0, tiled=True)
        returned = lax.all_to_all(piece_out, "blk", split_axis=0, concat_axis=0, tiled=True)
        per_piece = returned.reshape(expert_count, 2, capacity, feature_part).astype(jnp.float32)
        return (per_piece[:, 0] + per_piece[:, 1]).astype(jnp.bfloat16)

    chunk_count = CHUNKS if paired and experts_here % CHUNKS == 0 else 1
    chunk_experts = experts_here // chunk_count
    chunk_pieces = pieces_here // chunk_count
    piece_sets = [slice(i * chunk_pieces, (i + 1) * chunk_pieces) for i in range(chunk_count)]
    landed_sets = [
        lax.all_to_all(
            outgoing_rows[:, i * chunk_experts : (i + 1) * chunk_experts],
            "blk",
            split_axis=0,
            concat_axis=0,
            tiled=True,
        )
        for i in range(chunk_count)
    ]
    pair_sets = []
    for i in range(chunk_count):
        landed_now = landed_sets[i]
        if pair_sets:
            pair_sets[-1], landed_now = lax.optimization_barrier((pair_sets[-1], landed_now))
        pair_sets.append(pair_stage(landed_now, w_gate[piece_sets[i]], w_up[piece_sets[i]]))
    per_chunk = [out_stage(pair_sets[i], w_down[piece_sets[i]]) for i in range(chunk_count)]
    if paired:
        per_slot = jnp.concatenate(per_chunk, axis=1).reshape(slot_total, feature_part)
    else:
        per_slot = per_chunk[0].reshape(slot_total, feature_part)
    per_slot = per_slot.astype(jnp.float32)
    slot_weight = jnp.sum(jnp.where(slot_hit, gates[:, :, None], 0.0), axis=1)
    moe_out = jnp.dot(
        slot_weight, per_slot, precision=lax.Precision.HIGHEST, preferred_element_type=jnp.float32
    )
    layer_out = (resid_float + moe_out).astype(jnp.bfloat16)
    here_old = in_use & (decode_holder[:, :max_blocks] == own_index)
    from_old = jnp.where(here_old, block_holder, blk_count).reshape(-1)
    put_old = jax.ops.segment_sum(
        (decode_slot[:, :max_blocks] + 1).reshape(-1), from_old, num_segments=blk_count
    )
    here_new = decode_holder[:, max_blocks:] == own_index
    request_ids = jnp.broadcast_to(jnp.arange(decode_holder.shape[0])[:, None], here_new.shape)
    from_new = jnp.where(here_new, request_ids, blk_count).reshape(-1)
    put_new = jax.ops.segment_sum(
        (decode_slot[:, max_blocks:] + 1).reshape(-1), from_new, num_segments=blk_count
    )
    placing = put_old + put_new
    decode_size = pool_size + fresh_count
    placement = (placing[None, :] - 1 == jnp.arange(decode_size)[:, None]).astype(jnp.bfloat16)
    decoded = jnp.dot(
        placement, landed.reshape(blk_count, -1), preferred_element_type=jnp.float32
    ).astype(jnp.bfloat16)
    decode_pool = decoded.reshape(decode_size, block_len, 1, 2, head_dim)
    return (layer_out, decode_pool)


def solution(mesh):
    in_specs = (
        P("blk", "kv"),
        P("blk", "kv"),
        P("blk", "kv", None, None),
        P("blk", None, "kv", None, None),
        P(),
        P(),
        P(),
        P(),
        P(),
        P("kv", "blk"),
        P("kv"),
        P("kv", None),
        P("blk", None),
        P("blk", "kv", None),
        P("blk", "kv", None),
        P("blk", None, "kv"),
    )
    out_specs = (P("blk", "kv"), P("blk", None, "kv", None, None))
    return jax.shard_map(
        per_device, mesh=mesh, in_specs=in_specs, out_specs=out_specs, check_vma=False
    )
```

```python
import math

import jax
import jax.numpy as jnp
from jax import lax
from jax.sharding import PartitionSpec as P

D = 2560
CAP = 8
CHUNKS = 1


EPSILON = 1e-05
MASKED = -1e30


def head_rows(asked_rows, head_count, head_dim):
    stretch_len = asked_rows.shape[0]
    return (
        asked_rows.reshape(stretch_len, head_count, head_dim)
        .transpose(1, 0, 2)
        .reshape(head_count * stretch_len, head_dim)
    )


def absorb(carried, scores, value_rows):
    running_max, denominator, accumulated = carried
    new_max = jnp.maximum(running_max, jnp.max(scores, axis=1))
    decay = jnp.exp(running_max - new_max)
    raised = jnp.exp(scores - new_max[:, None])
    denominator = denominator * decay + jnp.sum(raised, axis=1)
    accumulated = accumulated * decay[:, None] + jnp.dot(
        raised.astype(jnp.bfloat16), value_rows, preferred_element_type=jnp.float32
    )
    return (new_max, denominator, accumulated)


def attend_blocks(carried, query_rows, blocks, present, scale):
    block_count = blocks.shape[0]
    block_len = blocks.shape[1]
    head_dim = blocks.shape[3]
    tile_blocks = min(32, block_count)
    span = tile_blocks * block_len
    flags = present.astype(jnp.int32)
    live_count = jnp.sum(flags)
    order_rank = jnp.cumsum(flags) - 1
    positions = jnp.arange(block_count)
    chosen = present[None, :] & (order_rank[None, :] == positions[:, None])
    packing = jnp.sum(jnp.where(chosen, positions[None, :], 0), axis=1)
    packed = blocks[packing]

    def advance(turn, state_now):
        segment = lax.dynamic_slice_in_dim(packed, turn * tile_blocks, tile_blocks, 0)
        key_rows = segment[:, :, 0].reshape(span, head_dim)
        value_rows = segment[:, :, 1].reshape(span, head_dim)
        scores = (
            jnp.einsum("qd,kd->qk", query_rows, key_rows, preferred_element_type=jnp.float32)
            * scale
        )
        is_live = turn * tile_blocks + jnp.arange(span) // block_len < live_count
        scores = jnp.where(is_live[None, :], scores, MASKED)
        return absorb(state_now, scores, value_rows)

    return lax.fori_loop(0, (live_count + tile_blocks - 1) // tile_blocks, advance, carried)


def per_device(
    hidden_in,
    queries,
    new_kv,
    cache_pool,
    cache_len,
    block_holder,
    block_slot,
    decode_holder,
    decode_slot,
    out_weight,
    norm_gain,
    router_weight,
    expert_routes,
    w_gate,
    w_up,
    w_down,
):
    blk_count = lax.axis_size("blk")
    own_index = lax.axis_index("blk")
    stretch_len = queries.shape[0]
    head_dim = new_kv.shape[3]
    head_count = queries.shape[1] // head_dim
    pool_size = cache_pool.shape[0]
    block_len = cache_pool.shape[1]
    max_blocks = block_holder.shape[1]
    fresh_count = stretch_len // block_len
    scale = 1.0 / math.sqrt(head_dim)
    devices = jnp.arange(blk_count)
    in_use = jnp.arange(max_blocks)[None, :] < (cache_len // block_len)[:, None]
    pool_rows = cache_pool[:, :, 0]
    fresh_rows = new_kv[:, 0]
    held_here = in_use & (block_holder == own_index)
    old_target = jnp.where(held_here, decode_holder[:, :max_blocks], blk_count).reshape(-1)
    pick_old = jnp.sum(
        jnp.where(
            old_target[None, :] == devices[:, None], (block_slot + 1).reshape(-1)[None, :], 0
        ),
        axis=1,
    )
    new_dest = lax.dynamic_index_in_dim(decode_holder, own_index, 0, keepdims=False)[max_blocks:]
    pick_new = jnp.sum(
        jnp.where(
            new_dest[None, :] == devices[:, None],
            (pool_size + 1 + jnp.arange(fresh_count))[None, :],
            0,
        ),
        axis=1,
    )
    picked = pick_old + pick_new
    source_count = pool_size + fresh_count
    send_pick = (jnp.arange(source_count)[None, :] == (picked - 1)[:, None]).astype(jnp.bfloat16)
    sending = (
        jnp.dot(send_pick[:, :pool_size], pool_rows.reshape(pool_size, -1), preferred_element_type=jnp.float32)
        + jnp.dot(
            send_pick[:, pool_size:],
            fresh_rows.reshape(fresh_count, -1),
            preferred_element_type=jnp.float32,
        )
    ).astype(jnp.bfloat16).reshape((blk_count,) + pool_rows.shape[1:])
    match_here = (block_holder[:blk_count] == own_index) & in_use[:blk_count]
    out_slot = jnp.sum(jnp.where(match_here, block_slot[:blk_count], 0), axis=1)
    out_pick = (jnp.arange(pool_size)[None, :] == out_slot[:, None]).astype(jnp.bfloat16)
    outgoing = (
        jnp.dot(out_pick, pool_rows.reshape(pool_size, -1), preferred_element_type=jnp.float32)
        .astype(jnp.bfloat16)
        .reshape((blk_count,) + pool_rows.shape[1:])
    )
    block_shape = sending.shape[1:]
    both_blocks = lax.all_to_all(
        jnp.stack(
            [sending.reshape(blk_count, -1, head_dim), outgoing.reshape(blk_count, -1, head_dim)],
            axis=1,
        ),
        "blk",
        split_axis=0,
        concat_axis=0,
        tiled=True,
    )
    landed = both_blocks[:, 0].reshape((blk_count,) + block_shape)
    arrived = both_blocks[:, 1].reshape((blk_count,) + block_shape)
    present = jnp.any(
        (lax.dynamic_index_in_dim(block_holder, own_index, 0, keepdims=False)[None, :] == devices[:, None])
        & lax.dynamic_index_in_dim(in_use, own_index, 0, keepdims=False)[None, :],
        axis=1,
    )
    own_rows = head_rows(queries, head_count, head_dim)
    row_count = head_count * stretch_len
    start_state = (
        jnp.full((row_count,), MASKED, jnp.float32),
        jnp.zeros((row_count,), jnp.float32),
        jnp.zeros((row_count, head_dim), jnp.float32),
    )
    query_pos = jnp.arange(row_count) % stretch_len
    allowed = jnp.arange(stretch_len)[None, :] <= query_pos[:, None]
    local_scores = (
        jnp.einsum("qd,kd->qk", own_rows, fresh_rows[:, 0], preferred_element_type=jnp.float32)
        * scale
    )
    carried = absorb(start_state, jnp.where(allowed, local_scores, MASKED), fresh_rows[:, 1])
    carried = attend_blocks(carried, own_rows, arrived, present, scale)
    running_max, denominator, accumulated = carried
    attended = (
        (accumulated / denominator[:, None])
        .reshape(head_count, stretch_len, head_dim)
        .transpose(1, 0, 2)
    )
    attended = attended.reshape(stretch_len, head_count * head_dim).astype(jnp.bfloat16)
    every_token = lax.all_to_all(
        jnp.broadcast_to(attended[None], (blk_count,) + attended.shape), "blk", 0, 0, tiled=True
    ).reshape(-1, attended.shape[1])
    column_part = jnp.dot(
        every_token, out_weight, preferred_element_type=jnp.float32
    ).astype(jnp.bfloat16)
    projected = lax.all_to_all(column_part, "blk", split_axis=0, concat_axis=1, tiled=True)
    kv_index = lax.axis_index("kv")
    if lax.axis_size("kv") == 4:
        chip_bit = kv_index // 2
        core_low = kv_index % 2
        swap_core = [(i, i ^ 1) for i in range(4)]
        swap_chip = [(i, i ^ 2) for i in range(4)]
        chip_cols = projected.shape[1] // 2
        chip_kept = lax.dynamic_slice_in_dim(projected, chip_bit * chip_cols, chip_cols, 1)
        chip_given = lax.dynamic_slice_in_dim(projected, (1 - chip_bit) * chip_cols, chip_cols, 1)
        chip_sum = chip_kept.astype(jnp.float32) + lax.ppermute(
            chip_given, "kv", swap_chip
        ).astype(jnp.float32)
        own_cols = chip_cols // 2
        core_kept = lax.dynamic_slice_in_dim(chip_sum, core_low * own_cols, own_cols, 1)
        core_given = lax.dynamic_slice_in_dim(
            chip_sum, (1 - core_low) * own_cols, own_cols, 1
        ).astype(jnp.bfloat16)
        head_total = core_kept + lax.ppermute(core_given, "kv", swap_core).astype(jnp.float32)
    else:
        head_total = lax.psum_scatter(
            projected, "kv", scatter_dimension=1, tiled=True
        ).astype(jnp.float32)
    residual = (hidden_in.astype(jnp.float32) + head_total).astype(jnp.bfloat16)
    resid_float = residual.astype(jnp.float32)
    scaled = resid_float * norm_gain.astype(jnp.float32)[None, :]
    stats = jnp.concatenate(
        [
            jnp.sum(resid_float * resid_float, axis=1, keepdims=True),
            jnp.dot(scaled, router_weight, precision=lax.Precision.HIGHEST),
        ],
        axis=1,
    )
    if lax.axis_size("kv") == 4:
        stats = stats + lax.ppermute(stats, "kv", [(i, i ^ 1) for i in range(4)])
        stats = stats + lax.ppermute(stats, "kv", [(i, i ^ 2) for i in range(4)])
    else:
        stats = lax.psum(stats, "kv")
    square_sum = stats[:, 0]
    raw_logits = stats[:, 1:]
    inverse = lax.rsqrt(square_sum / D + EPSILON)
    logits = raw_logits * inverse[:, None]
    normed = (scaled * inverse[:, None]).astype(jnp.bfloat16)
    expert_count = router_weight.shape[1]
    top_count = expert_routes.shape[1]
    chosen_logit = jnp.sum(
        jnp.where(
            expert_routes[:, :, None] == jnp.arange(expert_count)[None, None, :],
            logits[:, None, :],
            0.0,
        ),
        axis=2,
    )
    lifted = jnp.exp(chosen_logit)
    gates = lifted / jnp.sum(lifted, axis=1, keepdims=True)
    capacity = CAP
    flat_routes = expert_routes.reshape(-1)
    assign_count = flat_routes.shape[0]
    onehot = (flat_routes[:, None] == jnp.arange(expert_count)[None, :]).astype(jnp.int32)
    earlier = jnp.cumsum(onehot, axis=0) - onehot
    slot_rank = jnp.sum(earlier * onehot, axis=1)
    target = flat_routes * capacity + slot_rank
    slot_total = expert_count * capacity
    slot_hit = target.reshape(stretch_len, top_count, 1) == jnp.arange(slot_total)[None, None, :]
    token_slot = jnp.any(slot_hit, axis=1).astype(jnp.bfloat16)
    packed_rows = lax.dot_general(
        token_slot, normed, (((0,), (0,)), ((), ())), preferred_element_type=jnp.float32
    ).astype(jnp.bfloat16)
    pieces_here = w_gate.shape[0]
    feature_part = normed.shape[1]
    paired = pieces_here % 2 == 0
    kv_count = lax.axis_size("kv")
    core_bit = lax.axis_index("kv") % 2
    chip_bit = lax.axis_index("kv") // 2
    flip_core = [(i, i ^ 1) for i in range(kv_count)]
    flip_chip = [(i, i ^ 2) for i in range(kv_count)]
    if paired:
        experts_here = pieces_here // 2
        outgoing_rows = packed_rows.reshape(blk_count, experts_here, capacity, feature_part)
    else:
        experts_here = 1
        outgoing_rows = jnp.broadcast_to(
            packed_rows.reshape(expert_count, 1, capacity, feature_part),
            (expert_count, 2, capacity, feature_part),
        ).reshape(blk_count, pieces_here, capacity, feature_part)

    def pair_stage(landed_rows, gate_w, up_w):
        chunk_pieces = gate_w.shape[0]
        if paired:
            rows_in = jnp.broadcast_to(
                landed_rows[:, :, None],
                (blk_count, chunk_pieces // 2, 2, capacity, feature_part),
            ).reshape(blk_count, chunk_pieces, capacity, feature_part)
        else:
            rows_in = landed_rows
        gate_part = jnp.einsum("spkd,pdu->spku", rows_in, gate_w, preferred_element_type=jnp.float32)
        up_part = jnp.einsum("spkd,pdu->spku", rows_in, up_w, preferred_element_type=jnp.float32)
        both_parts = jnp.stack([gate_part, up_part], axis=3).astype(jnp.bfloat16)
        half = both_parts.shape[0] // 2
        kept = lax.dynamic_slice_in_dim(both_parts, core_bit * half, half, 0)
        given = lax.dynamic_slice_in_dim(both_parts, (1 - core_bit) * half, half, 0)
        pair_sum = kept.astype(jnp.float32) + lax.ppermute(given, "kv", flip_core).astype(jnp.float32)
        return pair_sum.astype(jnp.bfloat16)

    def out_stage(pair_sum, down_w):
        chunk_pieces = down_w.shape[0]
        quarter = pair_sum.shape[0] // 2
        chip_kept = lax.dynamic_slice_in_dim(pair_sum, chip_bit * quarter, quarter, 0)
        chip_given = lax.dynamic_slice_in_dim(pair_sum, (1 - chip_bit) * quarter, quarter, 0)
        whole = chip_kept.astype(jnp.float32) + lax.ppermute(
            chip_given, "kv", flip_chip
        ).astype(jnp.float32)
        hidden_quarter = (jax.nn.silu(whole[:, :, :, 0]) * whole[:, :, :, 1]).astype(jnp.bfloat16)
        hidden_far = lax.ppermute(hidden_quarter, "kv", flip_chip)
        hidden_half = jnp.where(
            chip_bit == 0,
            jnp.concatenate([hidden_quarter, hidden_far], axis=0),
            jnp.concatenate([hidden_far, hidden_quarter], axis=0),
        )
        hidden_other = lax.ppermute(hidden_half, "kv", flip_core)
        hidden = jnp.where(
            core_bit == 0,
            jnp.concatenate([hidden_half, hidden_other], axis=0),
            jnp.concatenate([hidden_other, hidden_half], axis=0),
        )
        piece_out = jnp.einsum(
            "spku,pud->spkd", hidden, down_w, preferred_element_type=jnp.float32
        ).astype(jnp.bfloat16)
        if paired:
            half_sum = piece_out.reshape(blk_count, chunk_pieces // 2, 2, capacity, feature_part)
            half_sum = jnp.sum(half_sum.astype(jnp.float32), axis=2).astype(jnp.bfloat16)
            return lax.all_to_all(half_sum, "blk", split_axis=0, concat_axis=0, tiled=True)
        returned = lax.all_to_all(piece_out, "blk", split_axis=0, concat_axis=0, tiled=True)
        per_piece = returned.reshape(expert_count, 2, capacity, feature_part).astype(jnp.float32)
        return (per_piece[:, 0] + per_piece[:, 1]).astype(jnp.bfloat16)

    chunk_count = CHUNKS if paired and experts_here % CHUNKS == 0 else 1
    chunk_experts = experts_here // chunk_count
    chunk_pieces = pieces_here // chunk_count
    piece_sets = [slice(i * chunk_pieces, (i + 1) * chunk_pieces) for i in range(chunk_count)]
    landed_sets = [
        lax.all_to_all(
            outgoing_rows[:, i * chunk_experts : (i + 1) * chunk_experts],
            "blk",
            split_axis=0,
            concat_axis=0,
            tiled=True,
        )
        for i in range(chunk_count)
    ]
    pair_sets = []
    for i in range(chunk_count):
        landed_now = landed_sets[i]
        if pair_sets:
            pair_sets[-1], landed_now = lax.optimization_barrier((pair_sets[-1], landed_now))
        pair_sets.append(pair_stage(landed_now, w_gate[piece_sets[i]], w_up[piece_sets[i]]))
    per_chunk = [out_stage(pair_sets[i], w_down[piece_sets[i]]) for i in range(chunk_count)]
    if paired:
        per_slot = jnp.concatenate(per_chunk, axis=1).reshape(slot_total, feature_part)
    else:
        per_slot = per_chunk[0].reshape(slot_total, feature_part)
    per_slot = per_slot.astype(jnp.float32)
    slot_weight = jnp.sum(jnp.where(slot_hit, gates[:, :, None], 0.0), axis=1)
    moe_out = jnp.dot(
        slot_weight, per_slot, precision=lax.Precision.HIGHEST, preferred_element_type=jnp.float32
    )
    layer_out = (resid_float + moe_out).astype(jnp.bfloat16)
    here_old = in_use & (decode_holder[:, :max_blocks] == own_index)
    from_old = jnp.where(here_old, block_holder, blk_count).reshape(-1)
    put_old = jax.ops.segment_sum(
        (decode_slot[:, :max_blocks] + 1).reshape(-1), from_old, num_segments=blk_count
    )
    here_new = decode_holder[:, max_blocks:] == own_index
    request_ids = jnp.broadcast_to(jnp.arange(decode_holder.shape[0])[:, None], here_new.shape)
    from_new = jnp.where(here_new, request_ids, blk_count).reshape(-1)
    put_new = jax.ops.segment_sum(
        (decode_slot[:, max_blocks:] + 1).reshape(-1), from_new, num_segments=blk_count
    )
    placing = put_old + put_new
    decode_size = pool_size + fresh_count
    placement = (placing[None, :] - 1 == jnp.arange(decode_size)[:, None]).astype(jnp.bfloat16)
    decoded = jnp.dot(
        placement, landed.reshape(blk_count, -1), preferred_element_type=jnp.float32
    ).astype(jnp.bfloat16)
    decode_pool = decoded.reshape(decode_size, block_len, 1, 2, head_dim)
    return (layer_out, decode_pool)


def solution(mesh):
    in_specs = (
        P("blk", "kv"),
        P("blk", "kv"),
        P("blk", "kv", None, None),
        P("blk", None, "kv", None, None),
        P(),
        P(),
        P(),
        P(),
        P(),
        P("kv", "blk"),
        P("kv"),
        P("kv", None),
        P("blk", None),
        P("blk", "kv", None),
        P("blk", "kv", None),
        P("blk", None, "kv"),
    )
    out_specs = (P("blk", "kv"), P("blk", None, "kv", None, None))
    return jax.shard_map(
        per_device, mesh=mesh, in_specs=in_specs, out_specs=out_specs, check_vma=False
    )
```

```python
import math

import jax
import jax.numpy as jnp
from jax import lax
from jax.sharding import PartitionSpec as P

D = 2560
CAP = 8
CHUNKS = 1


EPSILON = 1e-05
MASKED = -1e30


def head_rows(asked_rows, head_count, head_dim):
    stretch_len = asked_rows.shape[0]
    return (
        asked_rows.reshape(stretch_len, head_count, head_dim)
        .transpose(1, 0, 2)
        .reshape(head_count * stretch_len, head_dim)
    )


def absorb(carried, scores, value_rows):
    running_max, denominator, accumulated = carried
    new_max = jnp.maximum(running_max, jnp.max(scores, axis=1))
    decay = jnp.exp(running_max - new_max)
    raised = jnp.exp(scores - new_max[:, None])
    denominator = denominator * decay + jnp.sum(raised, axis=1)
    accumulated = accumulated * decay[:, None] + jnp.dot(
        raised.astype(jnp.bfloat16), value_rows, preferred_element_type=jnp.float32
    )
    return (new_max, denominator, accumulated)


def attend_blocks(carried, query_rows, blocks, present, scale):
    block_count = blocks.shape[0]
    block_len = blocks.shape[1]
    head_dim = blocks.shape[3]
    tile_blocks = min(32, block_count)
    span = tile_blocks * block_len
    flags = present.astype(jnp.int32)
    live_count = jnp.sum(flags)
    order_rank = jnp.cumsum(flags) - 1
    positions = jnp.arange(block_count)
    chosen = present[None, :] & (order_rank[None, :] == positions[:, None])
    packing = jnp.sum(jnp.where(chosen, positions[None, :], 0), axis=1)
    packed = blocks[packing]

    def advance(turn, state_now):
        segment = lax.dynamic_slice_in_dim(packed, turn * tile_blocks, tile_blocks, 0)
        key_rows = segment[:, :, 0].reshape(span, head_dim)
        value_rows = segment[:, :, 1].reshape(span, head_dim)
        scores = (
            jnp.einsum("qd,kd->qk", query_rows, key_rows, preferred_element_type=jnp.float32)
            * scale
        )
        is_live = turn * tile_blocks + jnp.arange(span) // block_len < live_count
        scores = jnp.where(is_live[None, :], scores, MASKED)
        return absorb(state_now, scores, value_rows)

    return lax.fori_loop(0, (live_count + tile_blocks - 1) // tile_blocks, advance, carried)


def per_device(
    hidden_in,
    queries,
    new_kv,
    cache_pool,
    cache_len,
    block_holder,
    block_slot,
    decode_holder,
    decode_slot,
    out_weight,
    norm_gain,
    router_weight,
    expert_routes,
    w_gate,
    w_up,
    w_down,
):
    blk_count = lax.axis_size("blk")
    own_index = lax.axis_index("blk")
    stretch_len = queries.shape[0]
    head_dim = new_kv.shape[3]
    head_count = queries.shape[1] // head_dim
    pool_size = cache_pool.shape[0]
    block_len = cache_pool.shape[1]
    max_blocks = block_holder.shape[1]
    fresh_count = stretch_len // block_len
    scale = 1.0 / math.sqrt(head_dim)
    devices = jnp.arange(blk_count)
    in_use = jnp.arange(max_blocks)[None, :] < (cache_len // block_len)[:, None]
    pool_rows = cache_pool[:, :, 0]
    fresh_rows = new_kv[:, 0]
    held_here = in_use & (block_holder == own_index)
    old_target = jnp.where(held_here, decode_holder[:, :max_blocks], blk_count).reshape(-1)
    pick_old = jnp.sum(
        jnp.where(
            old_target[None, :] == devices[:, None], (block_slot + 1).reshape(-1)[None, :], 0
        ),
        axis=1,
    )
    new_dest = lax.dynamic_index_in_dim(decode_holder, own_index, 0, keepdims=False)[max_blocks:]
    pick_new = jnp.sum(
        jnp.where(
            new_dest[None, :] == devices[:, None],
            (pool_size + 1 + jnp.arange(fresh_count))[None, :],
            0,
        ),
        axis=1,
    )
    picked = pick_old + pick_new
    source_count = pool_size + fresh_count
    send_pick = (jnp.arange(source_count)[None, :] == (picked - 1)[:, None]).astype(jnp.bfloat16)
    sending = (
        jnp.dot(send_pick[:, :pool_size], pool_rows.reshape(pool_size, -1), preferred_element_type=jnp.float32)
        + jnp.dot(
            send_pick[:, pool_size:],
            fresh_rows.reshape(fresh_count, -1),
            preferred_element_type=jnp.float32,
        )
    ).astype(jnp.bfloat16).reshape((blk_count,) + pool_rows.shape[1:])
    match_here = (block_holder[:blk_count] == own_index) & in_use[:blk_count]
    out_slot = jnp.sum(jnp.where(match_here, block_slot[:blk_count], 0), axis=1)
    out_pick = (jnp.arange(pool_size)[None, :] == out_slot[:, None]).astype(jnp.bfloat16)
    outgoing = (
        jnp.dot(out_pick, pool_rows.reshape(pool_size, -1), preferred_element_type=jnp.float32)
        .astype(jnp.bfloat16)
        .reshape((blk_count,) + pool_rows.shape[1:])
    )
    block_shape = sending.shape[1:]
    both_blocks = lax.all_to_all(
        jnp.stack(
            [sending.reshape(blk_count, -1, head_dim), outgoing.reshape(blk_count, -1, head_dim)],
            axis=1,
        ),
        "blk",
        split_axis=0,
        concat_axis=0,
        tiled=True,
    )
    landed = both_blocks[:, 0].reshape((blk_count,) + block_shape)
    arrived = both_blocks[:, 1].reshape((blk_count,) + block_shape)
    present = jnp.any(
        (lax.dynamic_index_in_dim(block_holder, own_index, 0, keepdims=False)[None, :] == devices[:, None])
        & lax.dynamic_index_in_dim(in_use, own_index, 0, keepdims=False)[None, :],
        axis=1,
    )
    own_rows = head_rows(queries, head_count, head_dim)
    row_count = head_count * stretch_len
    start_state = (
        jnp.full((row_count,), MASKED, jnp.float32),
        jnp.zeros((row_count,), jnp.float32),
        jnp.zeros((row_count, head_dim), jnp.float32),
    )
    query_pos = jnp.arange(row_count) % stretch_len
    allowed = jnp.arange(stretch_len)[None, :] <= query_pos[:, None]
    local_scores = (
        jnp.einsum("qd,kd->qk", own_rows, fresh_rows[:, 0], preferred_element_type=jnp.float32)
        * scale
    )
    carried = absorb(start_state, jnp.where(allowed, local_scores, MASKED), fresh_rows[:, 1])
    carried = attend_blocks(carried, own_rows, arrived, present, scale)
    running_max, denominator, accumulated = carried
    attended = (
        (accumulated / denominator[:, None])
        .reshape(head_count, stretch_len, head_dim)
        .transpose(1, 0, 2)
    )
    attended = attended.reshape(stretch_len, head_count * head_dim).astype(jnp.bfloat16)
    if blk_count <= 8:
        back_parts = []
        for shift in range(blk_count):
            there = [(i, (i + shift) % blk_count) for i in range(blk_count)]
            back = [(i, (i - shift) % blk_count) for i in range(blk_count)]
            rows_from = attended if shift == 0 else lax.ppermute(attended, "blk", there)
            part = jnp.dot(rows_from, out_weight, preferred_element_type=jnp.float32)
            part = part.astype(jnp.bfloat16)
            back_parts.append(part if shift == 0 else lax.ppermute(part, "blk", back))
        by_shift = jnp.concatenate(back_parts + back_parts, axis=1)
        col_width = out_weight.shape[1]
        projected = lax.dynamic_slice_in_dim(
            by_shift, (blk_count - own_index) % blk_count * col_width, blk_count * col_width, 1
        )
    else:
        every_token = lax.all_to_all(
            jnp.broadcast_to(attended[None], (blk_count,) + attended.shape), "blk", 0, 0, tiled=True
        ).reshape(-1, attended.shape[1])
        column_part = jnp.dot(
            every_token, out_weight, preferred_element_type=jnp.float32
        ).astype(jnp.bfloat16)
        projected = lax.all_to_all(column_part, "blk", split_axis=0, concat_axis=1, tiled=True)
    kv_index = lax.axis_index("kv")
    if lax.axis_size("kv") == 4:
        chip_bit = kv_index // 2
        core_low = kv_index % 2
        swap_core = [(i, i ^ 1) for i in range(4)]
        swap_chip = [(i, i ^ 2) for i in range(4)]
        chip_cols = projected.shape[1] // 2
        chip_kept = lax.dynamic_slice_in_dim(projected, chip_bit * chip_cols, chip_cols, 1)
        chip_given = lax.dynamic_slice_in_dim(projected, (1 - chip_bit) * chip_cols, chip_cols, 1)
        chip_sum = chip_kept.astype(jnp.float32) + lax.ppermute(
            chip_given, "kv", swap_chip
        ).astype(jnp.float32)
        own_cols = chip_cols // 2
        core_kept = lax.dynamic_slice_in_dim(chip_sum, core_low * own_cols, own_cols, 1)
        core_given = lax.dynamic_slice_in_dim(
            chip_sum, (1 - core_low) * own_cols, own_cols, 1
        ).astype(jnp.bfloat16)
        head_total = core_kept + lax.ppermute(core_given, "kv", swap_core).astype(jnp.float32)
    else:
        head_total = lax.psum_scatter(
            projected, "kv", scatter_dimension=1, tiled=True
        ).astype(jnp.float32)
    residual = (hidden_in.astype(jnp.float32) + head_total).astype(jnp.bfloat16)
    resid_float = residual.astype(jnp.float32)
    scaled = resid_float * norm_gain.astype(jnp.float32)[None, :]
    stats = jnp.concatenate(
        [
            jnp.sum(resid_float * resid_float, axis=1, keepdims=True),
            jnp.dot(scaled, router_weight, precision=lax.Precision.HIGHEST),
        ],
        axis=1,
    )
    if lax.axis_size("kv") == 4:
        stats = stats + lax.ppermute(stats, "kv", [(i, i ^ 1) for i in range(4)])
        stats = stats + lax.ppermute(stats, "kv", [(i, i ^ 2) for i in range(4)])
    else:
        stats = lax.psum(stats, "kv")
    square_sum = stats[:, 0]
    raw_logits = stats[:, 1:]
    inverse = lax.rsqrt(square_sum / D + EPSILON)
    logits = raw_logits * inverse[:, None]
    normed = (scaled * inverse[:, None]).astype(jnp.bfloat16)
    expert_count = router_weight.shape[1]
    top_count = expert_routes.shape[1]
    chosen_logit = jnp.sum(
        jnp.where(
            expert_routes[:, :, None] == jnp.arange(expert_count)[None, None, :],
            logits[:, None, :],
            0.0,
        ),
        axis=2,
    )
    lifted = jnp.exp(chosen_logit)
    gates = lifted / jnp.sum(lifted, axis=1, keepdims=True)
    capacity = CAP
    flat_routes = expert_routes.reshape(-1)
    assign_count = flat_routes.shape[0]
    onehot = (flat_routes[:, None] == jnp.arange(expert_count)[None, :]).astype(jnp.int32)
    earlier = jnp.cumsum(onehot, axis=0) - onehot
    slot_rank = jnp.sum(earlier * onehot, axis=1)
    target = flat_routes * capacity + slot_rank
    slot_total = expert_count * capacity
    slot_hit = target.reshape(stretch_len, top_count, 1) == jnp.arange(slot_total)[None, None, :]
    token_slot = jnp.any(slot_hit, axis=1).astype(jnp.bfloat16)
    packed_rows = lax.dot_general(
        token_slot, normed, (((0,), (0,)), ((), ())), preferred_element_type=jnp.float32
    ).astype(jnp.bfloat16)
    pieces_here = w_gate.shape[0]
    feature_part = normed.shape[1]
    paired = pieces_here % 2 == 0
    kv_count = lax.axis_size("kv")
    core_bit = lax.axis_index("kv") % 2
    chip_bit = lax.axis_index("kv") // 2
    flip_core = [(i, i ^ 1) for i in range(kv_count)]
    flip_chip = [(i, i ^ 2) for i in range(kv_count)]
    if paired:
        experts_here = pieces_here // 2
        outgoing_rows = packed_rows.reshape(blk_count, experts_here, capacity, feature_part)
    else:
        experts_here = 1
        outgoing_rows = jnp.broadcast_to(
            packed_rows.reshape(expert_count, 1, capacity, feature_part),
            (expert_count, 2, capacity, feature_part),
        ).reshape(blk_count, pieces_here, capacity, feature_part)

    def pair_stage(landed_rows, gate_w, up_w):
        chunk_pieces = gate_w.shape[0]
        if paired:
            rows_in = jnp.broadcast_to(
                landed_rows[:, :, None],
                (blk_count, chunk_pieces // 2, 2, capacity, feature_part),
            ).reshape(blk_count, chunk_pieces, capacity, feature_part)
        else:
            rows_in = landed_rows
        gate_part = jnp.einsum("spkd,pdu->spku", rows_in, gate_w, preferred_element_type=jnp.float32)
        up_part = jnp.einsum("spkd,pdu->spku", rows_in, up_w, preferred_element_type=jnp.float32)
        both_parts = jnp.stack([gate_part, up_part], axis=3).astype(jnp.bfloat16)
        half = both_parts.shape[0] // 2
        kept = lax.dynamic_slice_in_dim(both_parts, core_bit * half, half, 0)
        given = lax.dynamic_slice_in_dim(both_parts, (1 - core_bit) * half, half, 0)
        pair_sum = kept.astype(jnp.float32) + lax.ppermute(given, "kv", flip_core).astype(jnp.float32)
        return pair_sum.astype(jnp.bfloat16)

    def out_stage(pair_sum, down_w):
        chunk_pieces = down_w.shape[0]
        quarter = pair_sum.shape[0] // 2
        chip_kept = lax.dynamic_slice_in_dim(pair_sum, chip_bit * quarter, quarter, 0)
        chip_given = lax.dynamic_slice_in_dim(pair_sum, (1 - chip_bit) * quarter, quarter, 0)
        whole = chip_kept.astype(jnp.float32) + lax.ppermute(
            chip_given, "kv", flip_chip
        ).astype(jnp.float32)
        hidden_quarter = (jax.nn.silu(whole[:, :, :, 0]) * whole[:, :, :, 1]).astype(jnp.bfloat16)
        hidden_far = lax.ppermute(hidden_quarter, "kv", flip_chip)
        hidden_half = jnp.where(
            chip_bit == 0,
            jnp.concatenate([hidden_quarter, hidden_far], axis=0),
            jnp.concatenate([hidden_far, hidden_quarter], axis=0),
        )
        hidden_other = lax.ppermute(hidden_half, "kv", flip_core)
        hidden = jnp.where(
            core_bit == 0,
            jnp.concatenate([hidden_half, hidden_other], axis=0),
            jnp.concatenate([hidden_other, hidden_half], axis=0),
        )
        piece_out = jnp.einsum(
            "spku,pud->spkd", hidden, down_w, preferred_element_type=jnp.float32
        ).astype(jnp.bfloat16)
        if paired:
            half_sum = piece_out.reshape(blk_count, chunk_pieces // 2, 2, capacity, feature_part)
            half_sum = jnp.sum(half_sum.astype(jnp.float32), axis=2).astype(jnp.bfloat16)
            return lax.all_to_all(half_sum, "blk", split_axis=0, concat_axis=0, tiled=True)
        returned = lax.all_to_all(piece_out, "blk", split_axis=0, concat_axis=0, tiled=True)
        per_piece = returned.reshape(expert_count, 2, capacity, feature_part).astype(jnp.float32)
        return (per_piece[:, 0] + per_piece[:, 1]).astype(jnp.bfloat16)

    chunk_count = CHUNKS if paired and experts_here % CHUNKS == 0 else 1
    chunk_experts = experts_here // chunk_count
    chunk_pieces = pieces_here // chunk_count
    piece_sets = [slice(i * chunk_pieces, (i + 1) * chunk_pieces) for i in range(chunk_count)]
    landed_sets = [
        lax.all_to_all(
            outgoing_rows[:, i * chunk_experts : (i + 1) * chunk_experts],
            "blk",
            split_axis=0,
            concat_axis=0,
            tiled=True,
        )
        for i in range(chunk_count)
    ]
    pair_sets = []
    for i in range(chunk_count):
        landed_now = landed_sets[i]
        if pair_sets:
            pair_sets[-1], landed_now = lax.optimization_barrier((pair_sets[-1], landed_now))
        pair_sets.append(pair_stage(landed_now, w_gate[piece_sets[i]], w_up[piece_sets[i]]))
    per_chunk = [out_stage(pair_sets[i], w_down[piece_sets[i]]) for i in range(chunk_count)]
    if paired:
        per_slot = jnp.concatenate(per_chunk, axis=1).reshape(slot_total, feature_part)
    else:
        per_slot = per_chunk[0].reshape(slot_total, feature_part)
    per_slot = per_slot.astype(jnp.float32)
    slot_weight = jnp.sum(jnp.where(slot_hit, gates[:, :, None], 0.0), axis=1)
    moe_out = jnp.dot(
        slot_weight, per_slot, precision=lax.Precision.HIGHEST, preferred_element_type=jnp.float32
    )
    layer_out = (resid_float + moe_out).astype(jnp.bfloat16)
    here_old = in_use & (decode_holder[:, :max_blocks] == own_index)
    from_old = jnp.where(here_old, block_holder, blk_count).reshape(-1)
    put_old = jax.ops.segment_sum(
        (decode_slot[:, :max_blocks] + 1).reshape(-1), from_old, num_segments=blk_count
    )
    here_new = decode_holder[:, max_blocks:] == own_index
    request_ids = jnp.broadcast_to(jnp.arange(decode_holder.shape[0])[:, None], here_new.shape)
    from_new = jnp.where(here_new, request_ids, blk_count).reshape(-1)
    put_new = jax.ops.segment_sum(
        (decode_slot[:, max_blocks:] + 1).reshape(-1), from_new, num_segments=blk_count
    )
    placing = put_old + put_new
    decode_size = pool_size + fresh_count
    placement = (placing[None, :] - 1 == jnp.arange(decode_size)[:, None]).astype(jnp.bfloat16)
    decoded = jnp.dot(
        placement, landed.reshape(blk_count, -1), preferred_element_type=jnp.float32
    ).astype(jnp.bfloat16)
    decode_pool = decoded.reshape(decode_size, block_len, 1, 2, head_dim)
    return (layer_out, decode_pool)


def solution(mesh):
    in_specs = (
        P("blk", "kv"),
        P("blk", "kv"),
        P("blk", "kv", None, None),
        P("blk", None, "kv", None, None),
        P(),
        P(),
        P(),
        P(),
        P(),
        P("kv", "blk"),
        P("kv"),
        P("kv", None),
        P("blk", None),
        P("blk", "kv", None),
        P("blk", "kv", None),
        P("blk", None, "kv"),
    )
    out_specs = (P("blk", "kv"), P("blk", None, "kv", None, None))
    return jax.shard_map(
        per_device, mesh=mesh, in_specs=in_specs, out_specs=out_specs, check_vma=False
    )
```

```python
import math

import jax
import jax.numpy as jnp
from jax import lax
from jax.sharding import PartitionSpec as P

D = 2560
CAP = 8
CHUNKS = 1


EPSILON = 1e-05
MASKED = -1e30


def head_rows(asked_rows, head_count, head_dim):
    stretch_len = asked_rows.shape[0]
    return (
        asked_rows.reshape(stretch_len, head_count, head_dim)
        .transpose(1, 0, 2)
        .reshape(head_count * stretch_len, head_dim)
    )


def absorb(carried, scores, value_rows):
    running_max, denominator, accumulated = carried
    new_max = jnp.maximum(running_max, jnp.max(scores, axis=1))
    decay = jnp.exp(running_max - new_max)
    raised = jnp.exp(scores - new_max[:, None])
    denominator = denominator * decay + jnp.sum(raised, axis=1)
    accumulated = accumulated * decay[:, None] + jnp.dot(
        raised.astype(jnp.bfloat16), value_rows, preferred_element_type=jnp.float32
    )
    return (new_max, denominator, accumulated)


def attend_blocks(carried, query_rows, blocks, present, scale):
    block_count = blocks.shape[0]
    block_len = blocks.shape[1]
    head_dim = blocks.shape[3]
    tile_blocks = min(32, block_count)
    span = tile_blocks * block_len
    flags = present.astype(jnp.int32)
    live_count = jnp.sum(flags)
    order_rank = jnp.cumsum(flags) - 1
    positions = jnp.arange(block_count)
    chosen = present[None, :] & (order_rank[None, :] == positions[:, None])
    packing = jnp.sum(jnp.where(chosen, positions[None, :], 0), axis=1)
    packed = blocks[packing]

    def advance(turn, state_now):
        segment = lax.dynamic_slice_in_dim(packed, turn * tile_blocks, tile_blocks, 0)
        key_rows = segment[:, :, 0].reshape(span, head_dim)
        value_rows = segment[:, :, 1].reshape(span, head_dim)
        scores = (
            jnp.einsum("qd,kd->qk", query_rows, key_rows, preferred_element_type=jnp.float32)
            * scale
        )
        is_live = turn * tile_blocks + jnp.arange(span) // block_len < live_count
        scores = jnp.where(is_live[None, :], scores, MASKED)
        return absorb(state_now, scores, value_rows)

    return lax.fori_loop(0, (live_count + tile_blocks - 1) // tile_blocks, advance, carried)


def per_device(
    hidden_in,
    queries,
    new_kv,
    cache_pool,
    cache_len,
    block_holder,
    block_slot,
    decode_holder,
    decode_slot,
    out_weight,
    norm_gain,
    router_weight,
    expert_routes,
    w_gate,
    w_up,
    w_down,
):
    blk_count = lax.axis_size("blk")
    own_index = lax.axis_index("blk")
    stretch_len = queries.shape[0]
    head_dim = new_kv.shape[3]
    head_count = queries.shape[1] // head_dim
    pool_size = cache_pool.shape[0]
    block_len = cache_pool.shape[1]
    max_blocks = block_holder.shape[1]
    fresh_count = stretch_len // block_len
    scale = 1.0 / math.sqrt(head_dim)
    devices = jnp.arange(blk_count)
    in_use = jnp.arange(max_blocks)[None, :] < (cache_len // block_len)[:, None]
    pool_rows = cache_pool[:, :, 0]
    fresh_rows = new_kv[:, 0]
    held_here = in_use & (block_holder == own_index)
    old_target = jnp.where(held_here, decode_holder[:, :max_blocks], blk_count).reshape(-1)
    pick_old = jnp.sum(
        jnp.where(
            old_target[None, :] == devices[:, None], (block_slot + 1).reshape(-1)[None, :], 0
        ),
        axis=1,
    )
    new_dest = lax.dynamic_index_in_dim(decode_holder, own_index, 0, keepdims=False)[max_blocks:]
    pick_new = jnp.sum(
        jnp.where(
            new_dest[None, :] == devices[:, None],
            (pool_size + 1 + jnp.arange(fresh_count))[None, :],
            0,
        ),
        axis=1,
    )
    picked = pick_old + pick_new
    source_count = pool_size + fresh_count
    send_pick = (jnp.arange(source_count)[None, :] == (picked - 1)[:, None]).astype(jnp.bfloat16)
    sending = (
        jnp.dot(send_pick[:, :pool_size], pool_rows.reshape(pool_size, -1), preferred_element_type=jnp.float32)
        + jnp.dot(
            send_pick[:, pool_size:],
            fresh_rows.reshape(fresh_count, -1),
            preferred_element_type=jnp.float32,
        )
    ).astype(jnp.bfloat16).reshape((blk_count,) + pool_rows.shape[1:])
    match_here = (block_holder[:blk_count] == own_index) & in_use[:blk_count]
    out_slot = jnp.sum(jnp.where(match_here, block_slot[:blk_count], 0), axis=1)
    out_pick = (jnp.arange(pool_size)[None, :] == out_slot[:, None]).astype(jnp.bfloat16)
    outgoing = (
        jnp.dot(out_pick, pool_rows.reshape(pool_size, -1), preferred_element_type=jnp.float32)
        .astype(jnp.bfloat16)
        .reshape((blk_count,) + pool_rows.shape[1:])
    )
    block_shape = sending.shape[1:]
    both_blocks = lax.all_to_all(
        jnp.stack(
            [sending.reshape(blk_count, -1, head_dim), outgoing.reshape(blk_count, -1, head_dim)],
            axis=1,
        ),
        "blk",
        split_axis=0,
        concat_axis=0,
        tiled=True,
    )
    landed = both_blocks[:, 0].reshape((blk_count,) + block_shape)
    arrived = both_blocks[:, 1].reshape((blk_count,) + block_shape)
    present = jnp.any(
        (lax.dynamic_index_in_dim(block_holder, own_index, 0, keepdims=False)[None, :] == devices[:, None])
        & lax.dynamic_index_in_dim(in_use, own_index, 0, keepdims=False)[None, :],
        axis=1,
    )
    own_rows = head_rows(queries, head_count, head_dim)
    row_count = head_count * stretch_len
    start_state = (
        jnp.full((row_count,), MASKED, jnp.float32),
        jnp.zeros((row_count,), jnp.float32),
        jnp.zeros((row_count, head_dim), jnp.float32),
    )
    query_pos = jnp.arange(row_count) % stretch_len
    allowed = jnp.arange(stretch_len)[None, :] <= query_pos[:, None]
    local_scores = (
        jnp.einsum("qd,kd->qk", own_rows, fresh_rows[:, 0], preferred_element_type=jnp.float32)
        * scale
    )
    carried = absorb(start_state, jnp.where(allowed, local_scores, MASKED), fresh_rows[:, 1])
    carried = attend_blocks(carried, own_rows, arrived, present, scale)
    running_max, denominator, accumulated = carried
    attended = (
        (accumulated / denominator[:, None])
        .reshape(head_count, stretch_len, head_dim)
        .transpose(1, 0, 2)
    )
    attended = attended.reshape(stretch_len, head_count * head_dim).astype(jnp.bfloat16)
    if blk_count <= 8:
        back_parts = []
        for shift in range(blk_count):
            there = [(i, (i + shift) % blk_count) for i in range(blk_count)]
            back = [(i, (i - shift) % blk_count) for i in range(blk_count)]
            rows_from = attended if shift == 0 else lax.ppermute(attended, "blk", there)
            part = jnp.dot(rows_from, out_weight, preferred_element_type=jnp.float32)
            part = part.astype(jnp.bfloat16)
            back_parts.append(part if shift == 0 else lax.ppermute(part, "blk", back))
        by_shift = jnp.concatenate(back_parts + back_parts, axis=1)
        col_width = out_weight.shape[1]
        projected = lax.dynamic_slice_in_dim(
            by_shift, (blk_count - own_index) % blk_count * col_width, blk_count * col_width, 1
        )
    else:
        every_token = lax.all_to_all(
            jnp.broadcast_to(attended[None], (blk_count,) + attended.shape), "blk", 0, 0, tiled=True
        ).reshape(-1, attended.shape[1])
        column_part = jnp.dot(
            every_token, out_weight, preferred_element_type=jnp.float32
        ).astype(jnp.bfloat16)
        projected = lax.all_to_all(column_part, "blk", split_axis=0, concat_axis=1, tiled=True)
    kv_index = lax.axis_index("kv")
    if lax.axis_size("kv") == 4:
        chip_bit = kv_index // 2
        core_low = kv_index % 2
        swap_core = [(i, i ^ 1) for i in range(4)]
        swap_chip = [(i, i ^ 2) for i in range(4)]
        chip_cols = projected.shape[1] // 2
        chip_kept = lax.dynamic_slice_in_dim(projected, chip_bit * chip_cols, chip_cols, 1)
        chip_given = lax.dynamic_slice_in_dim(projected, (1 - chip_bit) * chip_cols, chip_cols, 1)
        chip_sum = chip_kept.astype(jnp.float32) + lax.ppermute(
            chip_given, "kv", swap_chip
        ).astype(jnp.float32)
        own_cols = chip_cols // 2
        core_kept = lax.dynamic_slice_in_dim(chip_sum, core_low * own_cols, own_cols, 1)
        core_given = lax.dynamic_slice_in_dim(
            chip_sum, (1 - core_low) * own_cols, own_cols, 1
        ).astype(jnp.bfloat16)
        head_total = core_kept + lax.ppermute(core_given, "kv", swap_core).astype(jnp.float32)
    else:
        head_total = lax.psum_scatter(
            projected, "kv", scatter_dimension=1, tiled=True
        ).astype(jnp.float32)
    residual = (hidden_in.astype(jnp.float32) + head_total).astype(jnp.bfloat16)
    resid_float = residual.astype(jnp.float32)
    scaled = resid_float * norm_gain.astype(jnp.float32)[None, :]
    stats = jnp.concatenate(
        [
            jnp.sum(resid_float * resid_float, axis=1, keepdims=True),
            jnp.dot(scaled, router_weight, precision=lax.Precision.HIGHEST),
        ],
        axis=1,
    )
    if lax.axis_size("kv") == 4:
        stats = stats + lax.ppermute(stats, "kv", [(i, i ^ 1) for i in range(4)])
        stats = stats + lax.ppermute(stats, "kv", [(i, i ^ 2) for i in range(4)])
    else:
        stats = lax.psum(stats, "kv")
    square_sum = stats[:, 0]
    raw_logits = stats[:, 1:]
    inverse = lax.rsqrt(square_sum / D + EPSILON)
    logits = raw_logits * inverse[:, None]
    normed = (scaled * inverse[:, None]).astype(jnp.bfloat16)
    expert_count = router_weight.shape[1]
    top_count = expert_routes.shape[1]
    chosen_logit = jnp.sum(
        jnp.where(
            expert_routes[:, :, None] == jnp.arange(expert_count)[None, None, :],
            logits[:, None, :],
            0.0,
        ),
        axis=2,
    )
    lifted = jnp.exp(chosen_logit)
    gates = lifted / jnp.sum(lifted, axis=1, keepdims=True)
    capacity = CAP
    flat_routes = expert_routes.reshape(-1)
    assign_count = flat_routes.shape[0]
    onehot = (flat_routes[:, None] == jnp.arange(expert_count)[None, :]).astype(jnp.int32)
    earlier = jnp.cumsum(onehot, axis=0) - onehot
    slot_rank = jnp.sum(earlier * onehot, axis=1)
    target = flat_routes * capacity + slot_rank
    slot_total = expert_count * capacity
    slot_hit = target.reshape(stretch_len, top_count, 1) == jnp.arange(slot_total)[None, None, :]
    token_slot = jnp.any(slot_hit, axis=1).astype(jnp.bfloat16)
    packed_rows = lax.dot_general(
        token_slot, normed, (((0,), (0,)), ((), ())), preferred_element_type=jnp.float32
    ).astype(jnp.bfloat16)
    pieces_here = w_gate.shape[0]
    feature_part = normed.shape[1]
    paired = pieces_here % 2 == 0
    kv_count = lax.axis_size("kv")
    core_bit = lax.axis_index("kv") % 2
    chip_bit = lax.axis_index("kv") // 2
    flip_core = [(i, i ^ 1) for i in range(kv_count)]
    flip_chip = [(i, i ^ 2) for i in range(kv_count)]
    if paired:
        experts_here = pieces_here // 2
        outgoing_rows = packed_rows.reshape(blk_count, experts_here, capacity, feature_part)
    else:
        experts_here = 1
        outgoing_rows = jnp.broadcast_to(
            packed_rows.reshape(expert_count, 1, capacity, feature_part),
            (expert_count, 2, capacity, feature_part),
        ).reshape(blk_count, pieces_here, capacity, feature_part)

    def pair_stage(landed_rows, gate_w, up_w):
        chunk_pieces = gate_w.shape[0]
        if paired:
            rows_in = jnp.broadcast_to(
                landed_rows[:, :, None],
                (blk_count, chunk_pieces // 2, 2, capacity, feature_part),
            ).reshape(blk_count, chunk_pieces, capacity, feature_part)
        else:
            rows_in = landed_rows
        gate_part = jnp.einsum("spkd,pdu->spku", rows_in, gate_w, preferred_element_type=jnp.float32)
        up_part = jnp.einsum("spkd,pdu->spku", rows_in, up_w, preferred_element_type=jnp.float32)
        both_parts = jnp.stack([gate_part, up_part], axis=3).astype(jnp.bfloat16)
        half = both_parts.shape[0] // 2
        kept = lax.dynamic_slice_in_dim(both_parts, core_bit * half, half, 0)
        given = lax.dynamic_slice_in_dim(both_parts, (1 - core_bit) * half, half, 0)
        pair_sum = kept.astype(jnp.float32) + lax.ppermute(given, "kv", flip_core).astype(jnp.float32)
        return pair_sum.astype(jnp.bfloat16)

    def out_stage(pair_sum, down_w):
        chunk_pieces = down_w.shape[0]
        quarter = pair_sum.shape[0] // 2
        chip_kept = lax.dynamic_slice_in_dim(pair_sum, chip_bit * quarter, quarter, 0)
        chip_given = lax.dynamic_slice_in_dim(pair_sum, (1 - chip_bit) * quarter, quarter, 0)
        whole = chip_kept.astype(jnp.float32) + lax.ppermute(
            chip_given, "kv", flip_chip
        ).astype(jnp.float32)
        hidden_quarter = (jax.nn.silu(whole[:, :, :, 0]) * whole[:, :, :, 1]).astype(jnp.bfloat16)
        hidden_far = lax.ppermute(hidden_quarter, "kv", flip_chip)
        hidden_half = jnp.where(
            chip_bit == 0,
            jnp.concatenate([hidden_quarter, hidden_far], axis=0),
            jnp.concatenate([hidden_far, hidden_quarter], axis=0),
        )
        hidden_other = lax.ppermute(hidden_half, "kv", flip_core)
        hidden = jnp.where(
            core_bit == 0,
            jnp.concatenate([hidden_half, hidden_other], axis=0),
            jnp.concatenate([hidden_other, hidden_half], axis=0),
        )
        piece_out = jnp.einsum(
            "spku,pud->spkd", hidden, down_w, preferred_element_type=jnp.float32
        ).astype(jnp.bfloat16)
        if paired:
            half_sum = piece_out.reshape(blk_count, chunk_pieces // 2, 2, capacity, feature_part)
            half_sum = jnp.sum(half_sum.astype(jnp.float32), axis=2).astype(jnp.bfloat16)
            if shifted:
                back_sets = [half_sum[0]] + [
                    lax.ppermute(
                        half_sum[shift],
                        "blk",
                        [(i, (i - shift) % blk_count) for i in range(blk_count)],
                    )
                    for shift in range(1, blk_count)
                ]
                by_shift = jnp.stack(back_sets + back_sets)
                return lax.dynamic_slice_in_dim(
                    by_shift, (blk_count - own_index) % blk_count, blk_count, 0
                )
            return lax.all_to_all(half_sum, "blk", split_axis=0, concat_axis=0, tiled=True)
        returned = lax.all_to_all(piece_out, "blk", split_axis=0, concat_axis=0, tiled=True)
        per_piece = returned.reshape(expert_count, 2, capacity, feature_part).astype(jnp.float32)
        return (per_piece[:, 0] + per_piece[:, 1]).astype(jnp.bfloat16)

    chunk_count = CHUNKS if paired and experts_here % CHUNKS == 0 else 1
    shifted = paired and blk_count <= 8
    chunk_experts = experts_here // chunk_count
    chunk_pieces = pieces_here // chunk_count
    piece_sets = [slice(i * chunk_pieces, (i + 1) * chunk_pieces) for i in range(chunk_count)]
    def dispatch(rows_now):
        if not shifted:
            return lax.all_to_all(rows_now, "blk", split_axis=0, concat_axis=0, tiled=True)
        arrivals = []
        for shift in range(blk_count):
            mine = lax.dynamic_index_in_dim(
                rows_now, (own_index + shift) % blk_count, 0, keepdims=False
            )
            if shift:
                mine = lax.ppermute(
                    mine, "blk", [(i, (i + shift) % blk_count) for i in range(blk_count)]
                )
            arrivals.append(mine)
        return jnp.stack(arrivals)

    landed_sets = [
        dispatch(outgoing_rows[:, i * chunk_experts : (i + 1) * chunk_experts])
        for i in range(chunk_count)
    ]
    pair_sets = []
    for i in range(chunk_count):
        landed_now = landed_sets[i]
        if pair_sets:
            pair_sets[-1], landed_now = lax.optimization_barrier((pair_sets[-1], landed_now))
        pair_sets.append(pair_stage(landed_now, w_gate[piece_sets[i]], w_up[piece_sets[i]]))
    per_chunk = [out_stage(pair_sets[i], w_down[piece_sets[i]]) for i in range(chunk_count)]
    if paired:
        per_slot = jnp.concatenate(per_chunk, axis=1).reshape(slot_total, feature_part)
    else:
        per_slot = per_chunk[0].reshape(slot_total, feature_part)
    per_slot = per_slot.astype(jnp.float32)
    slot_weight = jnp.sum(jnp.where(slot_hit, gates[:, :, None], 0.0), axis=1)
    moe_out = jnp.dot(
        slot_weight, per_slot, precision=lax.Precision.HIGHEST, preferred_element_type=jnp.float32
    )
    layer_out = (resid_float + moe_out).astype(jnp.bfloat16)
    here_old = in_use & (decode_holder[:, :max_blocks] == own_index)
    from_old = jnp.where(here_old, block_holder, blk_count).reshape(-1)
    put_old = jax.ops.segment_sum(
        (decode_slot[:, :max_blocks] + 1).reshape(-1), from_old, num_segments=blk_count
    )
    here_new = decode_holder[:, max_blocks:] == own_index
    request_ids = jnp.broadcast_to(jnp.arange(decode_holder.shape[0])[:, None], here_new.shape)
    from_new = jnp.where(here_new, request_ids, blk_count).reshape(-1)
    put_new = jax.ops.segment_sum(
        (decode_slot[:, max_blocks:] + 1).reshape(-1), from_new, num_segments=blk_count
    )
    placing = put_old + put_new
    decode_size = pool_size + fresh_count
    placement = (placing[None, :] - 1 == jnp.arange(decode_size)[:, None]).astype(jnp.bfloat16)
    decoded = jnp.dot(
        placement, landed.reshape(blk_count, -1), preferred_element_type=jnp.float32
    ).astype(jnp.bfloat16)
    decode_pool = decoded.reshape(decode_size, block_len, 1, 2, head_dim)
    return (layer_out, decode_pool)


def solution(mesh):
    in_specs = (
        P("blk", "kv"),
        P("blk", "kv"),
        P("blk", "kv", None, None),
        P("blk", None, "kv", None, None),
        P(),
        P(),
        P(),
        P(),
        P(),
        P("kv", "blk"),
        P("kv"),
        P("kv", None),
        P("blk", None),
        P("blk", "kv", None),
        P("blk", "kv", None),
        P("blk", None, "kv"),
    )
    out_specs = (P("blk", "kv"), P("blk", None, "kv", None, None))
    return jax.shard_map(
        per_device, mesh=mesh, in_specs=in_specs, out_specs=out_specs, check_vma=False
    )
```

```python
import math

import jax
import jax.numpy as jnp
from jax import lax
from jax.sharding import PartitionSpec as P

D = 2560
CAP = 8
CHUNKS = 1


EPSILON = 1e-05
MASKED = -1e30


def head_rows(asked_rows, head_count, head_dim):
    stretch_len = asked_rows.shape[0]
    return (
        asked_rows.reshape(stretch_len, head_count, head_dim)
        .transpose(1, 0, 2)
        .reshape(head_count * stretch_len, head_dim)
    )


def absorb(carried, scores, value_rows):
    running_max, denominator, accumulated = carried
    new_max = jnp.maximum(running_max, jnp.max(scores, axis=1))
    decay = jnp.exp(running_max - new_max)
    raised = jnp.exp(scores - new_max[:, None])
    denominator = denominator * decay + jnp.sum(raised, axis=1)
    accumulated = accumulated * decay[:, None] + jnp.dot(
        raised.astype(jnp.bfloat16), value_rows, preferred_element_type=jnp.float32
    )
    return (new_max, denominator, accumulated)


def attend_blocks(carried, query_rows, blocks, present, scale):
    block_count = blocks.shape[0]
    block_len = blocks.shape[1]
    head_dim = blocks.shape[3]
    tile_blocks = min(32, block_count)
    span = tile_blocks * block_len
    flags = present.astype(jnp.int32)
    live_count = jnp.sum(flags)
    order_rank = jnp.cumsum(flags) - 1
    positions = jnp.arange(block_count)
    chosen = present[None, :] & (order_rank[None, :] == positions[:, None])
    packing = jnp.sum(jnp.where(chosen, positions[None, :], 0), axis=1)
    packed = blocks[packing]

    def advance(turn, state_now):
        segment = lax.dynamic_slice_in_dim(packed, turn * tile_blocks, tile_blocks, 0)
        key_rows = segment[:, :, 0].reshape(span, head_dim)
        value_rows = segment[:, :, 1].reshape(span, head_dim)
        scores = (
            jnp.einsum("qd,kd->qk", query_rows, key_rows, preferred_element_type=jnp.float32)
            * scale
        )
        is_live = turn * tile_blocks + jnp.arange(span) // block_len < live_count
        scores = jnp.where(is_live[None, :], scores, MASKED)
        return absorb(state_now, scores, value_rows)

    return lax.fori_loop(0, (live_count + tile_blocks - 1) // tile_blocks, advance, carried)


def per_device(
    hidden_in,
    queries,
    new_kv,
    cache_pool,
    cache_len,
    block_holder,
    block_slot,
    decode_holder,
    decode_slot,
    out_weight,
    norm_gain,
    router_weight,
    expert_routes,
    w_gate,
    w_up,
    w_down,
):
    blk_count = lax.axis_size("blk")
    own_index = lax.axis_index("blk")
    stretch_len = queries.shape[0]
    head_dim = new_kv.shape[3]
    head_count = queries.shape[1] // head_dim
    pool_size = cache_pool.shape[0]
    block_len = cache_pool.shape[1]
    max_blocks = block_holder.shape[1]
    fresh_count = stretch_len // block_len
    scale = 1.0 / math.sqrt(head_dim)
    devices = jnp.arange(blk_count)
    in_use = jnp.arange(max_blocks)[None, :] < (cache_len // block_len)[:, None]
    pool_rows = cache_pool[:, :, 0]
    fresh_rows = new_kv[:, 0]
    held_here = in_use & (block_holder == own_index)
    old_target = jnp.where(held_here, decode_holder[:, :max_blocks], blk_count).reshape(-1)
    pick_old = jnp.sum(
        jnp.where(
            old_target[None, :] == devices[:, None], (block_slot + 1).reshape(-1)[None, :], 0
        ),
        axis=1,
    )
    new_dest = lax.dynamic_index_in_dim(decode_holder, own_index, 0, keepdims=False)[max_blocks:]
    pick_new = jnp.sum(
        jnp.where(
            new_dest[None, :] == devices[:, None],
            (pool_size + 1 + jnp.arange(fresh_count))[None, :],
            0,
        ),
        axis=1,
    )
    picked = pick_old + pick_new
    source_count = pool_size + fresh_count
    send_pick = (jnp.arange(source_count)[None, :] == (picked - 1)[:, None]).astype(jnp.bfloat16)
    sending = (
        jnp.dot(send_pick[:, :pool_size], pool_rows.reshape(pool_size, -1), preferred_element_type=jnp.float32)
        + jnp.dot(
            send_pick[:, pool_size:],
            fresh_rows.reshape(fresh_count, -1),
            preferred_element_type=jnp.float32,
        )
    ).astype(jnp.bfloat16).reshape((blk_count,) + pool_rows.shape[1:])
    match_here = (block_holder[:blk_count] == own_index) & in_use[:blk_count]
    out_slot = jnp.sum(jnp.where(match_here, block_slot[:blk_count], 0), axis=1)
    out_pick = (jnp.arange(pool_size)[None, :] == out_slot[:, None]).astype(jnp.bfloat16)
    outgoing = (
        jnp.dot(out_pick, pool_rows.reshape(pool_size, -1), preferred_element_type=jnp.float32)
        .astype(jnp.bfloat16)
        .reshape((blk_count,) + pool_rows.shape[1:])
    )
    block_shape = sending.shape[1:]
    block_pairs = jnp.stack(
        [sending.reshape(blk_count, -1, head_dim), outgoing.reshape(blk_count, -1, head_dim)],
        axis=1,
    )
    if blk_count <= 8:
        block_arrivals = []
        for shift in range(blk_count):
            mine = lax.dynamic_index_in_dim(
                block_pairs, (own_index - shift) % blk_count, 0, keepdims=False
            )
            if shift:
                mine = lax.ppermute(
                    mine, "blk", [(i, (i - shift) % blk_count) for i in range(blk_count)]
                )
            block_arrivals.append(mine)
        both_blocks = lax.dynamic_slice_in_dim(
            jnp.stack(block_arrivals + block_arrivals),
            (blk_count - own_index) % blk_count,
            blk_count,
            0,
        )
    else:
        both_blocks = lax.all_to_all(block_pairs, "blk", split_axis=0, concat_axis=0, tiled=True)
    landed = both_blocks[:, 0].reshape((blk_count,) + block_shape)
    arrived = both_blocks[:, 1].reshape((blk_count,) + block_shape)
    present = jnp.any(
        (lax.dynamic_index_in_dim(block_holder, own_index, 0, keepdims=False)[None, :] == devices[:, None])
        & lax.dynamic_index_in_dim(in_use, own_index, 0, keepdims=False)[None, :],
        axis=1,
    )
    own_rows = head_rows(queries, head_count, head_dim)
    row_count = head_count * stretch_len
    start_state = (
        jnp.full((row_count,), MASKED, jnp.float32),
        jnp.zeros((row_count,), jnp.float32),
        jnp.zeros((row_count, head_dim), jnp.float32),
    )
    query_pos = jnp.arange(row_count) % stretch_len
    allowed = jnp.arange(stretch_len)[None, :] <= query_pos[:, None]
    local_scores = (
        jnp.einsum("qd,kd->qk", own_rows, fresh_rows[:, 0], preferred_element_type=jnp.float32)
        * scale
    )
    carried = absorb(start_state, jnp.where(allowed, local_scores, MASKED), fresh_rows[:, 1])
    carried = attend_blocks(carried, own_rows, arrived, present, scale)
    running_max, denominator, accumulated = carried
    attended = (
        (accumulated / denominator[:, None])
        .reshape(head_count, stretch_len, head_dim)
        .transpose(1, 0, 2)
    )
    attended = attended.reshape(stretch_len, head_count * head_dim).astype(jnp.bfloat16)
    if blk_count <= 8:
        back_parts = []
        for shift in range(blk_count):
            there = [(i, (i + shift) % blk_count) for i in range(blk_count)]
            back = [(i, (i - shift) % blk_count) for i in range(blk_count)]
            rows_from = attended if shift == 0 else lax.ppermute(attended, "blk", there)
            part = jnp.dot(rows_from, out_weight, preferred_element_type=jnp.float32)
            part = part.astype(jnp.bfloat16)
            back_parts.append(part if shift == 0 else lax.ppermute(part, "blk", back))
        by_shift = jnp.concatenate(back_parts + back_parts, axis=1)
        col_width = out_weight.shape[1]
        projected = lax.dynamic_slice_in_dim(
            by_shift, (blk_count - own_index) % blk_count * col_width, blk_count * col_width, 1
        )
    else:
        every_token = lax.all_to_all(
            jnp.broadcast_to(attended[None], (blk_count,) + attended.shape), "blk", 0, 0, tiled=True
        ).reshape(-1, attended.shape[1])
        column_part = jnp.dot(
            every_token, out_weight, preferred_element_type=jnp.float32
        ).astype(jnp.bfloat16)
        projected = lax.all_to_all(column_part, "blk", split_axis=0, concat_axis=1, tiled=True)
    kv_index = lax.axis_index("kv")
    if lax.axis_size("kv") == 4:
        chip_bit = kv_index // 2
        core_low = kv_index % 2
        swap_core = [(i, i ^ 1) for i in range(4)]
        swap_chip = [(i, i ^ 2) for i in range(4)]
        chip_cols = projected.shape[1] // 2
        chip_kept = lax.dynamic_slice_in_dim(projected, chip_bit * chip_cols, chip_cols, 1)
        chip_given = lax.dynamic_slice_in_dim(projected, (1 - chip_bit) * chip_cols, chip_cols, 1)
        chip_sum = chip_kept.astype(jnp.float32) + lax.ppermute(
            chip_given, "kv", swap_chip
        ).astype(jnp.float32)
        own_cols = chip_cols // 2
        core_kept = lax.dynamic_slice_in_dim(chip_sum, core_low * own_cols, own_cols, 1)
        core_given = lax.dynamic_slice_in_dim(
            chip_sum, (1 - core_low) * own_cols, own_cols, 1
        ).astype(jnp.bfloat16)
        head_total = core_kept + lax.ppermute(core_given, "kv", swap_core).astype(jnp.float32)
    else:
        head_total = lax.psum_scatter(
            projected, "kv", scatter_dimension=1, tiled=True
        ).astype(jnp.float32)
    residual = (hidden_in.astype(jnp.float32) + head_total).astype(jnp.bfloat16)
    resid_float = residual.astype(jnp.float32)
    scaled = resid_float * norm_gain.astype(jnp.float32)[None, :]
    stats = jnp.concatenate(
        [
            jnp.sum(resid_float * resid_float, axis=1, keepdims=True),
            jnp.dot(scaled, router_weight, precision=lax.Precision.HIGHEST),
        ],
        axis=1,
    )
    if lax.axis_size("kv") == 4:
        stats = stats + lax.ppermute(stats, "kv", [(i, i ^ 1) for i in range(4)])
        stats = stats + lax.ppermute(stats, "kv", [(i, i ^ 2) for i in range(4)])
    else:
        stats = lax.psum(stats, "kv")
    square_sum = stats[:, 0]
    raw_logits = stats[:, 1:]
    inverse = lax.rsqrt(square_sum / D + EPSILON)
    logits = raw_logits * inverse[:, None]
    normed = (scaled * inverse[:, None]).astype(jnp.bfloat16)
    expert_count = router_weight.shape[1]
    top_count = expert_routes.shape[1]
    chosen_logit = jnp.sum(
        jnp.where(
            expert_routes[:, :, None] == jnp.arange(expert_count)[None, None, :],
            logits[:, None, :],
            0.0,
        ),
        axis=2,
    )
    lifted = jnp.exp(chosen_logit)
    gates = lifted / jnp.sum(lifted, axis=1, keepdims=True)
    capacity = CAP
    flat_routes = expert_routes.reshape(-1)
    assign_count = flat_routes.shape[0]
    onehot = (flat_routes[:, None] == jnp.arange(expert_count)[None, :]).astype(jnp.int32)
    earlier = jnp.cumsum(onehot, axis=0) - onehot
    slot_rank = jnp.sum(earlier * onehot, axis=1)
    target = flat_routes * capacity + slot_rank
    slot_total = expert_count * capacity
    slot_hit = target.reshape(stretch_len, top_count, 1) == jnp.arange(slot_total)[None, None, :]
    token_slot = jnp.any(slot_hit, axis=1).astype(jnp.bfloat16)
    packed_rows = lax.dot_general(
        token_slot, normed, (((0,), (0,)), ((), ())), preferred_element_type=jnp.float32
    ).astype(jnp.bfloat16)
    pieces_here = w_gate.shape[0]
    feature_part = normed.shape[1]
    paired = pieces_here % 2 == 0
    kv_count = lax.axis_size("kv")
    core_bit = lax.axis_index("kv") % 2
    chip_bit = lax.axis_index("kv") // 2
    flip_core = [(i, i ^ 1) for i in range(kv_count)]
    flip_chip = [(i, i ^ 2) for i in range(kv_count)]
    if paired:
        experts_here = pieces_here // 2
        outgoing_rows = packed_rows.reshape(blk_count, experts_here, capacity, feature_part)
    else:
        experts_here = 1
        outgoing_rows = jnp.broadcast_to(
            packed_rows.reshape(expert_count, 1, capacity, feature_part),
            (expert_count, 2, capacity, feature_part),
        ).reshape(blk_count, pieces_here, capacity, feature_part)

    def pair_stage(landed_rows, gate_w, up_w):
        chunk_pieces = gate_w.shape[0]
        if paired:
            rows_in = jnp.broadcast_to(
                landed_rows[:, :, None],
                (blk_count, chunk_pieces // 2, 2, capacity, feature_part),
            ).reshape(blk_count, chunk_pieces, capacity, feature_part)
        else:
            rows_in = landed_rows
        gate_part = jnp.einsum("spkd,pdu->spku", rows_in, gate_w, preferred_element_type=jnp.float32)
        up_part = jnp.einsum("spkd,pdu->spku", rows_in, up_w, preferred_element_type=jnp.float32)
        both_parts = jnp.stack([gate_part, up_part], axis=3).astype(jnp.bfloat16)
        half = both_parts.shape[0] // 2
        kept = lax.dynamic_slice_in_dim(both_parts, core_bit * half, half, 0)
        given = lax.dynamic_slice_in_dim(both_parts, (1 - core_bit) * half, half, 0)
        pair_sum = kept.astype(jnp.float32) + lax.ppermute(given, "kv", flip_core).astype(jnp.float32)
        return pair_sum.astype(jnp.bfloat16)

    def out_stage(pair_sum, down_w):
        chunk_pieces = down_w.shape[0]
        quarter = pair_sum.shape[0] // 2
        chip_kept = lax.dynamic_slice_in_dim(pair_sum, chip_bit * quarter, quarter, 0)
        chip_given = lax.dynamic_slice_in_dim(pair_sum, (1 - chip_bit) * quarter, quarter, 0)
        whole = chip_kept.astype(jnp.float32) + lax.ppermute(
            chip_given, "kv", flip_chip
        ).astype(jnp.float32)
        hidden_quarter = (jax.nn.silu(whole[:, :, :, 0]) * whole[:, :, :, 1]).astype(jnp.bfloat16)
        hidden_far = lax.ppermute(hidden_quarter, "kv", flip_chip)
        hidden_half = jnp.where(
            chip_bit == 0,
            jnp.concatenate([hidden_quarter, hidden_far], axis=0),
            jnp.concatenate([hidden_far, hidden_quarter], axis=0),
        )
        hidden_other = lax.ppermute(hidden_half, "kv", flip_core)
        hidden = jnp.where(
            core_bit == 0,
            jnp.concatenate([hidden_half, hidden_other], axis=0),
            jnp.concatenate([hidden_other, hidden_half], axis=0),
        )
        piece_out = jnp.einsum(
            "spku,pud->spkd", hidden, down_w, preferred_element_type=jnp.float32
        ).astype(jnp.bfloat16)
        if paired:
            half_sum = piece_out.reshape(blk_count, chunk_pieces // 2, 2, capacity, feature_part)
            half_sum = jnp.sum(half_sum.astype(jnp.float32), axis=2).astype(jnp.bfloat16)
            return lax.all_to_all(half_sum, "blk", split_axis=0, concat_axis=0, tiled=True)
        returned = lax.all_to_all(piece_out, "blk", split_axis=0, concat_axis=0, tiled=True)
        per_piece = returned.reshape(expert_count, 2, capacity, feature_part).astype(jnp.float32)
        return (per_piece[:, 0] + per_piece[:, 1]).astype(jnp.bfloat16)

    chunk_count = CHUNKS if paired and experts_here % CHUNKS == 0 else 1
    chunk_experts = experts_here // chunk_count
    chunk_pieces = pieces_here // chunk_count
    piece_sets = [slice(i * chunk_pieces, (i + 1) * chunk_pieces) for i in range(chunk_count)]
    landed_sets = [
        lax.all_to_all(
            outgoing_rows[:, i * chunk_experts : (i + 1) * chunk_experts],
            "blk",
            split_axis=0,
            concat_axis=0,
            tiled=True,
        )
        for i in range(chunk_count)
    ]
    pair_sets = []
    for i in range(chunk_count):
        landed_now = landed_sets[i]
        if pair_sets:
            pair_sets[-1], landed_now = lax.optimization_barrier((pair_sets[-1], landed_now))
        pair_sets.append(pair_stage(landed_now, w_gate[piece_sets[i]], w_up[piece_sets[i]]))
    per_chunk = [out_stage(pair_sets[i], w_down[piece_sets[i]]) for i in range(chunk_count)]
    if paired:
        per_slot = jnp.concatenate(per_chunk, axis=1).reshape(slot_total, feature_part)
    else:
        per_slot = per_chunk[0].reshape(slot_total, feature_part)
    per_slot = per_slot.astype(jnp.float32)
    slot_weight = jnp.sum(jnp.where(slot_hit, gates[:, :, None], 0.0), axis=1)
    moe_out = jnp.dot(
        slot_weight, per_slot, precision=lax.Precision.HIGHEST, preferred_element_type=jnp.float32
    )
    layer_out = (resid_float + moe_out).astype(jnp.bfloat16)
    here_old = in_use & (decode_holder[:, :max_blocks] == own_index)
    from_old = jnp.where(here_old, block_holder, blk_count).reshape(-1)
    put_old = jax.ops.segment_sum(
        (decode_slot[:, :max_blocks] + 1).reshape(-1), from_old, num_segments=blk_count
    )
    here_new = decode_holder[:, max_blocks:] == own_index
    request_ids = jnp.broadcast_to(jnp.arange(decode_holder.shape[0])[:, None], here_new.shape)
    from_new = jnp.where(here_new, request_ids, blk_count).reshape(-1)
    put_new = jax.ops.segment_sum(
        (decode_slot[:, max_blocks:] + 1).reshape(-1), from_new, num_segments=blk_count
    )
    placing = put_old + put_new
    decode_size = pool_size + fresh_count
    placement = (placing[None, :] - 1 == jnp.arange(decode_size)[:, None]).astype(jnp.bfloat16)
    decoded = jnp.dot(
        placement, landed.reshape(blk_count, -1), preferred_element_type=jnp.float32
    ).astype(jnp.bfloat16)
    decode_pool = decoded.reshape(decode_size, block_len, 1, 2, head_dim)
    return (layer_out, decode_pool)


def solution(mesh):
    in_specs = (
        P("blk", "kv"),
        P("blk", "kv"),
        P("blk", "kv", None, None),
        P("blk", None, "kv", None, None),
        P(),
        P(),
        P(),
        P(),
        P(),
        P("kv", "blk"),
        P("kv"),
        P("kv", None),
        P("blk", None),
        P("blk", "kv", None),
        P("blk", "kv", None),
        P("blk", None, "kv"),
    )
    out_specs = (P("blk", "kv"), P("blk", None, "kv", None, None))
    return jax.shard_map(
        per_device, mesh=mesh, in_specs=in_specs, out_specs=out_specs, check_vma=False
    )
```
